32 devices in a mesh: cond: 2 (over x), gx: 4 (over z), gy: 4 (over y, core).
Axes of the slice: x: 2, y: 2, z: 4, core: 2. Of those that a mesh axis runs over, the one named last changes fastest.
Arguments:
- psi_old: float32 [32, 4, 6, 2048], P('gx', 'cond', None, 'gy'), may hold values from -6 to 6
- objective_grad: float32 [32, 4, 6, 2048], P('gx', 'cond', None, 'gy'), may hold values from -6 to 6
- near_upper: float32 [32, 4, 6, 6, 2048], P('gx', 'cond', None, None, 'gy'), may hold values from -1 to 0.06
- far_upper: float32 [32, 4, 6, 6, 2048], P('gx', 'cond', None, None, 'gy'), may hold values from -1 to 0.03
- inverse_diag: float32 [32, 4, 6, 6, 2048], P('gx', 'cond', None, None, 'gy'), may hold values from -0.06 to 1
- near_lower: float32 [32, 4, 6, 6, 2048], P('gx', 'cond', None, None, 'gy'), may hold values from -1 to 0.06
- far_lower: float32 [32, 4, 6, 6, 2048], P('gx', 'cond', None, None, 'gy'), may hold values from -1 to 0.03
- y_inverse: float32 [32, 4, 6, 6, 2048], P('gx', 'cond', None, None, 'gy'), may hold values from -0.1 to 1.5
- z_inverse: float32 [4, 6, 32, 32], P('cond'), may hold values from -1 to 1
- sens_terms: float32 [32, 4, 3, 6, 2048], P('gx', 'cond', None, None, 'gy'), may hold values from -1.25 to 1.25
- wall_mask: int32 [32, 2048], P('gx', 'gy'), may hold values 0 or 1
- cond_index: int32 [4], P('cond'), may hold values from 0 to 7
- weight_table: float32 [8], replicated, may hold values from 0.5 to 2
Outputs:
- psi_new: float32 [32, 4, 6, 2048], P('gx', 'cond', None, 'gy')
- mesh_sens: float32 [32, 3, 2048], P('gx', None, 'gy')
The draws below stay inside these ranges and needn't reach their ends.
All inputs are finite; a program needn't handle non-finite values. No bound on the sum of `wall_mask` on one device may be relied on, other than what follows from the above.
Results may differ from the reference program's by a relative error of at most 0.0001.
Values sent between devices are 32-bit elements; how exact they have to be, the bound alone decides.
No kernel may reach another device: no remote copies, remote signals or barrier semaphores. Data moves between devices by JAX's collectives and lax.ppermute only.
A program may use at most 128 MiB of HBM per device.

```python
import math
import jax
import jax.numpy as jnp
from jax import lax

NV = 6
NZ = 32
ITERS = 2
NPOINTS = 8
NCOND = 4
STREAM_CELLS = 32
NY = 64
NYZ = 2048


def coupling(key):
    keys = jax.random.split(key, 8)
    rate_shape = (1, NCOND, NV, 1, NYZ)
    cell_shape = (STREAM_CELLS, NCOND, NV, 1, NYZ)
    full_shape = (STREAM_CELLS, NCOND, NV, NV, NYZ)
    slow_share = 0.5
    picked = jax.random.uniform(keys[0], rate_shape) < slow_share
    slow_low = 0.2 ** (1.0 / STREAM_CELLS)
    slow_high = 0.5 ** (1.0 / STREAM_CELLS)
    slow = slow_low + (slow_high - slow_low) * jax.random.uniform(keys[1], rate_shape)
    fast = jnp.exp(-jax.random.uniform(keys[2], rate_shape, minval=1.0 / 40.0, maxval=1.0 / 20.0))
    growth_rate = jnp.where(picked, slow, fast)
    coarse_guess = jax.random.uniform(keys[3], cell_shape, minval=0.985, maxval=1.0)
    spots = jax.random.randint(keys[4], (3,), 0, STREAM_CELLS)
    impact_hit = jnp.any(jnp.arange(STREAM_CELLS)[:, None] == spots[None, :], axis=1)
    sudden_jump = jnp.where(impact_hit, 0.65, 1.0).reshape(STREAM_CELLS, 1, 1, 1, 1)
    falloff_factor = growth_rate * coarse_guess * sudden_jump
    share = jax.random.uniform(keys[5], cell_shape, minval=0.75, maxval=0.9)
    ident = jnp.eye(NV, dtype=jnp.float32).reshape(1, 1, NV, NV, 1)
    near = -falloff_factor * share * ident + jax.random.uniform(keys[6], full_shape, minval=-0.06, maxval=0.06) * (1.0 - ident)
    far = -falloff_factor * (1.0 - share) * ident + jax.random.uniform(keys[7], full_shape, minval=-0.03, maxval=0.03) * (1.0 - ident)
    return (near, far)


def dominant(key, lower, upper, spread):
    keys = jax.random.split(key, 2)
    ident = jnp.eye(NV, dtype=jnp.float32).reshape(1, 1, NV, NV, 1)
    diagonal = jax.random.uniform(keys[0], (STREAM_CELLS, NCOND, NV, 1, NYZ), minval=lower, maxval=upper)
    rest = jax.random.uniform(keys[1], (STREAM_CELLS, NCOND, NV, NV, NYZ), minval=-spread, maxval=spread)
    return diagonal * ident + rest * (1.0 - ident)


def draw_near_upper(key, part):
    return coupling(jax.random.fold_in(key, 11))[0]


def draw_far_upper(key, part):
    return coupling(jax.random.fold_in(key, 11))[1]


def draw_near_lower(key, part):
    return coupling(jax.random.fold_in(key, 23))[0]


def draw_far_lower(key, part):
    return coupling(jax.random.fold_in(key, 23))[1]


def draw_inverse_diag(key, part):
    return dominant(jax.random.fold_in(key, 37), 0.8, 1.0, 0.06)


def draw_y_inverse(key, part):
    return dominant(jax.random.fold_in(key, 41), 0.5, 1.5, 0.1)


def set_ends(entries, rng, smallest, largest):
    index_at = [jax.random.randint(jax.random.fold_in(rng, axis), (), 0, length) for axis, length in enumerate(entries.shape)]
    longest = entries.shape.index(max(entries.shape))
    beside = index_at[:longest] + [(index_at[longest] + 1) % entries.shape[longest]] + index_at[longest + 1:]
    return entries.at[tuple(index_at)].set(smallest).at[tuple(beside)].set(largest)


def level_of(key, shape, cuts, low, top_value):
    def one(position, shards_of):
        steps = jax.random.uniform(jax.random.fold_in(jax.random.fold_in(key, 6), position), (shards_of,), jnp.float32, low / len(cuts), top_value / len(cuts))
        return jnp.repeat(jnp.exp(steps), shape[position] // shards_of).reshape((-1,) + (1,) * (len(shape) - position - 1))

    level = one(*cuts[0])
    for cut in cuts[1:]:
        level = level * one(*cut)
    return level


def noise(rng, dims, deviation, most, cuts=(), kind=jnp.bfloat16):
    entries = deviation * jax.random.normal(rng, dims, jnp.float32)
    if cuts:
        entries = entries * level_of(rng, dims, cuts, -0.22, 0.18)
    return jnp.clip(entries, -most, most).astype(kind)


def setup_inputs(seed: int = 0) -> dict:
    streams_of = jax.random.split(jax.random.key(seed), 14)
    psi_old = noise(streams_of[0], (STREAM_CELLS, NCOND, NV, NYZ), 1.0, 6.0, ((0, 4), (1, 2), (3, 4)), jnp.float32)
    objective_grad = noise(streams_of[1], (STREAM_CELLS, NCOND, NV, NYZ), 1.0, 6.0, ((0, 4), (1, 2), (3, 4)), jnp.float32)
    near_upper = draw_near_upper(jax.random.fold_in(streams_of[13], 71), 0)
    far_upper = draw_far_upper(jax.random.fold_in(streams_of[13], 71), 0)
    inverse_diag = draw_inverse_diag(jax.random.fold_in(streams_of[13], 71), 0)
    near_lower = draw_near_lower(jax.random.fold_in(streams_of[13], 71), 0)
    far_lower = draw_far_lower(jax.random.fold_in(streams_of[13], 71), 0)
    y_inverse = draw_y_inverse(jax.random.fold_in(streams_of[13], 71), 0)
    z_inverse = noise(streams_of[8], (NCOND, NV, NZ, NZ), NZ ** -0.5, 1.0, ((0, 2),), jnp.float32)
    sens_terms = noise(streams_of[9], (STREAM_CELLS, NCOND, 3, NV, NYZ), (NV * NCOND) ** -0.5, 1.25, ((0, 4), (1, 2), (4, 4)), jnp.float32)
    wall_mask = set_ends((jax.random.randint(streams_of[10], (STREAM_CELLS, NYZ), 0, 8) < 1).astype(jnp.int32), jax.random.fold_in(streams_of[10], 1), 0, 1)
    cond_index = set_ends(jax.random.randint(streams_of[11], (NCOND,), 0, NPOINTS), jax.random.fold_in(streams_of[11], 1), 0, NPOINTS - 1).astype(jnp.int32)
    weight_table = jnp.clip(jnp.exp(jax.random.uniform(streams_of[12], (NPOINTS,), jnp.float32, math.log(0.5), math.log(2.0))), 0.5, 2.0)
    return {"psi_old": psi_old, "objective_grad": objective_grad, "near_upper": near_upper, "far_upper": far_upper, "inverse_diag": inverse_diag, "near_lower": near_lower, "far_lower": far_lower, "y_inverse": y_inverse, "z_inverse": z_inverse, "sens_terms": sens_terms, "wall_mask": wall_mask, "cond_index": cond_index, "weight_table": weight_table}


def apply_block(blocks, vector):
    return jnp.sum(blocks * vector[..., None, :, :], axis=-2)


def apply_transpose(blocks, vector):
    return jnp.sum(blocks * vector[..., :, None, :], axis=-3)


def upper_sweep(rhs, near, far, incoming):
    def step(carry, item):
        last, before = carry
        value, near_cell, far_cell = item
        now = value - apply_block(near_cell, last) - apply_block(far_cell, before)
        return (now, last), now
    carry, values = lax.scan(step, (incoming[0], incoming[1]), (rhs, near, far))
    return values


def lower_sweep(rhs, inverse, near, far, incoming):
    def step(carry, item):
        pending, partial_value = carry
        value, inverse_cell, near_cell, far_cell = item
        now = apply_transpose(inverse_cell, value - pending)
        return (partial_value + apply_transpose(near_cell, now), apply_transpose(far_cell, now)), now
    carry, values = lax.scan(step, (incoming[0], incoming[1]), (rhs, inverse, near, far), reverse=True)
    return values


def reference(psi_old, objective_grad, near_upper, far_upper, inverse_diag, near_lower, far_lower, y_inverse, z_inverse, sens_terms, wall_mask, cond_index, weight_table):
    keep = (1.0 - wall_mask.astype(jnp.float32))[:, None, None, :]
    psi = psi_old
    zeros = jnp.zeros((2,) + psi_old.shape[1:], jnp.float32)
    for step in range(ITERS):
        grid = psi.reshape(STREAM_CELLS, NCOND, NV, NY, NZ)
        padded = jnp.pad(grid, ((1, 1), (0, 0), (0, 0), (1, 1), (0, 0)))
        beside_all = padded[2:, :, :, 1:-1] + padded[:-2, :, :, 1:-1] + padded[1:-1, :, :, 2:] + padded[1:-1, :, :, :-2]
        rhs = objective_grad + 0.5 * beside_all.reshape(psi.shape) - 2.0 * psi
        zres = jnp.einsum("icvjq,cvqk->icvjk", rhs.reshape(STREAM_CELLS, NCOND, NV, NY, NZ), z_inverse, precision=lax.Precision.HIGHEST).reshape(psi.shape)
        yres = apply_transpose(y_inverse, zres)
        upper = upper_sweep(yres, near_upper, far_upper, zeros)
        lower = lower_sweep(upper, inverse_diag, near_lower, far_lower, zeros)
        psi = (psi + 0.05 * lower) * keep
    onehot = (cond_index[:, None] == jnp.arange(NPOINTS)[None, :]).astype(jnp.float32)
    weights = jnp.sum(onehot * weight_table[None, :], axis=1)
    sens = jnp.einsum("icvl,icmvl->iml", psi * weights[None, :, None, None], sens_terms, precision=lax.Precision.HIGHEST)
    return psi, sens
```

```python
import jax
import jax.numpy as jnp
from jax import lax
from jax.experimental import pallas as pl
from jax.experimental.pallas import tpu as pltpu
from jax.sharding import PartitionSpec as P

NZ = 32
ITERS = 2


def extended(value, sides, width):
    for axis, dim in sides:
        size, length = (lax.axis_size(axis), value.shape[dim])
        up = [(i, (i + 1) % size) for i in range(size - 1)]
        down = [(j, i) for i, j in up]
        last = lax.slice_in_dim(value, length - width, length, axis=dim)
        first = lax.slice_in_dim(value, 0, width, axis=dim)
        before = lax.ppermute(last, axis, up)
        after = lax.ppermute(first, axis, down)
        value = jnp.concatenate([before, value, after], axis=dim)
    return value


def from_behind(value, axis, steps):
    count = lax.axis_size(axis)
    first, last = (max(0, -steps), min(count, count - steps))
    return lax.ppermute(value, axis, [(source, source + steps) for source in range(first, last)])


def _vmem_specs(n):
    return [pl.BlockSpec(memory_space=pltpu.VMEM) for _ in range(n)]


def _rows_times(blocks_ref, index, vec):
    total = None
    for a in range(vec.shape[0]):
        term = blocks_ref[index + (a,)] * vec[a : a + 1, :]
        total = term if total is None else total + term
    return total


def upper_pallas(rhs, near_t, far_t, incoming, want_values):
    count, conds, nv = near_t.shape[0], near_t.shape[1], near_t.shape[2]
    width = incoming.shape[1]
    has_rhs = rhs is not None

    def kernel(*refs):
        if has_rhs:
            rhs_ref, nt_ref, ft_ref, inc_ref = refs[:4]
            outs = refs[4:]
        else:
            nt_ref, ft_ref, inc_ref = refs[:3]
            outs = refs[3:]
        if want_values:
            val_ref, carry_ref = outs
        else:
            (carry_ref,) = outs
        carry_ref[...] = inc_ref[...]

        def step(i, unused):
            for k in range(width):
                for c in range(conds):
                    last = carry_ref[0, k, c]
                    before = carry_ref[1, k, c]
                    acc = _rows_times(nt_ref, (i, c), last) + _rows_times(ft_ref, (i, c), before)
                    if has_rhs:
                        now = rhs_ref[i, c] - acc
                    else:
                        now = -acc
                    carry_ref[1, k, c] = last
                    carry_ref[0, k, c] = now
                    if want_values:
                        val_ref[i, c] = now
            return unused

        lax.fori_loop(0, count, step, 0)

    shape = incoming.shape
    out_shape = [jax.ShapeDtypeStruct(shape, jnp.float32)]
    if want_values:
        out_shape = [jax.ShapeDtypeStruct(rhs.shape, jnp.float32)] + out_shape
    args = ([rhs] if has_rhs else []) + [near_t, far_t, incoming]
    return pl.pallas_call(
        kernel,
        out_shape=tuple(out_shape),
        in_specs=_vmem_specs(len(args)),
        out_specs=tuple(_vmem_specs(len(out_shape))),
    )(*args)


def lower_pallas(rhs, inverse, near, far, incoming, want_values):
    count, conds, nv = inverse.shape[0], inverse.shape[1], inverse.shape[2]
    width = incoming.shape[1]
    has_rhs = rhs is not None

    def kernel(*refs):
        if has_rhs:
            rhs_ref, d_ref, b_ref, a_ref, inc_ref = refs[:5]
            outs = refs[5:]
        else:
            d_ref, b_ref, a_ref, inc_ref = refs[:4]
            outs = refs[4:]
        if want_values:
            val_ref, carry_ref = outs
        else:
            (carry_ref,) = outs
        carry_ref[...] = inc_ref[...]

        def step(t, unused):
            i = count - 1 - t
            for k in range(width):
                for c in range(conds):
                    pending = carry_ref[0, k, c]
                    partial_value = carry_ref[1, k, c]
                    if has_rhs:
                        r = rhs_ref[i, c] - pending
                    else:
                        r = -pending
                    now = _rows_times(d_ref, (i, c), r)
                    carry_ref[0, k, c] = partial_value + _rows_times(b_ref, (i, c), now)
                    carry_ref[1, k, c] = _rows_times(a_ref, (i, c), now)
                    if want_values:
                        val_ref[i, c] = now
            return unused

        lax.fori_loop(0, count, step, 0)

    shape = incoming.shape
    out_shape = [jax.ShapeDtypeStruct(shape, jnp.float32)]
    if want_values:
        out_shape = [jax.ShapeDtypeStruct(rhs.shape, jnp.float32)] + out_shape
    args = ([rhs] if has_rhs else []) + [inverse, near, far, incoming]
    return pl.pallas_call(
        kernel,
        out_shape=tuple(out_shape),
        in_specs=_vmem_specs(len(args)),
        out_specs=tuple(_vmem_specs(len(out_shape))),
    )(*args)


def unit_carries(shape):
    width = 2 * shape[1]
    table = jnp.eye(width, dtype=jnp.float32).reshape(width, 2, shape[1]).transpose(1, 0, 2)
    return jnp.broadcast_to(table[:, :, None, :, None], (2, width, shape[0], shape[1], shape[2]))


def as_matrix(response):
    width = response.shape[1]
    return jnp.transpose(response, (1, 0, 3, 2, 4)).reshape(
        width, width, response.shape[2], response.shape[4]
    )


def as_vector(carry):
    return jnp.transpose(carry, (0, 2, 1, 3)).reshape(-1, carry.shape[1], carry.shape[3])


def from_vector(vector, count):
    return vector.reshape(2, count, vector.shape[1], vector.shape[2]).transpose(0, 2, 1, 3)


def carry_through(vector, matrix, offset):
    return jnp.einsum("kcl,kmcl->mcl", vector, matrix, precision=lax.Precision.HIGHEST) + offset


def on_device(
    psi_old,
    objective_grad,
    near_upper,
    far_upper,
    inverse_diag,
    near_lower,
    far_lower,
    y_inverse,
    z_inverse,
    sens_terms,
    wall_mask,
    cond_index,
    weight_table,
):
    keep = (1.0 - wall_mask.astype(jnp.float32))[:, None, None, :]
    carry_shape = psi_old.shape[1:]
    zeros = jnp.zeros((2, 1) + carry_shape, jnp.float32)
    units = unit_carries(carry_shape)
    near_t = jnp.swapaxes(near_upper, 2, 3)
    far_t = jnp.swapaxes(far_upper, 2, 3)
    (response,) = upper_pallas(None, near_t, far_t, units, False)
    matrix = as_matrix(response)
    (response,) = lower_pallas(None, inverse_diag, near_lower, far_lower, units, False)
    reverse_matrix = as_matrix(response)
    psi = psi_old
    for step in range(ITERS):
        stream_pad = extended(psi, (("gx", 0),), 1)
        span_pad = extended(psi, (("gy", 3),), NZ)
        beside_all = (
            stream_pad[2:] + stream_pad[:-2] + span_pad[..., 2 * NZ :] + span_pad[..., : -2 * NZ]
        )
        rhs = objective_grad + 0.5 * beside_all - 2.0 * psi
        grid = rhs.reshape(rhs.shape[0], rhs.shape[1], rhs.shape[2], rhs.shape[3] // NZ, NZ)
        zres = jnp.einsum(
            "icvjq,cvqk->icvjk", grid, z_inverse, precision=lax.Precision.HIGHEST
        ).reshape(rhs.shape)
        yres = jnp.sum(y_inverse * zres[..., :, None, :], axis=-3)
        _, offset = upper_pallas(yres, near_t, far_t, zeros, True)
        vector = as_vector(offset[:, 0])

        def upper_reversal(turn, incoming):
            return from_behind(carry_through(incoming, matrix, vector), "gx", 1)

        entering = lax.fori_loop(0, lax.axis_size("gx") - 1, upper_reversal, jnp.zeros_like(vector))
        upper, _ = upper_pallas(
            yres, near_t, far_t, from_vector(entering, carry_shape[1])[:, None], True
        )
        _, offset = lower_pallas(upper, inverse_diag, near_lower, far_lower, zeros, True)
        vector_back = as_vector(offset[:, 0])

        def lower_turn(turn, incoming):
            return from_behind(carry_through(incoming, reverse_matrix, vector_back), "gx", -1)

        entering = lax.fori_loop(
            0, lax.axis_size("gx") - 1, lower_turn, jnp.zeros_like(vector_back)
        )
        lower, _ = lower_pallas(
            upper,
            inverse_diag,
            near_lower,
            far_lower,
            from_vector(entering, carry_shape[1])[:, None],
            True,
        )
        psi = (psi + 0.05 * lower) * keep
    onehot = (cond_index[:, None] == jnp.arange(weight_table.shape[0])[None, :]).astype(jnp.float32)
    weights = jnp.sum(onehot * weight_table[None, :], axis=1)
    local_sens = jnp.einsum(
        "icvl,icmvl->iml",
        psi * weights[None, :, None, None],
        sens_terms,
        precision=lax.Precision.HIGHEST,
    )
    mesh_sens = lax.psum(local_sens, "cond")
    return (psi, mesh_sens)


def solution(mesh):
    placed = (
        P("gx", "cond", None, "gy"),
        P("gx", "cond", None, "gy"),
        P("gx", "cond", None, None, "gy"),
        P("gx", "cond", None, None, "gy"),
        P("gx", "cond", None, None, "gy"),
        P("gx", "cond", None, None, "gy"),
        P("gx", "cond", None, None, "gy"),
        P("gx", "cond", None, None, "gy"),
        P("cond", None, None, None),
        P("gx", "cond", None, None, "gy"),
        P("gx", "gy"),
        P("cond"),
        P(),
    )
    return jax.shard_map(
        on_device,
        mesh=mesh,
        in_specs=placed,
        out_specs=(P("gx", "cond", None, "gy"), P("gx", None, "gy")),
        check_vma=False,
    )
```

```python
import jax
import jax.numpy as jnp
from jax import lax
from jax.experimental import pallas as pl
from jax.experimental.pallas import tpu as pltpu
from jax.sharding import PartitionSpec as P

NZ = 32
ITERS = 2


def extended(value, sides, width):
    for axis, dim in sides:
        size, length = (lax.axis_size(axis), value.shape[dim])
        up = [(i, (i + 1) % size) for i in range(size - 1)]
        down = [(j, i) for i, j in up]
        last = lax.slice_in_dim(value, length - width, length, axis=dim)
        first = lax.slice_in_dim(value, 0, width, axis=dim)
        before = lax.ppermute(last, axis, up)
        after = lax.ppermute(first, axis, down)
        value = jnp.concatenate([before, value, after], axis=dim)
    return value


def from_behind(value, axis, steps):
    count = lax.axis_size(axis)
    first, last = (max(0, -steps), min(count, count - steps))
    return lax.ppermute(value, axis, [(source, source + steps) for source in range(first, last)])


def _vmem_specs(n):
    return [pl.BlockSpec(memory_space=pltpu.VMEM) for _ in range(n)]


def _rows_times(blocks_ref, index, vec):
    total = None
    for a in range(vec.shape[0]):
        term = blocks_ref[index + (a,)] * vec[a : a + 1, :]
        total = term if total is None else total + term
    return total


def upper_pallas(rhs, near_t, far_t, incoming, want_values):
    count, conds, nv = near_t.shape[0], near_t.shape[1], near_t.shape[2]
    width = incoming.shape[1]
    has_rhs = rhs is not None

    def kernel(*refs):
        if has_rhs:
            rhs_ref, nt_ref, ft_ref, inc_ref = refs[:4]
            outs = refs[4:]
        else:
            nt_ref, ft_ref, inc_ref = refs[:3]
            outs = refs[3:]
        if want_values:
            val_ref, carry_ref = outs
        else:
            (carry_ref,) = outs
        carry_ref[...] = inc_ref[...]

        def step(i, unused):
            for k in range(width):
                for c in range(conds):
                    last = carry_ref[0, k, c]
                    before = carry_ref[1, k, c]
                    acc = _rows_times(nt_ref, (i, c), last) + _rows_times(ft_ref, (i, c), before)
                    if has_rhs:
                        now = rhs_ref[i, c] - acc
                    else:
                        now = -acc
                    carry_ref[1, k, c] = last
                    carry_ref[0, k, c] = now
                    if want_values:
                        val_ref[i, c] = now
            return unused

        lax.fori_loop(0, count, step, 0)

    shape = incoming.shape
    out_shape = [jax.ShapeDtypeStruct(shape, jnp.float32)]
    if want_values:
        out_shape = [jax.ShapeDtypeStruct(rhs.shape, jnp.float32)] + out_shape
    args = ([rhs] if has_rhs else []) + [near_t, far_t, incoming]
    return pl.pallas_call(
        kernel,
        out_shape=tuple(out_shape),
        in_specs=_vmem_specs(len(args)),
        out_specs=tuple(_vmem_specs(len(out_shape))),
    )(*args)


def lower_pallas(rhs, inverse, near, far, incoming, want_values):
    count, conds, nv = inverse.shape[0], inverse.shape[1], inverse.shape[2]
    width = incoming.shape[1]
    has_rhs = rhs is not None

    def kernel(*refs):
        if has_rhs:
            rhs_ref, d_ref, b_ref, a_ref, inc_ref = refs[:5]
            outs = refs[5:]
        else:
            d_ref, b_ref, a_ref, inc_ref = refs[:4]
            outs = refs[4:]
        if want_values:
            val_ref, carry_ref = outs
        else:
            (carry_ref,) = outs
        carry_ref[...] = inc_ref[...]

        def step(t, unused):
            i = count - 1 - t
            for k in range(width):
                for c in range(conds):
                    pending = carry_ref[0, k, c]
                    partial_value = carry_ref[1, k, c]
                    if has_rhs:
                        r = rhs_ref[i, c] - pending
                    else:
                        r = -pending
                    now = _rows_times(d_ref, (i, c), r)
                    carry_ref[0, k, c] = partial_value + _rows_times(b_ref, (i, c), now)
                    carry_ref[1, k, c] = _rows_times(a_ref, (i, c), now)
                    if want_values:
                        val_ref[i, c] = now
            return unused

        lax.fori_loop(0, count, step, 0)

    shape = incoming.shape
    out_shape = [jax.ShapeDtypeStruct(shape, jnp.float32)]
    if want_values:
        out_shape = [jax.ShapeDtypeStruct(rhs.shape, jnp.float32)] + out_shape
    args = ([rhs] if has_rhs else []) + [inverse, near, far, incoming]
    return pl.pallas_call(
        kernel,
        out_shape=tuple(out_shape),
        in_specs=_vmem_specs(len(args)),
        out_specs=tuple(_vmem_specs(len(out_shape))),
    )(*args)


def unit_carries(shape):
    width = 2 * shape[1]
    table = jnp.eye(width, dtype=jnp.float32).reshape(width, 2, shape[1]).transpose(1, 0, 2)
    return jnp.broadcast_to(table[:, :, None, :, None], (2, width, shape[0], shape[1], shape[2]))


def as_matrix(response):
    width = response.shape[1]
    return jnp.transpose(response, (1, 0, 3, 2, 4)).reshape(
        width, width, response.shape[2], response.shape[4]
    )


def as_vector(carry):
    return jnp.transpose(carry, (0, 2, 1, 3)).reshape(-1, carry.shape[1], carry.shape[3])


def from_vector(vector, count):
    return vector.reshape(2, count, vector.shape[1], vector.shape[2]).transpose(0, 2, 1, 3)


def carry_through(vector, matrix, offset):
    return jnp.einsum("kcl,kmcl->mcl", vector, matrix, precision=lax.Precision.HIGHEST) + offset


def compose(first, then):
    return jnp.sum(first[:, :, None] * then[None], axis=1)


def chain_products(matrix, steps):
    count = lax.axis_size("gx")
    products = []
    reach = matrix
    for s in range(1, count - 1):
        arrived = from_behind(reach, "gx", steps)
        products.append(arrived)
        if s < count - 2:
            reach = compose(arrived, matrix)
    return products


def gathered_carry(vector, products, steps):
    count = lax.axis_size("gx")
    here = lax.axis_index("gx")
    offsets = lax.all_gather(vector, "gx")
    total = jnp.zeros_like(vector)
    for s in range(count - 1):
        source = here - steps * (s + 1)
        valid = jnp.logical_and(source >= 0, source < count)
        term = lax.dynamic_index_in_dim(offsets, jnp.clip(source, 0, count - 1), 0, keepdims=False)
        if s > 0:
            term = jnp.sum(term[:, None] * products[s - 1], axis=0)
        total = total + jnp.where(valid, term, 0.0)
    return total


def on_device(
    psi_old,
    objective_grad,
    near_upper,
    far_upper,
    inverse_diag,
    near_lower,
    far_lower,
    y_inverse,
    z_inverse,
    sens_terms,
    wall_mask,
    cond_index,
    weight_table,
):
    keep = (1.0 - wall_mask.astype(jnp.float32))[:, None, None, :]
    carry_shape = psi_old.shape[1:]
    zeros = jnp.zeros((2, 1) + carry_shape, jnp.float32)
    units = unit_carries(carry_shape)
    near_t = jnp.swapaxes(near_upper, 2, 3)
    far_t = jnp.swapaxes(far_upper, 2, 3)
    (response,) = upper_pallas(None, near_t, far_t, units, False)
    matrix = as_matrix(response)
    (response,) = lower_pallas(None, inverse_diag, near_lower, far_lower, units, False)
    reverse_matrix = as_matrix(response)
    upper_products = chain_products(matrix, 1)
    lower_products = chain_products(reverse_matrix, -1)
    psi = psi_old
    for step in range(ITERS):
        stream_pad = extended(psi, (("gx", 0),), 1)
        span_pad = extended(psi, (("gy", 3),), NZ)
        beside_all = (
            stream_pad[2:] + stream_pad[:-2] + span_pad[..., 2 * NZ :] + span_pad[..., : -2 * NZ]
        )
        rhs = objective_grad + 0.5 * beside_all - 2.0 * psi
        grid = rhs.reshape(rhs.shape[0], rhs.shape[1], rhs.shape[2], rhs.shape[3] // NZ, NZ)
        zres = jnp.einsum(
            "icvjq,cvqk->icvjk", grid, z_inverse, precision=lax.Precision.HIGHEST
        ).reshape(rhs.shape)
        yres = jnp.sum(y_inverse * zres[..., :, None, :], axis=-3)
        _, offset = upper_pallas(yres, near_t, far_t, zeros, True)
        entering = gathered_carry(as_vector(offset[:, 0]), upper_products, 1)
        upper, _ = upper_pallas(
            yres, near_t, far_t, from_vector(entering, carry_shape[1])[:, None], True
        )
        _, offset = lower_pallas(upper, inverse_diag, near_lower, far_lower, zeros, True)
        entering = gathered_carry(as_vector(offset[:, 0]), lower_products, -1)
        lower, _ = lower_pallas(
            upper,
            inverse_diag,
            near_lower,
            far_lower,
            from_vector(entering, carry_shape[1])[:, None],
            True,
        )
        psi = (psi + 0.05 * lower) * keep
    onehot = (cond_index[:, None] == jnp.arange(weight_table.shape[0])[None, :]).astype(jnp.float32)
    weights = jnp.sum(onehot * weight_table[None, :], axis=1)
    local_sens = jnp.einsum(
        "icvl,icmvl->iml",
        psi * weights[None, :, None, None],
        sens_terms,
        precision=lax.Precision.HIGHEST,
    )
    mesh_sens = lax.psum(local_sens, "cond")
    return (psi, mesh_sens)


def solution(mesh):
    placed = (
        P("gx", "cond", None, "gy"),
        P("gx", "cond", None, "gy"),
        P("gx", "cond", None, None, "gy"),
        P("gx", "cond", None, None, "gy"),
        P("gx", "cond", None, None, "gy"),
        P("gx", "cond", None, None, "gy"),
        P("gx", "cond", None, None, "gy"),
        P("gx", "cond", None, None, "gy"),
        P("cond", None, None, None),
        P("gx", "cond", None, None, "gy"),
        P("gx", "gy"),
        P("cond"),
        P(),
    )
    return jax.shard_map(
        on_device,
        mesh=mesh,
        in_specs=placed,
        out_specs=(P("gx", "cond", None, "gy"), P("gx", None, "gy")),
        check_vma=False,
    )
```

```python
import jax
import jax.numpy as jnp
from jax import lax
from jax.experimental import pallas as pl
from jax.experimental.pallas import tpu as pltpu
from jax.sharding import PartitionSpec as P

NZ = 32
ITERS = 2


def extended(value, sides, width):
    for axis, dim in sides:
        size, length = (lax.axis_size(axis), value.shape[dim])
        up = [(i, (i + 1) % size) for i in range(size - 1)]
        down = [(j, i) for i, j in up]
        last = lax.slice_in_dim(value, length - width, length, axis=dim)
        first = lax.slice_in_dim(value, 0, width, axis=dim)
        before = lax.ppermute(last, axis, up)
        after = lax.ppermute(first, axis, down)
        value = jnp.concatenate([before, value, after], axis=dim)
    return value


def from_behind(value, axis, steps):
    count = lax.axis_size(axis)
    first, last = (max(0, -steps), min(count, count - steps))
    return lax.ppermute(value, axis, [(source, source + steps) for source in range(first, last)])


def _vmem_specs(n):
    return [pl.BlockSpec(memory_space=pltpu.VMEM) for _ in range(n)]


def _rows_times(blocks_ref, index, vec):
    total = None
    for a in range(vec.shape[0]):
        term = blocks_ref[index + (a,)] * vec[a : a + 1, :]
        total = term if total is None else total + term
    return total


def upper_pallas(rhs, near_t, far_t, incoming, want_values):
    count, conds, nv = near_t.shape[0], near_t.shape[1], near_t.shape[2]
    width = incoming.shape[1]
    has_rhs = rhs is not None

    def kernel(*refs):
        if has_rhs:
            rhs_ref, nt_ref, ft_ref, inc_ref = refs[:4]
            outs = refs[4:]
        else:
            nt_ref, ft_ref, inc_ref = refs[:3]
            outs = refs[3:]
        if want_values:
            val_ref, carry_ref = outs
        else:
            (carry_ref,) = outs
        carry_ref[...] = inc_ref[...]

        def step(i, unused):
            for k in range(width):
                for c in range(conds):
                    last = carry_ref[0, k, c]
                    before = carry_ref[1, k, c]
                    acc = _rows_times(nt_ref, (i, c), last) + _rows_times(ft_ref, (i, c), before)
                    if has_rhs:
                        now = rhs_ref[i, c] - acc
                    else:
                        now = -acc
                    carry_ref[1, k, c] = last
                    carry_ref[0, k, c] = now
                    if want_values:
                        val_ref[i, c] = now
            return unused

        lax.fori_loop(0, count, step, 0)

    shape = incoming.shape
    out_shape = [jax.ShapeDtypeStruct(shape, jnp.float32)]
    if want_values:
        out_shape = [jax.ShapeDtypeStruct(rhs.shape, jnp.float32)] + out_shape
    args = ([rhs] if has_rhs else []) + [near_t, far_t, incoming]
    return pl.pallas_call(
        kernel,
        out_shape=tuple(out_shape),
        in_specs=_vmem_specs(len(args)),
        out_specs=tuple(_vmem_specs(len(out_shape))),
    )(*args)


def lower_pallas(rhs, inverse, near, far, incoming, want_values):
    count, conds, nv = inverse.shape[0], inverse.shape[1], inverse.shape[2]
    width = incoming.shape[1]
    has_rhs = rhs is not None

    def kernel(*refs):
        if has_rhs:
            rhs_ref, d_ref, b_ref, a_ref, inc_ref = refs[:5]
            outs = refs[5:]
        else:
            d_ref, b_ref, a_ref, inc_ref = refs[:4]
            outs = refs[4:]
        if want_values:
            val_ref, carry_ref = outs
        else:
            (carry_ref,) = outs
        carry_ref[...] = inc_ref[...]

        def step(t, unused):
            i = count - 1 - t
            for k in range(width):
                for c in range(conds):
                    pending = carry_ref[0, k, c]
                    partial_value = carry_ref[1, k, c]
                    if has_rhs:
                        r = rhs_ref[i, c] - pending
                    else:
                        r = -pending
                    now = _rows_times(d_ref, (i, c), r)
                    carry_ref[0, k, c] = partial_value + _rows_times(b_ref, (i, c), now)
                    carry_ref[1, k, c] = _rows_times(a_ref, (i, c), now)
                    if want_values:
                        val_ref[i, c] = now
            return unused

        lax.fori_loop(0, count, step, 0)

    shape = incoming.shape
    out_shape = [jax.ShapeDtypeStruct(shape, jnp.float32)]
    if want_values:
        out_shape = [jax.ShapeDtypeStruct(rhs.shape, jnp.float32)] + out_shape
    args = ([rhs] if has_rhs else []) + [inverse, near, far, incoming]
    return pl.pallas_call(
        kernel,
        out_shape=tuple(out_shape),
        in_specs=_vmem_specs(len(args)),
        out_specs=tuple(_vmem_specs(len(out_shape))),
    )(*args)


def unit_carries(shape):
    width = 2 * shape[1]
    table = jnp.eye(width, dtype=jnp.float32).reshape(width, 2, shape[1]).transpose(1, 0, 2)
    return jnp.broadcast_to(table[:, :, None, :, None], (2, width, shape[0], shape[1], shape[2]))


def as_matrix(response):
    width = response.shape[1]
    return jnp.transpose(response, (1, 0, 3, 2, 4)).reshape(
        width, width, response.shape[2], response.shape[4]
    )


def as_vector(carry):
    return jnp.transpose(carry, (0, 2, 1, 3)).reshape(-1, carry.shape[1], carry.shape[3])


def from_vector(vector, count):
    return vector.reshape(2, count, vector.shape[1], vector.shape[2]).transpose(0, 2, 1, 3)


def carry_through(vector, matrix, offset):
    return jnp.einsum("kcl,kmcl->mcl", vector, matrix, precision=lax.Precision.HIGHEST) + offset


def shifted_operators(matrix, steps):
    count = lax.axis_size("gx")
    return [from_behind(matrix, "gx", steps * s) for s in range(1, count - 1)]


def gathered_carry(vector, operators, steps):
    count = lax.axis_size("gx")
    if count == 1:
        return jnp.zeros_like(vector)
    total = from_behind(vector, "gx", steps * (count - 1))
    for s in range(count - 2, 0, -1):
        total = jnp.sum(total[:, None] * operators[s - 1], axis=0) + from_behind(
            vector, "gx", steps * s
        )
    return total


def on_device(
    psi_old,
    objective_grad,
    near_upper,
    far_upper,
    inverse_diag,
    near_lower,
    far_lower,
    y_inverse,
    z_inverse,
    sens_terms,
    wall_mask,
    cond_index,
    weight_table,
):
    keep = (1.0 - wall_mask.astype(jnp.float32))[:, None, None, :]
    carry_shape = psi_old.shape[1:]
    zeros = jnp.zeros((2, 1) + carry_shape, jnp.float32)
    units = unit_carries(carry_shape)
    near_t = jnp.swapaxes(near_upper, 2, 3)
    far_t = jnp.swapaxes(far_upper, 2, 3)
    (response,) = upper_pallas(None, near_t, far_t, units, False)
    matrix = as_matrix(response)
    (response,) = lower_pallas(None, inverse_diag, near_lower, far_lower, units, False)
    reverse_matrix = as_matrix(response)
    upper_products = shifted_operators(matrix, 1)
    lower_products = shifted_operators(reverse_matrix, -1)
    psi = psi_old
    for step in range(ITERS):
        stream_pad = extended(psi, (("gx", 0),), 1)
        span_pad = extended(psi, (("gy", 3),), NZ)
        beside_all = (
            stream_pad[2:] + stream_pad[:-2] + span_pad[..., 2 * NZ :] + span_pad[..., : -2 * NZ]
        )
        rhs = objective_grad + 0.5 * beside_all - 2.0 * psi
        grid = rhs.reshape(rhs.shape[0], rhs.shape[1], rhs.shape[2], rhs.shape[3] // NZ, NZ)
        zres = jnp.einsum(
            "icvjq,cvqk->icvjk", grid, z_inverse, precision=lax.Precision.HIGHEST
        ).reshape(rhs.shape)
        yres = jnp.sum(y_inverse * zres[..., :, None, :], axis=-3)
        _, offset = upper_pallas(yres, near_t, far_t, zeros, True)
        entering = gathered_carry(as_vector(offset[:, 0]), upper_products, 1)
        upper, _ = upper_pallas(
            yres, near_t, far_t, from_vector(entering, carry_shape[1])[:, None], True
        )
        _, offset = lower_pallas(upper, inverse_diag, near_lower, far_lower, zeros, True)
        entering = gathered_carry(as_vector(offset[:, 0]), lower_products, -1)
        lower, _ = lower_pallas(
            upper,
            inverse_diag,
            near_lower,
            far_lower,
            from_vector(entering, carry_shape[1])[:, None],
            True,
        )
        psi = (psi + 0.05 * lower) * keep
    onehot = (cond_index[:, None] == jnp.arange(weight_table.shape[0])[None, :]).astype(jnp.float32)
    weights = jnp.sum(onehot * weight_table[None, :], axis=1)
    local_sens = jnp.einsum(
        "icvl,icmvl->iml",
        psi * weights[None, :, None, None],
        sens_terms,
        precision=lax.Precision.HIGHEST,
    )
    mesh_sens = lax.psum(local_sens, "cond")
    return (psi, mesh_sens)


def solution(mesh):
    placed = (
        P("gx", "cond", None, "gy"),
        P("gx", "cond", None, "gy"),
        P("gx", "cond", None, None, "gy"),
        P("gx", "cond", None, None, "gy"),
        P("gx", "cond", None, None, "gy"),
        P("gx", "cond", None, None, "gy"),
        P("gx", "cond", None, None, "gy"),
        P("gx", "cond", None, None, "gy"),
        P("cond", None, None, None),
        P("gx", "cond", None, None, "gy"),
        P("gx", "gy"),
        P("cond"),
        P(),
    )
    return jax.shard_map(
        on_device,
        mesh=mesh,
        in_specs=placed,
        out_specs=(P("gx", "cond", None, "gy"), P("gx", None, "gy")),
        check_vma=False,
    )
```

```python
import jax
import jax.numpy as jnp
from jax import lax
from jax.experimental import pallas as pl
from jax.experimental.pallas import tpu as pltpu
from jax.sharding import PartitionSpec as P

NZ = 32
ITERS = 2


def extended(value, sides, width):
    for axis, dim in sides:
        size, length = (lax.axis_size(axis), value.shape[dim])
        up = [(i, (i + 1) % size) for i in range(size - 1)]
        down = [(j, i) for i, j in up]
        last = lax.slice_in_dim(value, length - width, length, axis=dim)
        first = lax.slice_in_dim(value, 0, width, axis=dim)
        before = lax.ppermute(last, axis, up)
        after = lax.ppermute(first, axis, down)
        value = jnp.concatenate([before, value, after], axis=dim)
    return value


def from_behind(value, axis, steps):
    count = lax.axis_size(axis)
    first, last = (max(0, -steps), min(count, count - steps))
    return lax.ppermute(value, axis, [(source, source + steps) for source in range(first, last)])


def _vmem_specs(n):
    return [pl.BlockSpec(memory_space=pltpu.VMEM) for _ in range(n)]


def _rows_times(blocks_ref, index, vec):
    total = None
    for a in range(vec.shape[0]):
        term = blocks_ref[index + (a,)] * vec[a : a + 1, :]
        total = term if total is None else total + term
    return total


def _init_carry(carry_ref, inc_ref):
    if inc_ref is not None:
        carry_ref[...] = inc_ref[...]
        return
    slots, width, conds, nv, lanes = carry_ref.shape
    rows = lax.broadcasted_iota(jnp.int32, (nv, lanes), 0)
    for slot in range(slots):
        for k in range(width):
            unit = (rows == k - slot * nv).astype(jnp.float32)
            for c in range(conds):
                carry_ref[slot, k, c] = unit


def upper_pallas(rhs, near_t, far_t, incoming, want_values):
    count, conds, nv = near_t.shape[0], near_t.shape[1], near_t.shape[2]
    has_inc = not isinstance(incoming, tuple)
    shape = incoming.shape if has_inc else incoming
    width = shape[1]
    has_rhs = rhs is not None

    def kernel(*refs):
        refs = list(refs)
        rhs_ref = refs.pop(0) if has_rhs else None
        nt_ref, ft_ref = refs.pop(0), refs.pop(0)
        inc_ref = refs.pop(0) if has_inc else None
        outs = refs
        if want_values:
            val_ref, carry_ref = outs
        else:
            (carry_ref,) = outs
        _init_carry(carry_ref, inc_ref)

        def step(i, unused):
            for k in range(width):
                for c in range(conds):
                    last = carry_ref[0, k, c]
                    before = carry_ref[1, k, c]
                    acc = _rows_times(nt_ref, (i, c), last) + _rows_times(ft_ref, (i, c), before)
                    if has_rhs:
                        now = rhs_ref[i, c] - acc
                    else:
                        now = -acc
                    carry_ref[1, k, c] = last
                    carry_ref[0, k, c] = now
                    if want_values:
                        val_ref[i, c] = now
            return unused

        lax.fori_loop(0, count, step, 0)

    out_shape = [jax.ShapeDtypeStruct(shape, jnp.float32)]
    if want_values:
        out_shape = [jax.ShapeDtypeStruct(rhs.shape, jnp.float32)] + out_shape
    args = ([rhs] if has_rhs else []) + [near_t, far_t] + ([incoming] if has_inc else [])
    return pl.pallas_call(
        kernel,
        out_shape=tuple(out_shape),
        in_specs=_vmem_specs(len(args)),
        out_specs=tuple(_vmem_specs(len(out_shape))),
    )(*args)


def lower_pallas(rhs, inverse, near, far, incoming, want_values):
    count, conds, nv = inverse.shape[0], inverse.shape[1], inverse.shape[2]
    has_inc = not isinstance(incoming, tuple)
    shape = incoming.shape if has_inc else incoming
    width = shape[1]
    has_rhs = rhs is not None

    def kernel(*refs):
        refs = list(refs)
        rhs_ref = refs.pop(0) if has_rhs else None
        d_ref, b_ref, a_ref = refs.pop(0), refs.pop(0), refs.pop(0)
        inc_ref = refs.pop(0) if has_inc else None
        outs = refs
        if want_values:
            val_ref, carry_ref = outs
        else:
            (carry_ref,) = outs
        _init_carry(carry_ref, inc_ref)

        def step(t, unused):
            i = count - 1 - t
            for k in range(width):
                for c in range(conds):
                    pending = carry_ref[0, k, c]
                    partial_value = carry_ref[1, k, c]
                    if has_rhs:
                        r = rhs_ref[i, c] - pending
                    else:
                        r = -pending
                    now = _rows_times(d_ref, (i, c), r)
                    carry_ref[0, k, c] = partial_value + _rows_times(b_ref, (i, c), now)
                    carry_ref[1, k, c] = _rows_times(a_ref, (i, c), now)
                    if want_values:
                        val_ref[i, c] = now
            return unused

        lax.fori_loop(0, count, step, 0)

    out_shape = [jax.ShapeDtypeStruct(shape, jnp.float32)]
    if want_values:
        out_shape = [jax.ShapeDtypeStruct(rhs.shape, jnp.float32)] + out_shape
    args = ([rhs] if has_rhs else []) + [inverse, near, far] + ([incoming] if has_inc else [])
    return pl.pallas_call(
        kernel,
        out_shape=tuple(out_shape),
        in_specs=_vmem_specs(len(args)),
        out_specs=tuple(_vmem_specs(len(out_shape))),
    )(*args)


def carry_through(vector, response):
    slots, width, conds, nv, lanes = response.shape
    split = response.reshape(slots, slots, nv, conds, nv, lanes)
    inputs = jnp.transpose(vector, (0, 2, 1, 3))[None, :, :, :, None, :]
    return jnp.sum(jnp.sum(split * inputs, axis=2), axis=1)


def shifted_operators(matrix, steps):
    count = lax.axis_size("gx")
    return [from_behind(matrix, "gx", steps * s) for s in range(1, count - 1)]


def gathered_carry(vector, operators, steps):
    count = lax.axis_size("gx")
    if count == 1:
        return jnp.zeros_like(vector)
    total = from_behind(vector, "gx", steps * (count - 1))
    for s in range(count - 2, 0, -1):
        total = carry_through(total, operators[s - 1]) + from_behind(
            vector, "gx", steps * s
        )
    return total


def on_device(
    psi_old,
    objective_grad,
    near_upper,
    far_upper,
    inverse_diag,
    near_lower,
    far_lower,
    y_inverse,
    z_inverse,
    sens_terms,
    wall_mask,
    cond_index,
    weight_table,
):
    keep = (1.0 - wall_mask.astype(jnp.float32))[:, None, None, :]
    carry_shape = psi_old.shape[1:]
    zeros = jnp.zeros((2, 1) + carry_shape, jnp.float32)
    units = (2, 2 * carry_shape[1]) + carry_shape
    near_t = jnp.swapaxes(near_upper, 2, 3)
    far_t = jnp.swapaxes(far_upper, 2, 3)
    (response,) = upper_pallas(None, near_t, far_t, units, False)
    matrix = response
    (response,) = lower_pallas(None, inverse_diag, near_lower, far_lower, units, False)
    reverse_matrix = response
    upper_products = shifted_operators(matrix, 1)
    lower_products = shifted_operators(reverse_matrix, -1)
    psi = psi_old
    for step in range(ITERS):
        stream_pad = extended(psi, (("gx", 0),), 1)
        span_pad = extended(psi, (("gy", 3),), NZ)
        beside_all = (
            stream_pad[2:] + stream_pad[:-2] + span_pad[..., 2 * NZ :] + span_pad[..., : -2 * NZ]
        )
        rhs = objective_grad + 0.5 * beside_all - 2.0 * psi
        grid = rhs.reshape(rhs.shape[0], rhs.shape[1], rhs.shape[2], rhs.shape[3] // NZ, NZ)
        zres = jnp.einsum(
            "icvjq,cvqk->icvjk", grid, z_inverse, precision=lax.Precision.HIGHEST
        ).reshape(rhs.shape)
        yres = jnp.sum(y_inverse * zres[..., :, None, :], axis=-3)
        _, offset = upper_pallas(yres, near_t, far_t, zeros, True)
        entering = gathered_carry(offset[:, 0], upper_products, 1)
        upper, _ = upper_pallas(yres, near_t, far_t, entering[:, None], True)
        _, offset = lower_pallas(upper, inverse_diag, near_lower, far_lower, zeros, True)
        entering = gathered_carry(offset[:, 0], lower_products, -1)
        lower, _ = lower_pallas(upper, inverse_diag, near_lower, far_lower, entering[:, None], True)
        psi = (psi + 0.05 * lower) * keep
    onehot = (cond_index[:, None] == jnp.arange(weight_table.shape[0])[None, :]).astype(jnp.float32)
    weights = jnp.sum(onehot * weight_table[None, :], axis=1)
    local_sens = jnp.einsum(
        "icvl,icmvl->iml",
        psi * weights[None, :, None, None],
        sens_terms,
        precision=lax.Precision.HIGHEST,
    )
    if lax.axis_size("cond") == 2:
        mesh_sens = local_sens + lax.ppermute(local_sens, "cond", [(0, 1), (1, 0)])
    else:
        mesh_sens = lax.psum(local_sens, "cond")
    return (psi, mesh_sens)


def solution(mesh):
    placed = (
        P("gx", "cond", None, "gy"),
        P("gx", "cond", None, "gy"),
        P("gx", "cond", None, None, "gy"),
        P("gx", "cond", None, None, "gy"),
        P("gx", "cond", None, None, "gy"),
        P("gx", "cond", None, None, "gy"),
        P("gx", "cond", None, None, "gy"),
        P("gx", "cond", None, None, "gy"),
        P("cond", None, None, None),
        P("gx", "cond", None, None, "gy"),
        P("gx", "gy"),
        P("cond"),
        P(),
    )
    return jax.shard_map(
        on_device,
        mesh=mesh,
        in_specs=placed,
        out_specs=(P("gx", "cond", None, "gy"), P("gx", None, "gy")),
        check_vma=False,
    )
```

```python
import jax
import jax.numpy as jnp
from jax import lax
from jax.experimental import pallas as pl
from jax.experimental.pallas import tpu as pltpu
from jax.sharding import PartitionSpec as P

NZ = 32
ITERS = 2


def extended(value, sides, width):
    for axis, dim in sides:
        size, length = (lax.axis_size(axis), value.shape[dim])
        up = [(i, (i + 1) % size) for i in range(size - 1)]
        down = [(j, i) for i, j in up]
        last = lax.slice_in_dim(value, length - width, length, axis=dim)
        first = lax.slice_in_dim(value, 0, width, axis=dim)
        before = lax.ppermute(last, axis, up)
        after = lax.ppermute(first, axis, down)
        value = jnp.concatenate([before, value, after], axis=dim)
    return value


def from_behind(value, axis, steps):
    count = lax.axis_size(axis)
    first, last = (max(0, -steps), min(count, count - steps))
    return lax.ppermute(value, axis, [(source, source + steps) for source in range(first, last)])


def _vmem_specs(n):
    return [pl.BlockSpec(memory_space=pltpu.VMEM) for _ in range(n)]


def _rows_times(blocks_ref, index, vec):
    total = None
    for a in range(vec.shape[0]):
        term = blocks_ref[index + (a,)] * vec[a : a + 1, :]
        total = term if total is None else total + term
    return total


def _init_carry(carry_ref, inc_ref):
    if inc_ref is not None:
        carry_ref[...] = inc_ref[...]
        return
    slots, width, conds, nv, lanes = carry_ref.shape
    rows = lax.broadcasted_iota(jnp.int32, (nv, lanes), 0)
    for slot in range(slots):
        for k in range(width):
            unit = (rows == k - slot * nv).astype(jnp.float32)
            for c in range(conds):
                carry_ref[slot, k, c] = unit


def upper_pallas(rhs, near_t, far_t, incoming, want_values):
    count, conds, nv = near_t.shape[0], near_t.shape[1], near_t.shape[2]
    has_inc = not isinstance(incoming, tuple)
    shape = incoming.shape if has_inc else incoming
    width = shape[1]
    has_rhs = rhs is not None

    def kernel(*refs):
        refs = list(refs)
        rhs_ref = refs.pop(0) if has_rhs else None
        nt_ref, ft_ref = refs.pop(0), refs.pop(0)
        inc_ref = refs.pop(0) if has_inc else None
        outs = refs
        if want_values:
            val_ref, carry_ref = outs
        else:
            (carry_ref,) = outs
        _init_carry(carry_ref, inc_ref)

        def step(i, unused):
            for k in range(width):
                for c in range(conds):
                    last = carry_ref[0, k, c]
                    before = carry_ref[1, k, c]
                    acc = _rows_times(nt_ref, (i, c), last) + _rows_times(ft_ref, (i, c), before)
                    if has_rhs:
                        now = rhs_ref[i, c] - acc
                    else:
                        now = -acc
                    carry_ref[1, k, c] = last
                    carry_ref[0, k, c] = now
                    if want_values:
                        val_ref[i, c] = now
            return unused

        lax.fori_loop(0, count, step, 0)

    out_shape = [jax.ShapeDtypeStruct(shape, jnp.float32)]
    if want_values:
        out_shape = [jax.ShapeDtypeStruct(rhs.shape, jnp.float32)] + out_shape
    args = ([rhs] if has_rhs else []) + [near_t, far_t] + ([incoming] if has_inc else [])
    return pl.pallas_call(
        kernel,
        out_shape=tuple(out_shape),
        in_specs=_vmem_specs(len(args)),
        out_specs=tuple(_vmem_specs(len(out_shape))),
    )(*args)


def lower_pallas(rhs, inverse, near, far, incoming, want_values):
    count, conds, nv = inverse.shape[0], inverse.shape[1], inverse.shape[2]
    has_inc = not isinstance(incoming, tuple)
    shape = incoming.shape if has_inc else incoming
    width = shape[1]
    has_rhs = rhs is not None

    def kernel(*refs):
        refs = list(refs)
        rhs_ref = refs.pop(0) if has_rhs else None
        d_ref, b_ref, a_ref = refs.pop(0), refs.pop(0), refs.pop(0)
        inc_ref = refs.pop(0) if has_inc else None
        outs = refs
        if want_values:
            val_ref, carry_ref = outs
        else:
            (carry_ref,) = outs
        _init_carry(carry_ref, inc_ref)

        def step(t, unused):
            i = count - 1 - t
            for k in range(width):
                for c in range(conds):
                    pending = carry_ref[0, k, c]
                    partial_value = carry_ref[1, k, c]
                    if has_rhs:
                        r = rhs_ref[i, c] - pending
                    else:
                        r = -pending
                    now = _rows_times(d_ref, (i, c), r)
                    carry_ref[0, k, c] = partial_value + _rows_times(b_ref, (i, c), now)
                    carry_ref[1, k, c] = _rows_times(a_ref, (i, c), now)
                    if want_values:
                        val_ref[i, c] = now
            return unused

        lax.fori_loop(0, count, step, 0)

    out_shape = [jax.ShapeDtypeStruct(shape, jnp.float32)]
    if want_values:
        out_shape = [jax.ShapeDtypeStruct(rhs.shape, jnp.float32)] + out_shape
    args = ([rhs] if has_rhs else []) + [inverse, near, far] + ([incoming] if has_inc else [])
    return pl.pallas_call(
        kernel,
        out_shape=tuple(out_shape),
        in_specs=_vmem_specs(len(args)),
        out_specs=tuple(_vmem_specs(len(out_shape))),
    )(*args)


def carry_through(vector, response):
    slots, width, conds, nv, lanes = response.shape
    split = response.reshape(slots, slots, nv, conds, nv, lanes)
    inputs = jnp.transpose(vector, (0, 2, 1, 3))[None, :, :, :, None, :]
    return jnp.sum(jnp.sum(split * inputs, axis=2), axis=1)


def shifted_operators(matrix, steps):
    count = lax.axis_size("gx")
    return [from_behind(matrix, "gx", steps * s) for s in range(1, count - 1)]


def gathered_carry(vector, operators, steps):
    count = lax.axis_size("gx")
    if count == 1:
        return jnp.zeros_like(vector)
    total = from_behind(vector, "gx", steps * (count - 1))
    for s in range(count - 2, 0, -1):
        total = carry_through(total, operators[s - 1]) + from_behind(
            vector, "gx", steps * s
        )
    return total


def on_device(
    psi_old,
    objective_grad,
    near_upper,
    far_upper,
    inverse_diag,
    near_lower,
    far_lower,
    y_inverse,
    z_inverse,
    sens_terms,
    wall_mask,
    cond_index,
    weight_table,
):
    keep = (1.0 - wall_mask.astype(jnp.float32))[:, None, None, :]
    carry_shape = psi_old.shape[1:]
    zeros = jnp.zeros((2, 1) + carry_shape, jnp.float32)
    units = (2, 2 * carry_shape[1]) + carry_shape
    near_t = jnp.swapaxes(near_upper, 2, 3)
    far_t = jnp.swapaxes(far_upper, 2, 3)
    (response,) = upper_pallas(None, near_t, far_t, units, False)
    matrix = response
    (response,) = lower_pallas(None, inverse_diag, near_lower, far_lower, units, False)
    reverse_matrix = response
    upper_products = shifted_operators(matrix, 1)
    lower_products = shifted_operators(reverse_matrix, -1)
    psi = psi_old
    for step in range(ITERS):
        stream_pad = extended(psi, (("gx", 0),), 1)
        span_pad = extended(psi, (("gy", 3),), NZ)
        beside_all = (
            stream_pad[2:] + stream_pad[:-2] + span_pad[..., 2 * NZ :] + span_pad[..., : -2 * NZ]
        )
        rhs = objective_grad + 0.5 * beside_all - 2.0 * psi
        grid = rhs.reshape(rhs.shape[0], rhs.shape[1], rhs.shape[2], rhs.shape[3] // NZ, NZ)
        zres = jnp.einsum(
            "icvjq,cvqk->icvjk", grid, z_inverse, precision=lax.Precision.HIGHEST
        ).reshape(rhs.shape)
        yres = jnp.sum(y_inverse * zres[..., :, None, :], axis=-3)
        if step == 0:
            yres, _ = lax.optimization_barrier((yres, reverse_matrix))
        _, offset = upper_pallas(yres, near_t, far_t, zeros, True)
        entering = gathered_carry(offset[:, 0], upper_products, 1)
        upper, _ = upper_pallas(yres, near_t, far_t, entering[:, None], True)
        _, offset = lower_pallas(upper, inverse_diag, near_lower, far_lower, zeros, True)
        entering = gathered_carry(offset[:, 0], lower_products, -1)
        lower, _ = lower_pallas(upper, inverse_diag, near_lower, far_lower, entering[:, None], True)
        psi = (psi + 0.05 * lower) * keep
    onehot = (cond_index[:, None] == jnp.arange(weight_table.shape[0])[None, :]).astype(jnp.float32)
    weights = jnp.sum(onehot * weight_table[None, :], axis=1)
    local_sens = jnp.einsum(
        "icvl,icmvl->iml",
        psi * weights[None, :, None, None],
        sens_terms,
        precision=lax.Precision.HIGHEST,
    )
    if lax.axis_size("cond") == 2:
        mesh_sens = local_sens + lax.ppermute(local_sens, "cond", [(0, 1), (1, 0)])
    else:
        mesh_sens = lax.psum(local_sens, "cond")
    return (psi, mesh_sens)


def solution(mesh):
    placed = (
        P("gx", "cond", None, "gy"),
        P("gx", "cond", None, "gy"),
        P("gx", "cond", None, None, "gy"),
        P("gx", "cond", None, None, "gy"),
        P("gx", "cond", None, None, "gy"),
        P("gx", "cond", None, None, "gy"),
        P("gx", "cond", None, None, "gy"),
        P("gx", "cond", None, None, "gy"),
        P("cond", None, None, None),
        P("gx", "cond", None, None, "gy"),
        P("gx", "gy"),
        P("cond"),
        P(),
    )
    return jax.shard_map(
        on_device,
        mesh=mesh,
        in_specs=placed,
        out_specs=(P("gx", "cond", None, "gy"), P("gx", None, "gy")),
        check_vma=False,
    )
```

```python
import jax
import jax.numpy as jnp
from jax import lax
from jax.experimental import pallas as pl
from jax.experimental.pallas import tpu as pltpu
from jax.sharding import PartitionSpec as P

NZ = 32
ITERS = 2


def extended(value, sides, width):
    for axis, dim in sides:
        size, length = (lax.axis_size(axis), value.shape[dim])
        up = [(i, (i + 1) % size) for i in range(size - 1)]
        down = [(j, i) for i, j in up]
        last = lax.slice_in_dim(value, length - width, length, axis=dim)
        first = lax.slice_in_dim(value, 0, width, axis=dim)
        before = lax.ppermute(last, axis, up)
        after = lax.ppermute(first, axis, down)
        value = jnp.concatenate([before, value, after], axis=dim)
    return value


def from_behind(value, axis, steps):
    count = lax.axis_size(axis)
    first, last = (max(0, -steps), min(count, count - steps))
    return lax.ppermute(value, axis, [(source, source + steps) for source in range(first, last)])


def _vmem_specs(n):
    return [pl.BlockSpec(memory_space=pltpu.VMEM) for _ in range(n)]


def _rows_times(blocks_ref, index, vec):
    i, c = index
    nv = vec.shape[0]
    total = None
    for a in range(nv):
        rows = blocks_ref[i, pl.ds((c * nv + a) * nv, nv), :]
        term = rows * vec[a : a + 1, :]
        total = term if total is None else total + term
    return total


def dense(blocks):
    return blocks.reshape(blocks.shape[0], -1, blocks.shape[-1])


def _init_carry(carry_ref, inc_ref):
    if inc_ref is not None:
        carry_ref[...] = inc_ref[...]
        return
    slots, width, conds, nv, lanes = carry_ref.shape
    rows = lax.broadcasted_iota(jnp.int32, (nv, lanes), 0)
    for slot in range(slots):
        for k in range(width):
            unit = (rows == k - slot * nv).astype(jnp.float32)
            for c in range(conds):
                carry_ref[slot, k, c] = unit


def upper_pallas(rhs, near_t, far_t, incoming, want_values):
    count, conds, nv = near_t.shape[0], near_t.shape[1], near_t.shape[2]
    near_t, far_t = dense(near_t), dense(far_t)
    has_inc = not isinstance(incoming, tuple)
    shape = incoming.shape if has_inc else incoming
    width = shape[1]
    has_rhs = rhs is not None

    def kernel(*refs):
        refs = list(refs)
        rhs_ref = refs.pop(0) if has_rhs else None
        nt_ref, ft_ref = refs.pop(0), refs.pop(0)
        inc_ref = refs.pop(0) if has_inc else None
        outs = refs
        if want_values:
            val_ref, carry_ref = outs
        else:
            (carry_ref,) = outs
        _init_carry(carry_ref, inc_ref)

        def step(i, unused):
            for k in range(width):
                for c in range(conds):
                    last = carry_ref[0, k, c]
                    before = carry_ref[1, k, c]
                    acc = _rows_times(nt_ref, (i, c), last) + _rows_times(ft_ref, (i, c), before)
                    if has_rhs:
                        now = rhs_ref[i, c] - acc
                    else:
                        now = -acc
                    carry_ref[1, k, c] = last
                    carry_ref[0, k, c] = now
                    if want_values:
                        val_ref[i, c] = now
            return unused

        lax.fori_loop(0, count, step, 0)

    out_shape = [jax.ShapeDtypeStruct(shape, jnp.float32)]
    if want_values:
        out_shape = [jax.ShapeDtypeStruct(rhs.shape, jnp.float32)] + out_shape
    args = ([rhs] if has_rhs else []) + [near_t, far_t] + ([incoming] if has_inc else [])
    return pl.pallas_call(
        kernel,
        out_shape=tuple(out_shape),
        in_specs=_vmem_specs(len(args)),
        out_specs=tuple(_vmem_specs(len(out_shape))),
    )(*args)


def lower_pallas(rhs, inverse, near, far, incoming, want_values):
    count, conds, nv = inverse.shape[0], inverse.shape[1], inverse.shape[2]
    inverse, near, far = dense(inverse), dense(near), dense(far)
    has_inc = not isinstance(incoming, tuple)
    shape = incoming.shape if has_inc else incoming
    width = shape[1]
    has_rhs = rhs is not None

    def kernel(*refs):
        refs = list(refs)
        rhs_ref = refs.pop(0) if has_rhs else None
        d_ref, b_ref, a_ref = refs.pop(0), refs.pop(0), refs.pop(0)
        inc_ref = refs.pop(0) if has_inc else None
        outs = refs
        if want_values:
            val_ref, carry_ref = outs
        else:
            (carry_ref,) = outs
        _init_carry(carry_ref, inc_ref)

        def step(t, unused):
            i = count - 1 - t
            for k in range(width):
                for c in range(conds):
                    pending = carry_ref[0, k, c]
                    partial_value = carry_ref[1, k, c]
                    if has_rhs:
                        r = rhs_ref[i, c] - pending
                    else:
                        r = -pending
                    now = _rows_times(d_ref, (i, c), r)
                    carry_ref[0, k, c] = partial_value + _rows_times(b_ref, (i, c), now)
                    carry_ref[1, k, c] = _rows_times(a_ref, (i, c), now)
                    if want_values:
                        val_ref[i, c] = now
            return unused

        lax.fori_loop(0, count, step, 0)

    out_shape = [jax.ShapeDtypeStruct(shape, jnp.float32)]
    if want_values:
        out_shape = [jax.ShapeDtypeStruct(rhs.shape, jnp.float32)] + out_shape
    args = ([rhs] if has_rhs else []) + [inverse, near, far] + ([incoming] if has_inc else [])
    return pl.pallas_call(
        kernel,
        out_shape=tuple(out_shape),
        in_specs=_vmem_specs(len(args)),
        out_specs=tuple(_vmem_specs(len(out_shape))),
    )(*args)


def carry_through(vector, response):
    slots, width, conds, nv, lanes = response.shape
    split = response.reshape(slots, slots, nv, conds, nv, lanes)
    inputs = jnp.transpose(vector, (0, 2, 1, 3))[None, :, :, :, None, :]
    return jnp.sum(jnp.sum(split * inputs, axis=2), axis=1)


def shifted_operators(matrix, steps):
    count = lax.axis_size("gx")
    return [from_behind(matrix, "gx", steps * s) for s in range(1, count - 1)]


def gathered_carry(vector, operators, steps):
    count = lax.axis_size("gx")
    if count == 1:
        return jnp.zeros_like(vector)
    total = from_behind(vector, "gx", steps * (count - 1))
    for s in range(count - 2, 0, -1):
        total = carry_through(total, operators[s - 1]) + from_behind(
            vector, "gx", steps * s
        )
    return total


def on_device(
    psi_old,
    objective_grad,
    near_upper,
    far_upper,
    inverse_diag,
    near_lower,
    far_lower,
    y_inverse,
    z_inverse,
    sens_terms,
    wall_mask,
    cond_index,
    weight_table,
):
    keep = (1.0 - wall_mask.astype(jnp.float32))[:, None, None, :]
    carry_shape = psi_old.shape[1:]
    zeros = jnp.zeros((2, 1) + carry_shape, jnp.float32)
    units = (2, 2 * carry_shape[1]) + carry_shape
    near_t = jnp.swapaxes(near_upper, 2, 3)
    far_t = jnp.swapaxes(far_upper, 2, 3)
    (response,) = upper_pallas(None, near_t, far_t, units, False)
    matrix = response
    (response,) = lower_pallas(None, inverse_diag, near_lower, far_lower, units, False)
    reverse_matrix = response
    upper_products = shifted_operators(matrix, 1)
    lower_products = shifted_operators(reverse_matrix, -1)
    psi = psi_old
    for step in range(ITERS):
        stream_pad = extended(psi, (("gx", 0),), 1)
        span_pad = extended(psi, (("gy", 3),), NZ)
        beside_all = (
            stream_pad[2:] + stream_pad[:-2] + span_pad[..., 2 * NZ :] + span_pad[..., : -2 * NZ]
        )
        rhs = objective_grad + 0.5 * beside_all - 2.0 * psi
        grid = rhs.reshape(rhs.shape[0], rhs.shape[1], rhs.shape[2], rhs.shape[3] // NZ, NZ)
        zres = jnp.einsum(
            "icvjq,cvqk->icvjk", grid, z_inverse, precision=lax.Precision.HIGHEST
        ).reshape(rhs.shape)
        yres = jnp.sum(y_inverse * zres[..., :, None, :], axis=-3)
        if step == 0:
            yres, _ = lax.optimization_barrier((yres, reverse_matrix))
        _, offset = upper_pallas(yres, near_t, far_t, zeros, True)
        entering = gathered_carry(offset[:, 0], upper_products, 1)
        upper, _ = upper_pallas(yres, near_t, far_t, entering[:, None], True)
        _, offset = lower_pallas(upper, inverse_diag, near_lower, far_lower, zeros, True)
        entering = gathered_carry(offset[:, 0], lower_products, -1)
        lower, _ = lower_pallas(upper, inverse_diag, near_lower, far_lower, entering[:, None], True)
        psi = (psi + 0.05 * lower) * keep
    onehot = (cond_index[:, None] == jnp.arange(weight_table.shape[0])[None, :]).astype(jnp.float32)
    weights = jnp.sum(onehot * weight_table[None, :], axis=1)
    local_sens = jnp.einsum(
        "icvl,icmvl->iml",
        psi * weights[None, :, None, None],
        sens_terms,
        precision=lax.Precision.HIGHEST,
    )
    if lax.axis_size("cond") == 2:
        mesh_sens = local_sens + lax.ppermute(local_sens, "cond", [(0, 1), (1, 0)])
    else:
        mesh_sens = lax.psum(local_sens, "cond")
    return (psi, mesh_sens)


def solution(mesh):
    placed = (
        P("gx", "cond", None, "gy"),
        P("gx", "cond", None, "gy"),
        P("gx", "cond", None, None, "gy"),
        P("gx", "cond", None, None, "gy"),
        P("gx", "cond", None, None, "gy"),
        P("gx", "cond", None, None, "gy"),
        P("gx", "cond", None, None, "gy"),
        P("gx", "cond", None, None, "gy"),
        P("cond", None, None, None),
        P("gx", "cond", None, None, "gy"),
        P("gx", "gy"),
        P("cond"),
        P(),
    )
    return jax.shard_map(
        on_device,
        mesh=mesh,
        in_specs=placed,
        out_specs=(P("gx", "cond", None, "gy"), P("gx", None, "gy")),
        check_vma=False,
    )
```

```python
import jax
import jax.numpy as jnp
from jax import lax
from jax.experimental import pallas as pl
from jax.experimental.pallas import tpu as pltpu
from jax.sharding import PartitionSpec as P

NZ = 32
ITERS = 2


def extended(value, sides, width):
    for axis, dim in sides:
        size, length = (lax.axis_size(axis), value.shape[dim])
        up = [(i, (i + 1) % size) for i in range(size - 1)]
        down = [(j, i) for i, j in up]
        last = lax.slice_in_dim(value, length - width, length, axis=dim)
        first = lax.slice_in_dim(value, 0, width, axis=dim)
        before = lax.ppermute(last, axis, up)
        after = lax.ppermute(first, axis, down)
        value = jnp.concatenate([before, value, after], axis=dim)
    return value


def from_behind(value, axis, steps):
    count = lax.axis_size(axis)
    first, last = (max(0, -steps), min(count, count - steps))
    return lax.ppermute(value, axis, [(source, source + steps) for source in range(first, last)])


def _vmem_specs(n):
    return [pl.BlockSpec(memory_space=pltpu.VMEM) for _ in range(n)]


def _rows_times(blocks_ref, index, vec):
    terms = [blocks_ref[index + (a,)] * vec[a : a + 1, :] for a in range(vec.shape[0])]
    while len(terms) > 1:
        paired = [terms[j] + terms[j + 1] for j in range(0, len(terms) - 1, 2)]
        if len(terms) % 2:
            paired.append(terms[-1])
        terms = paired
    return terms[0]


def _init_carry(carry_ref, inc_ref):
    if inc_ref is not None:
        carry_ref[...] = inc_ref[...]
        return
    slots, width, conds, nv, lanes = carry_ref.shape
    rows = lax.broadcasted_iota(jnp.int32, (nv, lanes), 0)
    for slot in range(slots):
        for k in range(width):
            unit = (rows == k - slot * nv).astype(jnp.float32)
            for c in range(conds):
                carry_ref[slot, k, c] = unit


def upper_pallas(rhs, near_t, far_t, incoming, want_values):
    count, conds, nv = near_t.shape[0], near_t.shape[1], near_t.shape[2]
    has_inc = not isinstance(incoming, tuple)
    shape = incoming.shape if has_inc else incoming
    width = shape[1]
    has_rhs = rhs is not None

    def kernel(*refs):
        refs = list(refs)
        rhs_ref = refs.pop(0) if has_rhs else None
        nt_ref, ft_ref = refs.pop(0), refs.pop(0)
        inc_ref = refs.pop(0) if has_inc else None
        outs = refs
        if want_values:
            val_ref, carry_ref = outs
        else:
            (carry_ref,) = outs
        if width == 1:
            lasts = [inc_ref[0, 0, c] for c in range(conds)]
            befores = [inc_ref[1, 0, c] for c in range(conds)]
            for i in range(count):
                for c in range(conds):
                    acc = _rows_times(nt_ref, (i, c), lasts[c]) + _rows_times(
                        ft_ref, (i, c), befores[c]
                    )
                    now = rhs_ref[i, c] - acc
                    befores[c] = lasts[c]
                    lasts[c] = now
                    if want_values:
                        val_ref[i, c] = now
            for c in range(conds):
                carry_ref[0, 0, c] = lasts[c]
                carry_ref[1, 0, c] = befores[c]
            return
        _init_carry(carry_ref, inc_ref)

        def step(i, unused):
            for k in range(width):
                for c in range(conds):
                    last = carry_ref[0, k, c]
                    before = carry_ref[1, k, c]
                    acc = _rows_times(nt_ref, (i, c), last) + _rows_times(ft_ref, (i, c), before)
                    if has_rhs:
                        now = rhs_ref[i, c] - acc
                    else:
                        now = -acc
                    carry_ref[1, k, c] = last
                    carry_ref[0, k, c] = now
                    if want_values:
                        val_ref[i, c] = now
            return unused

        lax.fori_loop(0, count, step, 0)

    out_shape = [jax.ShapeDtypeStruct(shape, jnp.float32)]
    if want_values:
        out_shape = [jax.ShapeDtypeStruct(rhs.shape, jnp.float32)] + out_shape
    args = ([rhs] if has_rhs else []) + [near_t, far_t] + ([incoming] if has_inc else [])
    return pl.pallas_call(
        kernel,
        out_shape=tuple(out_shape),
        in_specs=_vmem_specs(len(args)),
        out_specs=tuple(_vmem_specs(len(out_shape))),
    )(*args)


def lower_pallas(rhs, inverse, near, far, incoming, want_values):
    count, conds, nv = inverse.shape[0], inverse.shape[1], inverse.shape[2]
    has_inc = not isinstance(incoming, tuple)
    shape = incoming.shape if has_inc else incoming
    width = shape[1]
    has_rhs = rhs is not None

    def kernel(*refs):
        refs = list(refs)
        rhs_ref = refs.pop(0) if has_rhs else None
        d_ref, b_ref, a_ref = refs.pop(0), refs.pop(0), refs.pop(0)
        inc_ref = refs.pop(0) if has_inc else None
        outs = refs
        if want_values:
            val_ref, carry_ref = outs
        else:
            (carry_ref,) = outs
        if width == 1:
            pendings = [inc_ref[0, 0, c] for c in range(conds)]
            partials = [inc_ref[1, 0, c] for c in range(conds)]
            for i in range(count - 1, -1, -1):
                for c in range(conds):
                    now = _rows_times(d_ref, (i, c), rhs_ref[i, c] - pendings[c])
                    pendings[c] = partials[c] + _rows_times(b_ref, (i, c), now)
                    partials[c] = _rows_times(a_ref, (i, c), now)
                    if want_values:
                        val_ref[i, c] = now
            for c in range(conds):
                carry_ref[0, 0, c] = pendings[c]
                carry_ref[1, 0, c] = partials[c]
            return
        _init_carry(carry_ref, inc_ref)

        def step(t, unused):
            i = count - 1 - t
            for k in range(width):
                for c in range(conds):
                    pending = carry_ref[0, k, c]
                    partial_value = carry_ref[1, k, c]
                    if has_rhs:
                        r = rhs_ref[i, c] - pending
                    else:
                        r = -pending
                    now = _rows_times(d_ref, (i, c), r)
                    carry_ref[0, k, c] = partial_value + _rows_times(b_ref, (i, c), now)
                    carry_ref[1, k, c] = _rows_times(a_ref, (i, c), now)
                    if want_values:
                        val_ref[i, c] = now
            return unused

        lax.fori_loop(0, count, step, 0)

    out_shape = [jax.ShapeDtypeStruct(shape, jnp.float32)]
    if want_values:
        out_shape = [jax.ShapeDtypeStruct(rhs.shape, jnp.float32)] + out_shape
    args = ([rhs] if has_rhs else []) + [inverse, near, far] + ([incoming] if has_inc else [])
    return pl.pallas_call(
        kernel,
        out_shape=tuple(out_shape),
        in_specs=_vmem_specs(len(args)),
        out_specs=tuple(_vmem_specs(len(out_shape))),
    )(*args)


def carry_through(vector, response):
    slots, width, conds, nv, lanes = response.shape
    split = response.reshape(slots, slots, nv, conds, nv, lanes)
    inputs = jnp.transpose(vector, (0, 2, 1, 3))[None, :, :, :, None, :]
    return jnp.sum(jnp.sum(split * inputs, axis=2), axis=1)


def shifted_operators(matrix, steps):
    count = lax.axis_size("gx")
    return [from_behind(matrix, "gx", steps * s) for s in range(1, count - 1)]


def gathered_carry(vector, operators, steps):
    count = lax.axis_size("gx")
    if count == 1:
        return jnp.zeros_like(vector)
    total = from_behind(vector, "gx", steps * (count - 1))
    for s in range(count - 2, 0, -1):
        total = carry_through(total, operators[s - 1]) + from_behind(
            vector, "gx", steps * s
        )
    return total


def on_device(
    psi_old,
    objective_grad,
    near_upper,
    far_upper,
    inverse_diag,
    near_lower,
    far_lower,
    y_inverse,
    z_inverse,
    sens_terms,
    wall_mask,
    cond_index,
    weight_table,
):
    keep = (1.0 - wall_mask.astype(jnp.float32))[:, None, None, :]
    carry_shape = psi_old.shape[1:]
    zeros = jnp.zeros((2, 1) + carry_shape, jnp.float32)
    units = (2, 2 * carry_shape[1]) + carry_shape
    near_t = jnp.swapaxes(near_upper, 2, 3)
    far_t = jnp.swapaxes(far_upper, 2, 3)
    (response,) = upper_pallas(None, near_t, far_t, units, False)
    matrix = response
    (response,) = lower_pallas(None, inverse_diag, near_lower, far_lower, units, False)
    reverse_matrix = response
    upper_products = shifted_operators(matrix, 1)
    lower_products = shifted_operators(reverse_matrix, -1)
    psi = psi_old
    for step in range(ITERS):
        stream_pad = extended(psi, (("gx", 0),), 1)
        span_pad = extended(psi, (("gy", 3),), NZ)
        beside_all = (
            stream_pad[2:] + stream_pad[:-2] + span_pad[..., 2 * NZ :] + span_pad[..., : -2 * NZ]
        )
        rhs = objective_grad + 0.5 * beside_all - 2.0 * psi
        grid = rhs.reshape(rhs.shape[0], rhs.shape[1], rhs.shape[2], rhs.shape[3] // NZ, NZ)
        zres = jnp.einsum(
            "icvjq,cvqk->icvjk", grid, z_inverse, precision=lax.Precision.HIGHEST
        ).reshape(rhs.shape)
        yres = jnp.sum(y_inverse * zres[..., :, None, :], axis=-3)
        _, offset = upper_pallas(yres, near_t, far_t, zeros, True)
        entering = gathered_carry(offset[:, 0], upper_products, 1)
        upper, _ = upper_pallas(yres, near_t, far_t, entering[:, None], True)
        _, offset = lower_pallas(upper, inverse_diag, near_lower, far_lower, zeros, True)
        entering = gathered_carry(offset[:, 0], lower_products, -1)
        lower, _ = lower_pallas(upper, inverse_diag, near_lower, far_lower, entering[:, None], True)
        psi = (psi + 0.05 * lower) * keep
    onehot = (cond_index[:, None] == jnp.arange(weight_table.shape[0])[None, :]).astype(jnp.float32)
    weights = jnp.sum(onehot * weight_table[None, :], axis=1)
    local_sens = jnp.einsum(
        "icvl,icmvl->iml",
        psi * weights[None, :, None, None],
        sens_terms,
        precision=lax.Precision.HIGHEST,
    )
    if lax.axis_size("cond") == 2:
        mesh_sens = local_sens + lax.ppermute(local_sens, "cond", [(0, 1), (1, 0)])
    else:
        mesh_sens = lax.psum(local_sens, "cond")
    return (psi, mesh_sens)


def solution(mesh):
    placed = (
        P("gx", "cond", None, "gy"),
        P("gx", "cond", None, "gy"),
        P("gx", "cond", None, None, "gy"),
        P("gx", "cond", None, None, "gy"),
        P("gx", "cond", None, None, "gy"),
        P("gx", "cond", None, None, "gy"),
        P("gx", "cond", None, None, "gy"),
        P("gx", "cond", None, None, "gy"),
        P("cond", None, None, None),
        P("gx", "cond", None, None, "gy"),
        P("gx", "gy"),
        P("cond"),
        P(),
    )
    return jax.shard_map(
        on_device,
        mesh=mesh,
        in_specs=placed,
        out_specs=(P("gx", "cond", None, "gy"), P("gx", None, "gy")),
        check_vma=False,
    )
```

```python
import jax
import jax.numpy as jnp
from jax import lax
from jax.experimental import pallas as pl
from jax.experimental.pallas import tpu as pltpu
from jax.sharding import PartitionSpec as P

NZ = 32
ITERS = 2


def extended(value, sides, width):
    for axis, dim in sides:
        size, length = (lax.axis_size(axis), value.shape[dim])
        up = [(i, (i + 1) % size) for i in range(size - 1)]
        down = [(j, i) for i, j in up]
        last = lax.slice_in_dim(value, length - width, length, axis=dim)
        first = lax.slice_in_dim(value, 0, width, axis=dim)
        before = lax.ppermute(last, axis, up)
        after = lax.ppermute(first, axis, down)
        value = jnp.concatenate([before, value, after], axis=dim)
    return value


def from_behind(value, axis, steps):
    count = lax.axis_size(axis)
    first, last = (max(0, -steps), min(count, count - steps))
    return lax.ppermute(value, axis, [(source, source + steps) for source in range(first, last)])


def _vmem_specs(n):
    return [pl.BlockSpec(memory_space=pltpu.VMEM) for _ in range(n)]


def _rows_times(blocks_ref, index, vec):
    terms = [blocks_ref[index + (a,)] * vec[a : a + 1, :] for a in range(vec.shape[0])]
    while len(terms) > 1:
        paired = [terms[j] + terms[j + 1] for j in range(0, len(terms) - 1, 2)]
        if len(terms) % 2:
            paired.append(terms[-1])
        terms = paired
    return terms[0]


def _init_carry(carry_ref, inc_ref):
    if inc_ref is not None:
        carry_ref[...] = inc_ref[...]
        return
    slots, width, conds, nv, lanes = carry_ref.shape
    rows = lax.broadcasted_iota(jnp.int32, (nv, lanes), 0)
    for slot in range(slots):
        for k in range(width):
            unit = (rows == k - slot * nv).astype(jnp.float32)
            for c in range(conds):
                carry_ref[slot, k, c] = unit


def upper_pallas(rhs, near_t, far_t, incoming, want_values):
    count, conds, nv = near_t.shape[0], near_t.shape[1], near_t.shape[2]
    has_inc = not isinstance(incoming, tuple)
    shape = incoming.shape if has_inc else incoming
    width = shape[1]
    has_rhs = rhs is not None

    def kernel(*refs):
        refs = list(refs)
        rhs_ref = refs.pop(0) if has_rhs else None
        nt_ref, ft_ref = refs.pop(0), refs.pop(0)
        inc_ref = refs.pop(0) if has_inc else None
        outs = refs
        if want_values:
            val_ref, carry_ref = outs
        else:
            (carry_ref,) = outs
        if width == 1:
            lasts = [inc_ref[0, 0, c] for c in range(conds)]
            befores = [inc_ref[1, 0, c] for c in range(conds)]
            for i in range(count):
                for c in range(conds):
                    acc = _rows_times(nt_ref, (i, c), lasts[c]) + _rows_times(
                        ft_ref, (i, c), befores[c]
                    )
                    now = rhs_ref[i, c] - acc
                    befores[c] = lasts[c]
                    lasts[c] = now
                    if want_values:
                        val_ref[i, c] = now
            for c in range(conds):
                carry_ref[0, 0, c] = lasts[c]
                carry_ref[1, 0, c] = befores[c]
            return
        _init_carry(carry_ref, inc_ref)

        def step(i, unused):
            for k in range(width):
                for c in range(conds):
                    last = carry_ref[0, k, c]
                    before = carry_ref[1, k, c]
                    acc = _rows_times(nt_ref, (i, c), last) + _rows_times(ft_ref, (i, c), before)
                    if has_rhs:
                        now = rhs_ref[i, c] - acc
                    else:
                        now = -acc
                    carry_ref[1, k, c] = last
                    carry_ref[0, k, c] = now
                    if want_values:
                        val_ref[i, c] = now
            return unused

        lax.fori_loop(0, count, step, 0)

    out_shape = [jax.ShapeDtypeStruct(shape, jnp.float32)]
    if want_values:
        out_shape = [jax.ShapeDtypeStruct(rhs.shape, jnp.float32)] + out_shape
    args = ([rhs] if has_rhs else []) + [near_t, far_t] + ([incoming] if has_inc else [])
    return pl.pallas_call(
        kernel,
        out_shape=tuple(out_shape),
        in_specs=_vmem_specs(len(args)),
        out_specs=tuple(_vmem_specs(len(out_shape))),
    )(*args)


def lower_pallas(rhs, inverse, near, far, incoming, want_values):
    count, conds, nv = inverse.shape[0], inverse.shape[1], inverse.shape[2]
    has_inc = not isinstance(incoming, tuple)
    shape = incoming.shape if has_inc else incoming
    width = shape[1]
    has_rhs = rhs is not None

    def kernel(*refs):
        refs = list(refs)
        rhs_ref = refs.pop(0) if has_rhs else None
        d_ref, b_ref, a_ref = refs.pop(0), refs.pop(0), refs.pop(0)
        inc_ref = refs.pop(0) if has_inc else None
        outs = refs
        if want_values:
            val_ref, carry_ref = outs
        else:
            (carry_ref,) = outs
        if width == 1:
            pendings = [inc_ref[0, 0, c] for c in range(conds)]
            partials = [inc_ref[1, 0, c] for c in range(conds)]
            for i in range(count - 1, -1, -1):
                for c in range(conds):
                    now = _rows_times(d_ref, (i, c), rhs_ref[i, c] - pendings[c])
                    pendings[c] = partials[c] + _rows_times(b_ref, (i, c), now)
                    partials[c] = _rows_times(a_ref, (i, c), now)
                    if want_values:
                        val_ref[i, c] = now
            for c in range(conds):
                carry_ref[0, 0, c] = pendings[c]
                carry_ref[1, 0, c] = partials[c]
            return
        _init_carry(carry_ref, inc_ref)

        def step(t, unused):
            i = count - 1 - t
            for k in range(width):
                for c in range(conds):
                    pending = carry_ref[0, k, c]
                    partial_value = carry_ref[1, k, c]
                    if has_rhs:
                        r = rhs_ref[i, c] - pending
                    else:
                        r = -pending
                    now = _rows_times(d_ref, (i, c), r)
                    carry_ref[0, k, c] = partial_value + _rows_times(b_ref, (i, c), now)
                    carry_ref[1, k, c] = _rows_times(a_ref, (i, c), now)
                    if want_values:
                        val_ref[i, c] = now
            return unused

        lax.fori_loop(0, count, step, 0)

    out_shape = [jax.ShapeDtypeStruct(shape, jnp.float32)]
    if want_values:
        out_shape = [jax.ShapeDtypeStruct(rhs.shape, jnp.float32)] + out_shape
    args = ([rhs] if has_rhs else []) + [inverse, near, far] + ([incoming] if has_inc else [])
    return pl.pallas_call(
        kernel,
        out_shape=tuple(out_shape),
        in_specs=_vmem_specs(len(args)),
        out_specs=tuple(_vmem_specs(len(out_shape))),
    )(*args)


def upper_then_lower(rhs, near_t, far_t, incoming, inverse, near, far):
    count, conds = near_t.shape[0], near_t.shape[1]
    carry = jax.ShapeDtypeStruct((2, 1) + rhs.shape[1:], jnp.float32)

    def kernel(rhs_ref, nt_ref, ft_ref, inc_ref, d_ref, b_ref, a_ref, val_ref, carry_ref):
        for c in range(conds):
            last, before = inc_ref[0, 0, c], inc_ref[1, 0, c]
            for i in range(count):
                acc = _rows_times(nt_ref, (i, c), last) + _rows_times(ft_ref, (i, c), before)
                before, last = last, rhs_ref[i, c] - acc
                val_ref[i, c] = last
            pending = None
            partial_value = None
            for i in range(count - 1, -1, -1):
                r = val_ref[i, c] if pending is None else val_ref[i, c] - pending
                now = _rows_times(d_ref, (i, c), r)
                near_part = _rows_times(b_ref, (i, c), now)
                pending = near_part if partial_value is None else partial_value + near_part
                partial_value = _rows_times(a_ref, (i, c), now)
            carry_ref[0, 0, c] = pending
            carry_ref[1, 0, c] = partial_value

    return pl.pallas_call(
        kernel,
        out_shape=(jax.ShapeDtypeStruct(rhs.shape, jnp.float32), carry),
        in_specs=_vmem_specs(7),
        out_specs=tuple(_vmem_specs(2)),
    )(rhs, near_t, far_t, incoming, inverse, near, far)


def carry_through(vector, response):
    slots, width, conds, nv, lanes = response.shape
    split = response.reshape(slots, slots, nv, conds, nv, lanes)
    inputs = jnp.transpose(vector, (0, 2, 1, 3))[None, :, :, :, None, :]
    return jnp.sum(jnp.sum(split * inputs, axis=2), axis=1)


def shifted_operators(matrix, steps):
    count = lax.axis_size("gx")
    return [from_behind(matrix, "gx", steps * s) for s in range(1, count - 1)]


def gathered_carry(vector, operators, steps):
    count = lax.axis_size("gx")
    if count == 1:
        return jnp.zeros_like(vector)
    total = from_behind(vector, "gx", steps * (count - 1))
    for s in range(count - 2, 0, -1):
        total = carry_through(total, operators[s - 1]) + from_behind(
            vector, "gx", steps * s
        )
    return total


def on_device(
    psi_old,
    objective_grad,
    near_upper,
    far_upper,
    inverse_diag,
    near_lower,
    far_lower,
    y_inverse,
    z_inverse,
    sens_terms,
    wall_mask,
    cond_index,
    weight_table,
):
    keep = (1.0 - wall_mask.astype(jnp.float32))[:, None, None, :]
    carry_shape = psi_old.shape[1:]
    zeros = jnp.zeros((2, 1) + carry_shape, jnp.float32)
    units = (2, 2 * carry_shape[1]) + carry_shape
    near_t = jnp.swapaxes(near_upper, 2, 3)
    far_t = jnp.swapaxes(far_upper, 2, 3)
    (response,) = upper_pallas(None, near_t, far_t, units, False)
    matrix = response
    (response,) = lower_pallas(None, inverse_diag, near_lower, far_lower, units, False)
    reverse_matrix = response
    upper_products = shifted_operators(matrix, 1)
    lower_products = shifted_operators(reverse_matrix, -1)
    psi = psi_old
    for step in range(ITERS):
        stream_pad = extended(psi, (("gx", 0),), 1)
        span_pad = extended(psi, (("gy", 3),), NZ)
        beside_all = (
            stream_pad[2:] + stream_pad[:-2] + span_pad[..., 2 * NZ :] + span_pad[..., : -2 * NZ]
        )
        rhs = objective_grad + 0.5 * beside_all - 2.0 * psi
        grid = rhs.reshape(rhs.shape[0], rhs.shape[1], rhs.shape[2], rhs.shape[3] // NZ, NZ)
        zres = jnp.einsum(
            "icvjq,cvqk->icvjk", grid, z_inverse, precision=lax.Precision.HIGHEST
        ).reshape(rhs.shape)
        yres = jnp.sum(y_inverse * zres[..., :, None, :], axis=-3)
        (offset,) = upper_pallas(yres, near_t, far_t, zeros, False)
        entering = gathered_carry(offset[:, 0], upper_products, 1)
        upper, offset = upper_then_lower(
            yres, near_t, far_t, entering[:, None], inverse_diag, near_lower, far_lower
        )
        entering = gathered_carry(offset[:, 0], lower_products, -1)
        lower, _ = lower_pallas(upper, inverse_diag, near_lower, far_lower, entering[:, None], True)
        psi = (psi + 0.05 * lower) * keep
    onehot = (cond_index[:, None] == jnp.arange(weight_table.shape[0])[None, :]).astype(jnp.float32)
    weights = jnp.sum(onehot * weight_table[None, :], axis=1)
    local_sens = jnp.einsum(
        "icvl,icmvl->iml",
        psi * weights[None, :, None, None],
        sens_terms,
        precision=lax.Precision.HIGHEST,
    )
    if lax.axis_size("cond") == 2:
        mesh_sens = local_sens + lax.ppermute(local_sens, "cond", [(0, 1), (1, 0)])
    else:
        mesh_sens = lax.psum(local_sens, "cond")
    return (psi, mesh_sens)


def solution(mesh):
    placed = (
        P("gx", "cond", None, "gy"),
        P("gx", "cond", None, "gy"),
        P("gx", "cond", None, None, "gy"),
        P("gx", "cond", None, None, "gy"),
        P("gx", "cond", None, None, "gy"),
        P("gx", "cond", None, None, "gy"),
        P("gx", "cond", None, None, "gy"),
        P("gx", "cond", None, None, "gy"),
        P("cond", None, None, None),
        P("gx", "cond", None, None, "gy"),
        P("gx", "gy"),
        P("cond"),
        P(),
    )
    return jax.shard_map(
        on_device,
        mesh=mesh,
        in_specs=placed,
        out_specs=(P("gx", "cond", None, "gy"), P("gx", None, "gy")),
        check_vma=False,
    )
```

```python
import jax
import jax.numpy as jnp
from jax import lax
from jax.experimental import pallas as pl
from jax.experimental.pallas import tpu as pltpu
from jax.sharding import PartitionSpec as P

NZ = 32
ITERS = 2


def extended(value, sides, width):
    for axis, dim in sides:
        size, length = (lax.axis_size(axis), value.shape[dim])
        up = [(i, (i + 1) % size) for i in range(size - 1)]
        down = [(j, i) for i, j in up]
        last = lax.slice_in_dim(value, length - width, length, axis=dim)
        first = lax.slice_in_dim(value, 0, width, axis=dim)
        before = lax.ppermute(last, axis, up)
        after = lax.ppermute(first, axis, down)
        value = jnp.concatenate([before, value, after], axis=dim)
    return value


def from_behind(value, axis, steps):
    count = lax.axis_size(axis)
    first, last = (max(0, -steps), min(count, count - steps))
    return lax.ppermute(value, axis, [(source, source + steps) for source in range(first, last)])


def _vmem_specs(n):
    return [pl.BlockSpec(memory_space=pltpu.VMEM) for _ in range(n)]


def _rows_times(blocks_ref, index, vec):
    terms = [blocks_ref[index + (a,)] * vec[a : a + 1, :] for a in range(vec.shape[0])]
    while len(terms) > 1:
        paired = [terms[j] + terms[j + 1] for j in range(0, len(terms) - 1, 2)]
        if len(terms) % 2:
            paired.append(terms[-1])
        terms = paired
    return terms[0]


def _init_carry(carry_ref, inc_ref):
    if inc_ref is not None:
        carry_ref[...] = inc_ref[...]
        return
    slots, width, conds, nv, lanes = carry_ref.shape
    rows = lax.broadcasted_iota(jnp.int32, (nv, lanes), 0)
    for slot in range(slots):
        for k in range(width):
            unit = (rows == k - slot * nv).astype(jnp.float32)
            for c in range(conds):
                carry_ref[slot, k, c] = unit


def upper_pallas(rhs, near_t, far_t, incoming, want_values):
    count, conds, nv = near_t.shape[0], near_t.shape[1], near_t.shape[2]
    has_inc = not isinstance(incoming, tuple)
    shape = incoming.shape if has_inc else incoming
    width = shape[1]
    has_rhs = rhs is not None

    def kernel(*refs):
        refs = list(refs)
        rhs_ref = refs.pop(0) if has_rhs else None
        nt_ref, ft_ref = refs.pop(0), refs.pop(0)
        inc_ref = refs.pop(0) if has_inc else None
        outs = refs
        if want_values:
            val_ref, carry_ref = outs
        else:
            (carry_ref,) = outs
        if width == 1:
            lasts = [inc_ref[0, 0, c] for c in range(conds)]
            befores = [inc_ref[1, 0, c] for c in range(conds)]
            for i in range(count):
                for c in range(conds):
                    acc = _rows_times(nt_ref, (i, c), lasts[c]) + _rows_times(
                        ft_ref, (i, c), befores[c]
                    )
                    now = rhs_ref[i, c] - acc
                    befores[c] = lasts[c]
                    lasts[c] = now
                    if want_values:
                        val_ref[i, c] = now
            for c in range(conds):
                carry_ref[0, 0, c] = lasts[c]
                carry_ref[1, 0, c] = befores[c]
            return
        _init_carry(carry_ref, inc_ref)

        def step(i, unused):
            for k in range(width):
                for c in range(conds):
                    last = carry_ref[0, k, c]
                    before = carry_ref[1, k, c]
                    acc = _rows_times(nt_ref, (i, c), last) + _rows_times(ft_ref, (i, c), before)
                    if has_rhs:
                        now = rhs_ref[i, c] - acc
                    else:
                        now = -acc
                    carry_ref[1, k, c] = last
                    carry_ref[0, k, c] = now
                    if want_values:
                        val_ref[i, c] = now
            return unused

        lax.fori_loop(0, count, step, 0)

    out_shape = [jax.ShapeDtypeStruct(shape, jnp.float32)]
    if want_values:
        out_shape = [jax.ShapeDtypeStruct(rhs.shape, jnp.float32)] + out_shape
    args = ([rhs] if has_rhs else []) + [near_t, far_t] + ([incoming] if has_inc else [])
    return pl.pallas_call(
        kernel,
        out_shape=tuple(out_shape),
        in_specs=_vmem_specs(len(args)),
        out_specs=tuple(_vmem_specs(len(out_shape))),
    )(*args)


def lower_pallas(rhs, inverse, near, far, incoming, want_values):
    count, conds, nv = inverse.shape[0], inverse.shape[1], inverse.shape[2]
    has_inc = not isinstance(incoming, tuple)
    shape = incoming.shape if has_inc else incoming
    width = shape[1]
    has_rhs = rhs is not None

    def kernel(*refs):
        refs = list(refs)
        rhs_ref = refs.pop(0) if has_rhs else None
        d_ref, b_ref, a_ref = refs.pop(0), refs.pop(0), refs.pop(0)
        inc_ref = refs.pop(0) if has_inc else None
        outs = refs
        if want_values:
            val_ref, carry_ref = outs
        else:
            (carry_ref,) = outs
        if width == 1:
            pendings = [inc_ref[0, 0, c] for c in range(conds)]
            partials = [inc_ref[1, 0, c] for c in range(conds)]
            for i in range(count - 1, -1, -1):
                for c in range(conds):
                    now = _rows_times(d_ref, (i, c), rhs_ref[i, c] - pendings[c])
                    pendings[c] = partials[c] + _rows_times(b_ref, (i, c), now)
                    partials[c] = _rows_times(a_ref, (i, c), now)
                    if want_values:
                        val_ref[i, c] = now
            for c in range(conds):
                carry_ref[0, 0, c] = pendings[c]
                carry_ref[1, 0, c] = partials[c]
            return
        _init_carry(carry_ref, inc_ref)

        def step(t, unused):
            i = count - 1 - t
            for k in range(width):
                for c in range(conds):
                    pending = carry_ref[0, k, c]
                    partial_value = carry_ref[1, k, c]
                    if has_rhs:
                        r = rhs_ref[i, c] - pending
                    else:
                        r = -pending
                    now = _rows_times(d_ref, (i, c), r)
                    carry_ref[0, k, c] = partial_value + _rows_times(b_ref, (i, c), now)
                    carry_ref[1, k, c] = _rows_times(a_ref, (i, c), now)
                    if want_values:
                        val_ref[i, c] = now
            return unused

        lax.fori_loop(0, count, step, 0)

    out_shape = [jax.ShapeDtypeStruct(shape, jnp.float32)]
    if want_values:
        out_shape = [jax.ShapeDtypeStruct(rhs.shape, jnp.float32)] + out_shape
    args = ([rhs] if has_rhs else []) + [inverse, near, far] + ([incoming] if has_inc else [])
    return pl.pallas_call(
        kernel,
        out_shape=tuple(out_shape),
        in_specs=_vmem_specs(len(args)),
        out_specs=tuple(_vmem_specs(len(out_shape))),
    )(*args)


def upper_then_lower(rhs, near_t, far_t, incoming, inverse, near, far):
    count, conds = near_t.shape[0], near_t.shape[1]
    carry = jax.ShapeDtypeStruct((2, 1) + rhs.shape[1:], jnp.float32)

    def kernel(rhs_ref, nt_ref, ft_ref, inc_ref, d_ref, b_ref, a_ref, val_ref, carry_ref):
        for c in range(conds):
            last, before = inc_ref[0, 0, c], inc_ref[1, 0, c]
            for i in range(count):
                acc = _rows_times(nt_ref, (i, c), last) + _rows_times(ft_ref, (i, c), before)
                before, last = last, rhs_ref[i, c] - acc
                val_ref[i, c] = last
            pending = None
            partial_value = None
            for i in range(count - 1, -1, -1):
                r = val_ref[i, c] if pending is None else val_ref[i, c] - pending
                now = _rows_times(d_ref, (i, c), r)
                near_part = _rows_times(b_ref, (i, c), now)
                pending = near_part if partial_value is None else partial_value + near_part
                partial_value = _rows_times(a_ref, (i, c), now)
            carry_ref[0, 0, c] = pending
            carry_ref[1, 0, c] = partial_value

    return pl.pallas_call(
        kernel,
        out_shape=(jax.ShapeDtypeStruct(rhs.shape, jnp.float32), carry),
        in_specs=_vmem_specs(7),
        out_specs=tuple(_vmem_specs(2)),
    )(rhs, near_t, far_t, incoming, inverse, near, far)


def carry_through(vector, response):
    slots, width, conds, nv, lanes = response.shape
    split = response.reshape(slots, slots, nv, conds, nv, lanes)
    inputs = jnp.transpose(vector, (0, 2, 1, 3))[None, :, :, :, None, :]
    return jnp.sum(jnp.sum(split * inputs, axis=2), axis=1)


def shifted_operators(matrix, steps):
    count = lax.axis_size("gx")
    return [from_behind(matrix, "gx", steps * s) for s in range(1, count - 1)]


def gathered_carry(vector, operators, steps):
    count = lax.axis_size("gx")
    if count == 1:
        return jnp.zeros_like(vector)
    total = from_behind(vector, "gx", steps * (count - 1))
    for s in range(count - 2, 0, -1):
        total = carry_through(total, operators[s - 1]) + from_behind(
            vector, "gx", steps * s
        )
    return total


def relayed_carry(vector, behind, steps):
    count = lax.axis_size("gx")
    if count == 1:
        return jnp.zeros_like(vector)
    nearest = from_behind(vector, "gx", steps)
    if count == 2:
        return nearest
    total = nearest + carry_through(from_behind(vector, "gx", 2 * steps), behind)
    for _ in range(count - 3):
        total = nearest + carry_through(from_behind(total, "gx", steps), behind)
    return total


def on_device(
    psi_old,
    objective_grad,
    near_upper,
    far_upper,
    inverse_diag,
    near_lower,
    far_lower,
    y_inverse,
    z_inverse,
    sens_terms,
    wall_mask,
    cond_index,
    weight_table,
):
    keep = (1.0 - wall_mask.astype(jnp.float32))[:, None, None, :]
    carry_shape = psi_old.shape[1:]
    zeros = jnp.zeros((2, 1) + carry_shape, jnp.float32)
    units = (2, 2 * carry_shape[1]) + carry_shape
    near_t = jnp.swapaxes(near_upper, 2, 3)
    far_t = jnp.swapaxes(far_upper, 2, 3)
    (response,) = upper_pallas(None, near_t, far_t, units, False)
    matrix = response
    (response,) = lower_pallas(None, inverse_diag, near_lower, far_lower, units, False)
    reverse_matrix = response
    upper_products = shifted_operators(matrix, 1)
    lower_behind = from_behind(reverse_matrix, "gx", -1)
    psi = psi_old
    for step in range(ITERS):
        stream_pad = extended(psi, (("gx", 0),), 1)
        span_pad = extended(psi, (("gy", 3),), NZ)
        beside_all = (
            stream_pad[2:] + stream_pad[:-2] + span_pad[..., 2 * NZ :] + span_pad[..., : -2 * NZ]
        )
        rhs = objective_grad + 0.5 * beside_all - 2.0 * psi
        grid = rhs.reshape(rhs.shape[0], rhs.shape[1], rhs.shape[2], rhs.shape[3] // NZ, NZ)
        zres = jnp.einsum(
            "icvjq,cvqk->icvjk", grid, z_inverse, precision=lax.Precision.HIGHEST
        ).reshape(rhs.shape)
        yres = jnp.sum(y_inverse * zres[..., :, None, :], axis=-3)
        (offset,) = upper_pallas(yres, near_t, far_t, zeros, False)
        entering = gathered_carry(offset[:, 0], upper_products, 1)
        upper, offset = upper_then_lower(
            yres, near_t, far_t, entering[:, None], inverse_diag, near_lower, far_lower
        )
        entering = relayed_carry(offset[:, 0], lower_behind, -1)
        lower, _ = lower_pallas(upper, inverse_diag, near_lower, far_lower, entering[:, None], True)
        psi = (psi + 0.05 * lower) * keep
    onehot = (cond_index[:, None] == jnp.arange(weight_table.shape[0])[None, :]).astype(jnp.float32)
    weights = jnp.sum(onehot * weight_table[None, :], axis=1)
    local_sens = jnp.einsum(
        "icvl,icmvl->iml",
        psi * weights[None, :, None, None],
        sens_terms,
        precision=lax.Precision.HIGHEST,
    )
    if lax.axis_size("cond") == 2:
        mesh_sens = local_sens + lax.ppermute(local_sens, "cond", [(0, 1), (1, 0)])
    else:
        mesh_sens = lax.psum(local_sens, "cond")
    return (psi, mesh_sens)


def solution(mesh):
    placed = (
        P("gx", "cond", None, "gy"),
        P("gx", "cond", None, "gy"),
        P("gx", "cond", None, None, "gy"),
        P("gx", "cond", None, None, "gy"),
        P("gx", "cond", None, None, "gy"),
        P("gx", "cond", None, None, "gy"),
        P("gx", "cond", None, None, "gy"),
        P("gx", "cond", None, None, "gy"),
        P("cond", None, None, None),
        P("gx", "cond", None, None, "gy"),
        P("gx", "gy"),
        P("cond"),
        P(),
    )
    return jax.shard_map(
        on_device,
        mesh=mesh,
        in_specs=placed,
        out_specs=(P("gx", "cond", None, "gy"), P("gx", None, "gy")),
        check_vma=False,
    )
```

```python
import jax
import jax.numpy as jnp
from jax import lax
from jax.experimental import pallas as pl
from jax.experimental.pallas import tpu as pltpu
from jax.sharding import PartitionSpec as P

NZ = 32
ITERS = 2


def extended(value, sides, width):
    for axis, dim in sides:
        size, length = (lax.axis_size(axis), value.shape[dim])
        up = [(i, (i + 1) % size) for i in range(size - 1)]
        down = [(j, i) for i, j in up]
        last = lax.slice_in_dim(value, length - width, length, axis=dim)
        first = lax.slice_in_dim(value, 0, width, axis=dim)
        before = lax.ppermute(last, axis, up)
        after = lax.ppermute(first, axis, down)
        value = jnp.concatenate([before, value, after], axis=dim)
    return value


def from_behind(value, axis, steps):
    count = lax.axis_size(axis)
    first, last = (max(0, -steps), min(count, count - steps))
    return lax.ppermute(value, axis, [(source, source + steps) for source in range(first, last)])


def _vmem_specs(n):
    return [pl.BlockSpec(memory_space=pltpu.VMEM) for _ in range(n)]


def _rows_times(blocks_ref, index, vec):
    terms = [blocks_ref[index + (a,)] * vec[a : a + 1, :] for a in range(vec.shape[0])]
    while len(terms) > 1:
        paired = [terms[j] + terms[j + 1] for j in range(0, len(terms) - 1, 2)]
        if len(terms) % 2:
            paired.append(terms[-1])
        terms = paired
    return terms[0]


def _init_carry(carry_ref, inc_ref):
    if inc_ref is not None:
        carry_ref[...] = inc_ref[...]
        return
    slots, width, conds, nv, lanes = carry_ref.shape
    rows = lax.broadcasted_iota(jnp.int32, (nv, lanes), 0)
    for slot in range(slots):
        for k in range(width):
            unit = (rows == k - slot * nv).astype(jnp.float32)
            for c in range(conds):
                carry_ref[slot, k, c] = unit


def upper_pallas(rhs, near_t, far_t, incoming, want_values):
    count, conds, nv = near_t.shape[0], near_t.shape[1], near_t.shape[2]
    has_inc = not isinstance(incoming, tuple)
    shape = incoming.shape if has_inc else incoming
    width = shape[1]
    has_rhs = rhs is not None

    def kernel(*refs):
        refs = list(refs)
        rhs_ref = refs.pop(0) if has_rhs else None
        nt_ref, ft_ref = refs.pop(0), refs.pop(0)
        inc_ref = refs.pop(0) if has_inc else None
        outs = refs
        if want_values:
            val_ref, carry_ref = outs
        else:
            (carry_ref,) = outs
        if width == 1:
            lasts = [inc_ref[0, 0, c] for c in range(conds)]
            befores = [inc_ref[1, 0, c] for c in range(conds)]
            for i in range(count):
                for c in range(conds):
                    acc = _rows_times(nt_ref, (i, c), lasts[c]) + _rows_times(
                        ft_ref, (i, c), befores[c]
                    )
                    now = rhs_ref[i, c] - acc
                    befores[c] = lasts[c]
                    lasts[c] = now
                    if want_values:
                        val_ref[i, c] = now
            for c in range(conds):
                carry_ref[0, 0, c] = lasts[c]
                carry_ref[1, 0, c] = befores[c]
            return
        _init_carry(carry_ref, inc_ref)

        def step(i, unused):
            for k in range(width):
                for c in range(conds):
                    last = carry_ref[0, k, c]
                    before = carry_ref[1, k, c]
                    acc = _rows_times(nt_ref, (i, c), last) + _rows_times(ft_ref, (i, c), before)
                    if has_rhs:
                        now = rhs_ref[i, c] - acc
                    else:
                        now = -acc
                    carry_ref[1, k, c] = last
                    carry_ref[0, k, c] = now
                    if want_values:
                        val_ref[i, c] = now
            return unused

        lax.fori_loop(0, count, step, 0)

    out_shape = [jax.ShapeDtypeStruct(shape, jnp.float32)]
    if want_values:
        out_shape = [jax.ShapeDtypeStruct(rhs.shape, jnp.float32)] + out_shape
    args = ([rhs] if has_rhs else []) + [near_t, far_t] + ([incoming] if has_inc else [])
    return pl.pallas_call(
        kernel,
        out_shape=tuple(out_shape),
        in_specs=_vmem_specs(len(args)),
        out_specs=tuple(_vmem_specs(len(out_shape))),
    )(*args)


def lower_pallas(rhs, inverse, near, far, incoming, want_values):
    count, conds, nv = inverse.shape[0], inverse.shape[1], inverse.shape[2]
    has_inc = not isinstance(incoming, tuple)
    shape = incoming.shape if has_inc else incoming
    width = shape[1]
    has_rhs = rhs is not None

    def kernel(*refs):
        refs = list(refs)
        rhs_ref = refs.pop(0) if has_rhs else None
        d_ref, b_ref, a_ref = refs.pop(0), refs.pop(0), refs.pop(0)
        inc_ref = refs.pop(0) if has_inc else None
        outs = refs
        if want_values:
            val_ref, carry_ref = outs
        else:
            (carry_ref,) = outs
        if width == 1:
            pendings = [inc_ref[0, 0, c] for c in range(conds)]
            partials = [inc_ref[1, 0, c] for c in range(conds)]
            for i in range(count - 1, -1, -1):
                for c in range(conds):
                    now = _rows_times(d_ref, (i, c), rhs_ref[i, c] - pendings[c])
                    pendings[c] = partials[c] + _rows_times(b_ref, (i, c), now)
                    partials[c] = _rows_times(a_ref, (i, c), now)
                    if want_values:
                        val_ref[i, c] = now
            for c in range(conds):
                carry_ref[0, 0, c] = pendings[c]
                carry_ref[1, 0, c] = partials[c]
            return
        _init_carry(carry_ref, inc_ref)

        def step(t, unused):
            i = count - 1 - t
            for k in range(width):
                for c in range(conds):
                    pending = carry_ref[0, k, c]
                    partial_value = carry_ref[1, k, c]
                    if has_rhs:
                        r = rhs_ref[i, c] - pending
                    else:
                        r = -pending
                    now = _rows_times(d_ref, (i, c), r)
                    carry_ref[0, k, c] = partial_value + _rows_times(b_ref, (i, c), now)
                    carry_ref[1, k, c] = _rows_times(a_ref, (i, c), now)
                    if want_values:
                        val_ref[i, c] = now
            return unused

        lax.fori_loop(0, count, step, 0)

    out_shape = [jax.ShapeDtypeStruct(shape, jnp.float32)]
    if want_values:
        out_shape = [jax.ShapeDtypeStruct(rhs.shape, jnp.float32)] + out_shape
    args = ([rhs] if has_rhs else []) + [inverse, near, far] + ([incoming] if has_inc else [])
    return pl.pallas_call(
        kernel,
        out_shape=tuple(out_shape),
        in_specs=_vmem_specs(len(args)),
        out_specs=tuple(_vmem_specs(len(out_shape))),
    )(*args)


def upper_then_lower(rhs, near_t, far_t, incoming, inverse, near, far):
    count, conds = near_t.shape[0], near_t.shape[1]
    carry = jax.ShapeDtypeStruct((2, 1) + rhs.shape[1:], jnp.float32)

    def kernel(rhs_ref, nt_ref, ft_ref, inc_ref, d_ref, b_ref, a_ref, val_ref, carry_ref):
        for c in range(conds):
            last, before = inc_ref[0, 0, c], inc_ref[1, 0, c]
            for i in range(count):
                acc = _rows_times(nt_ref, (i, c), last) + _rows_times(ft_ref, (i, c), before)
                before, last = last, rhs_ref[i, c] - acc
                val_ref[i, c] = last
            pending = None
            partial_value = None
            for i in range(count - 1, -1, -1):
                r = val_ref[i, c] if pending is None else val_ref[i, c] - pending
                now = _rows_times(d_ref, (i, c), r)
                near_part = _rows_times(b_ref, (i, c), now)
                pending = near_part if partial_value is None else partial_value + near_part
                partial_value = _rows_times(a_ref, (i, c), now)
            carry_ref[0, 0, c] = pending
            carry_ref[1, 0, c] = partial_value

    return pl.pallas_call(
        kernel,
        out_shape=(jax.ShapeDtypeStruct(rhs.shape, jnp.float32), carry),
        in_specs=_vmem_specs(7),
        out_specs=tuple(_vmem_specs(2)),
    )(rhs, near_t, far_t, incoming, inverse, near, far)


def carry_through(vector, response):
    slots, width, conds, nv, lanes = response.shape
    split = response.reshape(slots, slots, nv, conds, nv, lanes)
    inputs = jnp.transpose(vector, (0, 2, 1, 3))[None, :, :, :, None, :]
    return jnp.sum(jnp.sum(split * inputs, axis=2), axis=1)


def shifted_operators(matrix, steps):
    count = lax.axis_size("gx")
    return [from_behind(matrix, "gx", steps * s) for s in range(1, count - 1)]


def gathered_carry(vector, operators, steps):
    count = lax.axis_size("gx")
    if count == 1:
        return jnp.zeros_like(vector)
    total = from_behind(vector, "gx", steps * (count - 1))
    for s in range(count - 2, 0, -1):
        total = carry_through(total, operators[s - 1]) + from_behind(
            vector, "gx", steps * s
        )
    return total


def relayed_carry(vector, behind, steps):
    count = lax.axis_size("gx")
    if count == 1:
        return jnp.zeros_like(vector)
    nearest = from_behind(vector, "gx", steps)
    if count == 2:
        return nearest
    total = nearest + carry_through(from_behind(vector, "gx", 2 * steps), behind)
    for _ in range(count - 3):
        total = nearest + carry_through(from_behind(total, "gx", steps), behind)
    return total


def on_device(
    psi_old,
    objective_grad,
    near_upper,
    far_upper,
    inverse_diag,
    near_lower,
    far_lower,
    y_inverse,
    z_inverse,
    sens_terms,
    wall_mask,
    cond_index,
    weight_table,
):
    keep = (1.0 - wall_mask.astype(jnp.float32))[:, None, None, :]
    carry_shape = psi_old.shape[1:]
    zeros = jnp.zeros((2, 1) + carry_shape, jnp.float32)
    units = (2, 2 * carry_shape[1]) + carry_shape
    near_t = jnp.swapaxes(near_upper, 2, 3)
    far_t = jnp.swapaxes(far_upper, 2, 3)
    (response,) = upper_pallas(None, near_t, far_t, units, False)
    matrix = response
    (response,) = lower_pallas(None, inverse_diag, near_lower, far_lower, units, False)
    reverse_matrix = response
    upper_products = shifted_operators(matrix, 1)
    lower_behind = from_behind(reverse_matrix, "gx", -1)
    psi = psi_old
    for step in range(ITERS):
        stream_pad = extended(psi, (("gx", 0),), 1)
        span_pad = extended(psi, (("gy", 3),), NZ)
        beside_all = (
            stream_pad[2:] + stream_pad[:-2] + span_pad[..., 2 * NZ :] + span_pad[..., : -2 * NZ]
        )
        rhs = objective_grad + 0.5 * beside_all - 2.0 * psi
        grid = rhs.reshape(rhs.shape[0], rhs.shape[1], rhs.shape[2], rhs.shape[3] // NZ, NZ)
        zres = jnp.einsum(
            "icvjq,cvqk->icvjk", grid, z_inverse, precision=lax.Precision.HIGHEST
        ).reshape(rhs.shape)
        yres = jnp.sum(y_inverse * zres[..., :, None, :], axis=-3)
        (offset,) = upper_pallas(yres, near_t, far_t, zeros, False)
        entering = gathered_carry(offset[:, 0], upper_products, 1)
        upper, offset = upper_then_lower(
            yres, near_t, far_t, entering[:, None], inverse_diag, near_lower, far_lower
        )
        if step == 0:
            entering = jnp.zeros_like(offset[:, 0])
            for _ in range(lax.axis_size("gx") - 1):
                entering = from_behind(
                    carry_through(entering, reverse_matrix) + offset[:, 0], "gx", -1
                )
        else:
            entering = relayed_carry(offset[:, 0], lower_behind, -1)
        lower, _ = lower_pallas(upper, inverse_diag, near_lower, far_lower, entering[:, None], True)
        psi = (psi + 0.05 * lower) * keep
    onehot = (cond_index[:, None] == jnp.arange(weight_table.shape[0])[None, :]).astype(jnp.float32)
    weights = jnp.sum(onehot * weight_table[None, :], axis=1)
    local_sens = jnp.einsum(
        "icvl,icmvl->iml",
        psi * weights[None, :, None, None],
        sens_terms,
        precision=lax.Precision.HIGHEST,
    )
    if lax.axis_size("cond") == 2:
        mesh_sens = local_sens + lax.ppermute(local_sens, "cond", [(0, 1), (1, 0)])
    else:
        mesh_sens = lax.psum(local_sens, "cond")
    return (psi, mesh_sens)


def solution(mesh):
    placed = (
        P("gx", "cond", None, "gy"),
        P("gx", "cond", None, "gy"),
        P("gx", "cond", None, None, "gy"),
        P("gx", "cond", None, None, "gy"),
        P("gx", "cond", None, None, "gy"),
        P("gx", "cond", None, None, "gy"),
        P("gx", "cond", None, None, "gy"),
        P("gx", "cond", None, None, "gy"),
        P("cond", None, None, None),
        P("gx", "cond", None, None, "gy"),
        P("gx", "gy"),
        P("cond"),
        P(),
    )
    return jax.shard_map(
        on_device,
        mesh=mesh,
        in_specs=placed,
        out_specs=(P("gx", "cond", None, "gy"), P("gx", None, "gy")),
        check_vma=False,
    )
```

```python
import jax
import jax.numpy as jnp
from jax import lax
from jax.experimental import pallas as pl
from jax.experimental.pallas import tpu as pltpu
from jax.sharding import PartitionSpec as P

NZ = 32
ITERS = 2


def extended(value, sides, width):
    for axis, dim in sides:
        size, length = (lax.axis_size(axis), value.shape[dim])
        up = [(i, (i + 1) % size) for i in range(size - 1)]
        down = [(j, i) for i, j in up]
        last = lax.slice_in_dim(value, length - width, length, axis=dim)
        first = lax.slice_in_dim(value, 0, width, axis=dim)
        before = lax.ppermute(last, axis, up)
        after = lax.ppermute(first, axis, down)
        value = jnp.concatenate([before, value, after], axis=dim)
    return value


def from_behind(value, axis, steps):
    count = lax.axis_size(axis)
    first, last = (max(0, -steps), min(count, count - steps))
    return lax.ppermute(value, axis, [(source, source + steps) for source in range(first, last)])


def _vmem_specs(n):
    return [pl.BlockSpec(memory_space=pltpu.VMEM) for _ in range(n)]


def _rows_times(blocks_ref, index, vec):
    terms = [blocks_ref[index + (a,)] * vec[a : a + 1, :] for a in range(vec.shape[0])]
    while len(terms) > 1:
        paired = [terms[j] + terms[j + 1] for j in range(0, len(terms) - 1, 2)]
        if len(terms) % 2:
            paired.append(terms[-1])
        terms = paired
    return terms[0]


def _init_carry(carry_ref, inc_ref):
    if inc_ref is not None:
        carry_ref[...] = inc_ref[...]
        return
    slots, width, conds, nv, lanes = carry_ref.shape
    rows = lax.broadcasted_iota(jnp.int32, (nv, lanes), 0)
    for slot in range(slots):
        for k in range(width):
            unit = (rows == k - slot * nv).astype(jnp.float32)
            for c in range(conds):
                carry_ref[slot, k, c] = unit


def upper_pallas(rhs, near_t, far_t, incoming, want_values):
    count, conds, nv = near_t.shape[0], near_t.shape[1], near_t.shape[2]
    has_inc = not isinstance(incoming, tuple)
    shape = incoming.shape if has_inc else incoming
    width = shape[1]
    has_rhs = rhs is not None

    def kernel(*refs):
        refs = list(refs)
        rhs_ref = refs.pop(0) if has_rhs else None
        nt_ref, ft_ref = refs.pop(0), refs.pop(0)
        inc_ref = refs.pop(0) if has_inc else None
        outs = refs
        if want_values:
            val_ref, carry_ref = outs
        else:
            (carry_ref,) = outs
        if width == 1:
            lasts = [inc_ref[0, 0, c] for c in range(conds)]
            befores = [inc_ref[1, 0, c] for c in range(conds)]
            for i in range(count):
                for c in range(conds):
                    acc = _rows_times(nt_ref, (i, c), lasts[c]) + _rows_times(
                        ft_ref, (i, c), befores[c]
                    )
                    now = rhs_ref[i, c] - acc
                    befores[c] = lasts[c]
                    lasts[c] = now
                    if want_values:
                        val_ref[i, c] = now
            for c in range(conds):
                carry_ref[0, 0, c] = lasts[c]
                carry_ref[1, 0, c] = befores[c]
            return
        _init_carry(carry_ref, inc_ref)

        def step(i, unused):
            for k in range(width):
                for c in range(conds):
                    last = carry_ref[0, k, c]
                    before = carry_ref[1, k, c]
                    acc = _rows_times(nt_ref, (i, c), last) + _rows_times(ft_ref, (i, c), before)
                    if has_rhs:
                        now = rhs_ref[i, c] - acc
                    else:
                        now = -acc
                    carry_ref[1, k, c] = last
                    carry_ref[0, k, c] = now
                    if want_values:
                        val_ref[i, c] = now
            return unused

        lax.fori_loop(0, count, step, 0)

    out_shape = [jax.ShapeDtypeStruct(shape, jnp.float32)]
    if want_values:
        out_shape = [jax.ShapeDtypeStruct(rhs.shape, jnp.float32)] + out_shape
    args = ([rhs] if has_rhs else []) + [near_t, far_t] + ([incoming] if has_inc else [])
    return pl.pallas_call(
        kernel,
        out_shape=tuple(out_shape),
        in_specs=_vmem_specs(len(args)),
        out_specs=tuple(_vmem_specs(len(out_shape))),
    )(*args)


def lower_pallas(rhs, inverse, near, far, incoming, want_values):
    count, conds, nv = inverse.shape[0], inverse.shape[1], inverse.shape[2]
    has_inc = not isinstance(incoming, tuple)
    shape = incoming.shape if has_inc else incoming
    width = shape[1]
    has_rhs = rhs is not None

    def kernel(*refs):
        refs = list(refs)
        rhs_ref = refs.pop(0) if has_rhs else None
        d_ref, b_ref, a_ref = refs.pop(0), refs.pop(0), refs.pop(0)
        inc_ref = refs.pop(0) if has_inc else None
        outs = refs
        if want_values:
            val_ref, carry_ref = outs
        else:
            (carry_ref,) = outs
        if width == 1:
            pendings = [inc_ref[0, 0, c] for c in range(conds)]
            partials = [inc_ref[1, 0, c] for c in range(conds)]
            for i in range(count - 1, -1, -1):
                for c in range(conds):
                    now = _rows_times(d_ref, (i, c), rhs_ref[i, c] - pendings[c])
                    pendings[c] = partials[c] + _rows_times(b_ref, (i, c), now)
                    partials[c] = _rows_times(a_ref, (i, c), now)
                    if want_values:
                        val_ref[i, c] = now
            for c in range(conds):
                carry_ref[0, 0, c] = pendings[c]
                carry_ref[1, 0, c] = partials[c]
            return
        _init_carry(carry_ref, inc_ref)

        def step(t, unused):
            i = count - 1 - t
            for k in range(width):
                for c in range(conds):
                    pending = carry_ref[0, k, c]
                    partial_value = carry_ref[1, k, c]
                    if has_rhs:
                        r = rhs_ref[i, c] - pending
                    else:
                        r = -pending
                    now = _rows_times(d_ref, (i, c), r)
                    carry_ref[0, k, c] = partial_value + _rows_times(b_ref, (i, c), now)
                    carry_ref[1, k, c] = _rows_times(a_ref, (i, c), now)
                    if want_values:
                        val_ref[i, c] = now
            return unused

        lax.fori_loop(0, count, step, 0)

    out_shape = [jax.ShapeDtypeStruct(shape, jnp.float32)]
    if want_values:
        out_shape = [jax.ShapeDtypeStruct(rhs.shape, jnp.float32)] + out_shape
    args = ([rhs] if has_rhs else []) + [inverse, near, far] + ([incoming] if has_inc else [])
    return pl.pallas_call(
        kernel,
        out_shape=tuple(out_shape),
        in_specs=_vmem_specs(len(args)),
        out_specs=tuple(_vmem_specs(len(out_shape))),
    )(*args)


def upper_then_lower(rhs, near_t, far_t, incoming, inverse, near, far):
    count, conds = near_t.shape[0], near_t.shape[1]
    carry = jax.ShapeDtypeStruct((2, 1) + rhs.shape[1:], jnp.float32)

    def kernel(rhs_ref, nt_ref, ft_ref, inc_ref, d_ref, b_ref, a_ref, val_ref, carry_ref):
        for c in range(conds):
            last, before = inc_ref[0, 0, c], inc_ref[1, 0, c]
            for i in range(count):
                acc = _rows_times(nt_ref, (i, c), last) + _rows_times(ft_ref, (i, c), before)
                before, last = last, rhs_ref[i, c] - acc
                val_ref[i, c] = last
            pending = None
            partial_value = None
            for i in range(count - 1, -1, -1):
                r = val_ref[i, c] if pending is None else val_ref[i, c] - pending
                now = _rows_times(d_ref, (i, c), r)
                near_part = _rows_times(b_ref, (i, c), now)
                pending = near_part if partial_value is None else partial_value + near_part
                partial_value = _rows_times(a_ref, (i, c), now)
            carry_ref[0, 0, c] = pending
            carry_ref[1, 0, c] = partial_value

    return pl.pallas_call(
        kernel,
        out_shape=(jax.ShapeDtypeStruct(rhs.shape, jnp.float32), carry),
        in_specs=_vmem_specs(7),
        out_specs=tuple(_vmem_specs(2)),
    )(rhs, near_t, far_t, incoming, inverse, near, far)


def carry_through(vector, response):
    slots, width, conds, nv, lanes = response.shape
    split = response.reshape(slots, slots, nv, conds, nv, lanes)
    inputs = jnp.transpose(vector, (0, 2, 1, 3))[None, :, :, :, None, :]
    return jnp.sum(jnp.sum(split * inputs, axis=2), axis=1)


def shifted_operators(matrix, steps):
    count = lax.axis_size("gx")
    return [from_behind(matrix, "gx", steps * s) for s in range(1, count - 1)]


def gathered_carry(vector, operators, steps):
    count = lax.axis_size("gx")
    if count == 1:
        return jnp.zeros_like(vector)
    total = from_behind(vector, "gx", steps * (count - 1))
    for s in range(count - 2, 0, -1):
        total = carry_through(total, operators[s - 1]) + from_behind(
            vector, "gx", steps * s
        )
    return total


def relayed_carry(vector, behind, steps):
    count = lax.axis_size("gx")
    if count == 1:
        return jnp.zeros_like(vector)
    nearest = from_behind(vector, "gx", steps)
    if count == 2:
        return nearest
    total = nearest + carry_through(from_behind(vector, "gx", 2 * steps), behind)
    for _ in range(count - 3):
        total = nearest + carry_through(from_behind(total, "gx", steps), behind)
    return total


def on_device(
    psi_old,
    objective_grad,
    near_upper,
    far_upper,
    inverse_diag,
    near_lower,
    far_lower,
    y_inverse,
    z_inverse,
    sens_terms,
    wall_mask,
    cond_index,
    weight_table,
):
    keep = (1.0 - wall_mask.astype(jnp.float32))[:, None, None, :]
    carry_shape = psi_old.shape[1:]
    zeros = jnp.zeros((2, 1) + carry_shape, jnp.float32)
    units = (2, 2 * carry_shape[1]) + carry_shape
    near_t = jnp.swapaxes(near_upper, 2, 3)
    far_t = jnp.swapaxes(far_upper, 2, 3)
    (response,) = upper_pallas(None, near_t, far_t, units, False)
    matrix = response
    (response,) = lower_pallas(None, inverse_diag, near_lower, far_lower, units, False)
    reverse_matrix = response
    upper_products = shifted_operators(matrix, 1)
    lower_behind = from_behind(reverse_matrix, "gx", -1)
    psi, _, _ = lax.optimization_barrier((psi_old, matrix, reverse_matrix))
    for step in range(ITERS):
        stream_pad = extended(psi, (("gx", 0),), 1)
        span_pad = extended(psi, (("gy", 3),), NZ)
        beside_all = (
            stream_pad[2:] + stream_pad[:-2] + span_pad[..., 2 * NZ :] + span_pad[..., : -2 * NZ]
        )
        rhs = objective_grad + 0.5 * beside_all - 2.0 * psi
        grid = rhs.reshape(rhs.shape[0], rhs.shape[1], rhs.shape[2], rhs.shape[3] // NZ, NZ)
        zres = jnp.einsum(
            "icvjq,cvqk->icvjk", grid, z_inverse, precision=lax.Precision.HIGHEST
        ).reshape(rhs.shape)
        yres = jnp.sum(y_inverse * zres[..., :, None, :], axis=-3)
        (offset,) = upper_pallas(yres, near_t, far_t, zeros, False)
        entering = gathered_carry(offset[:, 0], upper_products, 1)
        upper, offset = upper_then_lower(
            yres, near_t, far_t, entering[:, None], inverse_diag, near_lower, far_lower
        )
        entering = relayed_carry(offset[:, 0], lower_behind, -1)
        lower, _ = lower_pallas(upper, inverse_diag, near_lower, far_lower, entering[:, None], True)
        psi = (psi + 0.05 * lower) * keep
    onehot = (cond_index[:, None] == jnp.arange(weight_table.shape[0])[None, :]).astype(jnp.float32)
    weights = jnp.sum(onehot * weight_table[None, :], axis=1)
    local_sens = jnp.einsum(
        "icvl,icmvl->iml",
        psi * weights[None, :, None, None],
        sens_terms,
        precision=lax.Precision.HIGHEST,
    )
    if lax.axis_size("cond") == 2:
        mesh_sens = local_sens + lax.ppermute(local_sens, "cond", [(0, 1), (1, 0)])
    else:
        mesh_sens = lax.psum(local_sens, "cond")
    return (psi, mesh_sens)


def solution(mesh):
    placed = (
        P("gx", "cond", None, "gy"),
        P("gx", "cond", None, "gy"),
        P("gx", "cond", None, None, "gy"),
        P("gx", "cond", None, None, "gy"),
        P("gx", "cond", None, None, "gy"),
        P("gx", "cond", None, None, "gy"),
        P("gx", "cond", None, None, "gy"),
        P("gx", "cond", None, None, "gy"),
        P("cond", None, None, None),
        P("gx", "cond", None, None, "gy"),
        P("gx", "gy"),
        P("cond"),
        P(),
    )
    return jax.shard_map(
        on_device,
        mesh=mesh,
        in_specs=placed,
        out_specs=(P("gx", "cond", None, "gy"), P("gx", None, "gy")),
        check_vma=False,
    )
```

```python
import jax
import jax.numpy as jnp
from jax import lax
from jax.experimental import pallas as pl
from jax.experimental.pallas import tpu as pltpu
from jax.sharding import PartitionSpec as P

NZ = 32
ITERS = 2


def extended(value, sides, width):
    for axis, dim in sides:
        size, length = (lax.axis_size(axis), value.shape[dim])
        up = [(i, (i + 1) % size) for i in range(size - 1)]
        down = [(j, i) for i, j in up]
        last = lax.slice_in_dim(value, length - width, length, axis=dim)
        first = lax.slice_in_dim(value, 0, width, axis=dim)
        before = lax.ppermute(last, axis, up)
        after = lax.ppermute(first, axis, down)
        value = jnp.concatenate([before, value, after], axis=dim)
    return value


def from_behind(value, axis, steps):
    count = lax.axis_size(axis)
    first, last = (max(0, -steps), min(count, count - steps))
    return lax.ppermute(value, axis, [(source, source + steps) for source in range(first, last)])


def _vmem_specs(n):
    return [pl.BlockSpec(memory_space=pltpu.VMEM) for _ in range(n)]


def _rows_times(blocks_ref, index, vec):
    terms = [blocks_ref[index + (a,)] * vec[a : a + 1, :] for a in range(vec.shape[0])]
    while len(terms) > 1:
        paired = [terms[j] + terms[j + 1] for j in range(0, len(terms) - 1, 2)]
        if len(terms) % 2:
            paired.append(terms[-1])
        terms = paired
    return terms[0]


def _init_carry(carry_ref, inc_ref):
    if inc_ref is not None:
        carry_ref[...] = inc_ref[...]
        return
    slots, width, conds, nv, lanes = carry_ref.shape
    rows = lax.broadcasted_iota(jnp.int32, (nv, lanes), 0)
    for slot in range(slots):
        for k in range(width):
            unit = (rows == k - slot * nv).astype(jnp.float32)
            for c in range(conds):
                carry_ref[slot, k, c] = unit


def upper_pallas(rhs, near_t, far_t, incoming, want_values):
    count, conds, nv = near_t.shape[0], near_t.shape[1], near_t.shape[2]
    has_inc = not isinstance(incoming, tuple)
    shape = incoming.shape if has_inc else incoming
    width = shape[1]
    has_rhs = rhs is not None

    def kernel(*refs):
        refs = list(refs)
        rhs_ref = refs.pop(0) if has_rhs else None
        nt_ref, ft_ref = refs.pop(0), refs.pop(0)
        inc_ref = refs.pop(0) if has_inc else None
        outs = refs
        if want_values:
            val_ref, carry_ref = outs
        else:
            (carry_ref,) = outs
        if width == 1:
            lasts = [inc_ref[0, 0, c] for c in range(conds)]
            befores = [inc_ref[1, 0, c] for c in range(conds)]
            for i in range(count):
                for c in range(conds):
                    acc = _rows_times(nt_ref, (i, c), lasts[c]) + _rows_times(
                        ft_ref, (i, c), befores[c]
                    )
                    now = rhs_ref[i, c] - acc
                    befores[c] = lasts[c]
                    lasts[c] = now
                    if want_values:
                        val_ref[i, c] = now
            for c in range(conds):
                carry_ref[0, 0, c] = lasts[c]
                carry_ref[1, 0, c] = befores[c]
            return
        _init_carry(carry_ref, inc_ref)

        def step(i, unused):
            for k in range(width):
                for c in range(conds):
                    last = carry_ref[0, k, c]
                    before = carry_ref[1, k, c]
                    acc = _rows_times(nt_ref, (i, c), last) + _rows_times(ft_ref, (i, c), before)
                    if has_rhs:
                        now = rhs_ref[i, c] - acc
                    else:
                        now = -acc
                    carry_ref[1, k, c] = last
                    carry_ref[0, k, c] = now
                    if want_values:
                        val_ref[i, c] = now
            return unused

        lax.fori_loop(0, count, step, 0)

    out_shape = [jax.ShapeDtypeStruct(shape, jnp.float32)]
    if want_values:
        out_shape = [jax.ShapeDtypeStruct(rhs.shape, jnp.float32)] + out_shape
    args = ([rhs] if has_rhs else []) + [near_t, far_t] + ([incoming] if has_inc else [])
    return pl.pallas_call(
        kernel,
        out_shape=tuple(out_shape),
        in_specs=_vmem_specs(len(args)),
        out_specs=tuple(_vmem_specs(len(out_shape))),
    )(*args)


def lower_pallas(rhs, inverse, near, far, incoming, want_values):
    count, conds, nv = inverse.shape[0], inverse.shape[1], inverse.shape[2]
    has_inc = not isinstance(incoming, tuple)
    shape = incoming.shape if has_inc else incoming
    width = shape[1]
    has_rhs = rhs is not None

    def kernel(*refs):
        refs = list(refs)
        rhs_ref = refs.pop(0) if has_rhs else None
        d_ref, b_ref, a_ref = refs.pop(0), refs.pop(0), refs.pop(0)
        inc_ref = refs.pop(0) if has_inc else None
        outs = refs
        if want_values:
            val_ref, carry_ref = outs
        else:
            (carry_ref,) = outs
        if width == 1:
            pendings = [inc_ref[0, 0, c] for c in range(conds)]
            partials = [inc_ref[1, 0, c] for c in range(conds)]
            for i in range(count - 1, -1, -1):
                for c in range(conds):
                    now = _rows_times(d_ref, (i, c), rhs_ref[i, c] - pendings[c])
                    pendings[c] = partials[c] + _rows_times(b_ref, (i, c), now)
                    partials[c] = _rows_times(a_ref, (i, c), now)
                    if want_values:
                        val_ref[i, c] = now
            for c in range(conds):
                carry_ref[0, 0, c] = pendings[c]
                carry_ref[1, 0, c] = partials[c]
            return
        _init_carry(carry_ref, inc_ref)

        def step(t, unused):
            i = count - 1 - t
            for k in range(width):
                for c in range(conds):
                    pending = carry_ref[0, k, c]
                    partial_value = carry_ref[1, k, c]
                    if has_rhs:
                        r = rhs_ref[i, c] - pending
                    else:
                        r = -pending
                    now = _rows_times(d_ref, (i, c), r)
                    carry_ref[0, k, c] = partial_value + _rows_times(b_ref, (i, c), now)
                    carry_ref[1, k, c] = _rows_times(a_ref, (i, c), now)
                    if want_values:
                        val_ref[i, c] = now
            return unused

        lax.fori_loop(0, count, step, 0)

    out_shape = [jax.ShapeDtypeStruct(shape, jnp.float32)]
    if want_values:
        out_shape = [jax.ShapeDtypeStruct(rhs.shape, jnp.float32)] + out_shape
    args = ([rhs] if has_rhs else []) + [inverse, near, far] + ([incoming] if has_inc else [])
    return pl.pallas_call(
        kernel,
        out_shape=tuple(out_shape),
        in_specs=_vmem_specs(len(args)),
        out_specs=tuple(_vmem_specs(len(out_shape))),
    )(*args)


def lower_update(rhs, inverse, near, far, incoming, psi, keep):
    count, conds = inverse.shape[0], inverse.shape[1]

    def kernel(rhs_ref, d_ref, b_ref, a_ref, inc_ref, psi_ref, keep_ref, out_ref):
        for c in range(conds):
            pending, partial_value = inc_ref[0, 0, c], inc_ref[1, 0, c]
            for i in range(count - 1, -1, -1):
                now = _rows_times(d_ref, (i, c), rhs_ref[i, c] - pending)
                pending = partial_value + _rows_times(b_ref, (i, c), now)
                partial_value = _rows_times(a_ref, (i, c), now)
                out_ref[i, c] = (psi_ref[i, c] + 0.05 * now) * keep_ref[i : i + 1, :]

    return pl.pallas_call(
        kernel,
        out_shape=jax.ShapeDtypeStruct(psi.shape, jnp.float32),
        in_specs=_vmem_specs(7),
        out_specs=pl.BlockSpec(memory_space=pltpu.VMEM),
    )(rhs, inverse, near, far, incoming, psi, keep)


def upper_then_lower(rhs, near_t, far_t, incoming, inverse, near, far):
    count, conds = near_t.shape[0], near_t.shape[1]
    carry = jax.ShapeDtypeStruct((2, 1) + rhs.shape[1:], jnp.float32)

    def kernel(rhs_ref, nt_ref, ft_ref, inc_ref, d_ref, b_ref, a_ref, val_ref, carry_ref):
        for c in range(conds):
            last, before = inc_ref[0, 0, c], inc_ref[1, 0, c]
            for i in range(count):
                acc = _rows_times(nt_ref, (i, c), last) + _rows_times(ft_ref, (i, c), before)
                before, last = last, rhs_ref[i, c] - acc
                val_ref[i, c] = last
            pending = None
            partial_value = None
            for i in range(count - 1, -1, -1):
                r = val_ref[i, c] if pending is None else val_ref[i, c] - pending
                now = _rows_times(d_ref, (i, c), r)
                near_part = _rows_times(b_ref, (i, c), now)
                pending = near_part if partial_value is None else partial_value + near_part
                partial_value = _rows_times(a_ref, (i, c), now)
            carry_ref[0, 0, c] = pending
            carry_ref[1, 0, c] = partial_value

    return pl.pallas_call(
        kernel,
        out_shape=(jax.ShapeDtypeStruct(rhs.shape, jnp.float32), carry),
        in_specs=_vmem_specs(7),
        out_specs=tuple(_vmem_specs(2)),
    )(rhs, near_t, far_t, incoming, inverse, near, far)


def carry_through(vector, response):
    slots, width, conds, nv, lanes = response.shape
    split = response.reshape(slots, slots, nv, conds, nv, lanes)
    inputs = jnp.transpose(vector, (0, 2, 1, 3))[None, :, :, :, None, :]
    return jnp.sum(jnp.sum(split * inputs, axis=2), axis=1)


def shifted_operators(matrix, steps):
    count = lax.axis_size("gx")
    return [from_behind(matrix, "gx", steps * s) for s in range(1, count - 1)]


def gathered_carry(vector, operators, steps):
    count = lax.axis_size("gx")
    if count == 1:
        return jnp.zeros_like(vector)
    total = from_behind(vector, "gx", steps * (count - 1))
    for s in range(count - 2, 0, -1):
        total = carry_through(total, operators[s - 1]) + from_behind(
            vector, "gx", steps * s
        )
    return total


def relayed_carry(vector, behind, steps):
    count = lax.axis_size("gx")
    if count == 1:
        return jnp.zeros_like(vector)
    nearest = from_behind(vector, "gx", steps)
    if count == 2:
        return nearest
    total = nearest + carry_through(from_behind(vector, "gx", 2 * steps), behind)
    for _ in range(count - 3):
        total = nearest + carry_through(from_behind(total, "gx", steps), behind)
    return total


def on_device(
    psi_old,
    objective_grad,
    near_upper,
    far_upper,
    inverse_diag,
    near_lower,
    far_lower,
    y_inverse,
    z_inverse,
    sens_terms,
    wall_mask,
    cond_index,
    weight_table,
):
    keep_rows = 1.0 - wall_mask.astype(jnp.float32)
    carry_shape = psi_old.shape[1:]
    zeros = jnp.zeros((2, 1) + carry_shape, jnp.float32)
    units = (2, 2 * carry_shape[1]) + carry_shape
    near_t = jnp.swapaxes(near_upper, 2, 3)
    far_t = jnp.swapaxes(far_upper, 2, 3)
    (response,) = upper_pallas(None, near_t, far_t, units, False)
    matrix = response
    (response,) = lower_pallas(None, inverse_diag, near_lower, far_lower, units, False)
    reverse_matrix = response
    upper_products = shifted_operators(matrix, 1)
    lower_behind = from_behind(reverse_matrix, "gx", -1)
    psi = psi_old
    for step in range(ITERS):
        stream_pad = extended(psi, (("gx", 0),), 1)
        span_pad = extended(psi, (("gy", 3),), NZ)
        beside_all = (
            stream_pad[2:] + stream_pad[:-2] + span_pad[..., 2 * NZ :] + span_pad[..., : -2 * NZ]
        )
        rhs = objective_grad + 0.5 * beside_all - 2.0 * psi
        grid = rhs.reshape(rhs.shape[0], rhs.shape[1], rhs.shape[2], rhs.shape[3] // NZ, NZ)
        zres = jnp.einsum(
            "icvjq,cvqk->icvjk", grid, z_inverse, precision=lax.Precision.HIGHEST
        ).reshape(rhs.shape)
        yres = jnp.sum(y_inverse * zres[..., :, None, :], axis=-3)
        (offset,) = upper_pallas(yres, near_t, far_t, zeros, False)
        entering = gathered_carry(offset[:, 0], upper_products, 1)
        upper, offset = upper_then_lower(
            yres, near_t, far_t, entering[:, None], inverse_diag, near_lower, far_lower
        )
        entering = relayed_carry(offset[:, 0], lower_behind, -1)
        psi = lower_update(
            upper, inverse_diag, near_lower, far_lower, entering[:, None], psi, keep_rows
        )
    onehot = (cond_index[:, None] == jnp.arange(weight_table.shape[0])[None, :]).astype(jnp.float32)
    weights = jnp.sum(onehot * weight_table[None, :], axis=1)
    local_sens = jnp.einsum(
        "icvl,icmvl->iml",
        psi * weights[None, :, None, None],
        sens_terms,
        precision=lax.Precision.HIGHEST,
    )
    if lax.axis_size("cond") == 2:
        mesh_sens = local_sens + lax.ppermute(local_sens, "cond", [(0, 1), (1, 0)])
    else:
        mesh_sens = lax.psum(local_sens, "cond")
    return (psi, mesh_sens)


def solution(mesh):
    placed = (
        P("gx", "cond", None, "gy"),
        P("gx", "cond", None, "gy"),
        P("gx", "cond", None, None, "gy"),
        P("gx", "cond", None, None, "gy"),
        P("gx", "cond", None, None, "gy"),
        P("gx", "cond", None, None, "gy"),
        P("gx", "cond", None, None, "gy"),
        P("gx", "cond", None, None, "gy"),
        P("cond", None, None, None),
        P("gx", "cond", None, None, "gy"),
        P("gx", "gy"),
        P("cond"),
        P(),
    )
    return jax.shard_map(
        on_device,
        mesh=mesh,
        in_specs=placed,
        out_specs=(P("gx", "cond", None, "gy"), P("gx", None, "gy")),
        check_vma=False,
    )
```

```python
import jax
import jax.numpy as jnp
from jax import lax
from jax.experimental import pallas as pl
from jax.experimental.pallas import tpu as pltpu
from jax.sharding import PartitionSpec as P

NZ = 32
ITERS = 2


def extended(value, sides, width):
    for axis, dim in sides:
        size, length = (lax.axis_size(axis), value.shape[dim])
        up = [(i, (i + 1) % size) for i in range(size - 1)]
        down = [(j, i) for i, j in up]
        last = lax.slice_in_dim(value, length - width, length, axis=dim)
        first = lax.slice_in_dim(value, 0, width, axis=dim)
        before = lax.ppermute(last, axis, up)
        after = lax.ppermute(first, axis, down)
        value = jnp.concatenate([before, value, after], axis=dim)
    return value


def from_behind(value, axis, steps):
    count = lax.axis_size(axis)
    first, last = (max(0, -steps), min(count, count - steps))
    return lax.ppermute(value, axis, [(source, source + steps) for source in range(first, last)])


def _vmem_specs(n):
    return [pl.BlockSpec(memory_space=pltpu.VMEM) for _ in range(n)]


def _rows_times(blocks_ref, index, vec):
    terms = [blocks_ref[index + (a,)] * vec[a : a + 1, :] for a in range(vec.shape[0])]
    while len(terms) > 1:
        paired = [terms[j] + terms[j + 1] for j in range(0, len(terms) - 1, 2)]
        if len(terms) % 2:
            paired.append(terms[-1])
        terms = paired
    return terms[0]


def _init_carry(carry_ref, inc_ref):
    if inc_ref is not None:
        carry_ref[...] = inc_ref[...]
        return
    slots, width, conds, nv, lanes = carry_ref.shape
    rows = lax.broadcasted_iota(jnp.int32, (nv, lanes), 0)
    for slot in range(slots):
        for k in range(width):
            unit = (rows == k - slot * nv).astype(jnp.float32)
            for c in range(conds):
                carry_ref[slot, k, c] = unit


def upper_pallas(rhs, near_t, far_t, incoming, want_values):
    count, conds, nv = near_t.shape[0], near_t.shape[1], near_t.shape[2]
    has_inc = not isinstance(incoming, tuple)
    shape = incoming.shape if has_inc else incoming
    width = shape[1]
    has_rhs = rhs is not None

    def kernel(*refs):
        refs = list(refs)
        rhs_ref = refs.pop(0) if has_rhs else None
        nt_ref, ft_ref = refs.pop(0), refs.pop(0)
        inc_ref = refs.pop(0) if has_inc else None
        outs = refs
        if want_values:
            val_ref, carry_ref = outs
        else:
            (carry_ref,) = outs
        if width == 1:
            lasts = [inc_ref[0, 0, c] for c in range(conds)]
            befores = [inc_ref[1, 0, c] for c in range(conds)]
            for i in range(count):
                for c in range(conds):
                    acc = _rows_times(nt_ref, (i, c), lasts[c]) + _rows_times(
                        ft_ref, (i, c), befores[c]
                    )
                    now = rhs_ref[i, c] - acc
                    befores[c] = lasts[c]
                    lasts[c] = now
                    if want_values:
                        val_ref[i, c] = now
            for c in range(conds):
                carry_ref[0, 0, c] = lasts[c]
                carry_ref[1, 0, c] = befores[c]
            return
        _init_carry(carry_ref, inc_ref)

        def step(i, unused):
            for k in range(width):
                for c in range(conds):
                    last = carry_ref[0, k, c]
                    before = carry_ref[1, k, c]
                    acc = _rows_times(nt_ref, (i, c), last) + _rows_times(ft_ref, (i, c), before)
                    if has_rhs:
                        now = rhs_ref[i, c] - acc
                    else:
                        now = -acc
                    carry_ref[1, k, c] = last
                    carry_ref[0, k, c] = now
                    if want_values:
                        val_ref[i, c] = now
            return unused

        lax.fori_loop(0, count, step, 0)

    out_shape = [jax.ShapeDtypeStruct(shape, jnp.float32)]
    if want_values:
        out_shape = [jax.ShapeDtypeStruct(rhs.shape, jnp.float32)] + out_shape
    args = ([rhs] if has_rhs else []) + [near_t, far_t] + ([incoming] if has_inc else [])
    return pl.pallas_call(
        kernel,
        out_shape=tuple(out_shape),
        in_specs=_vmem_specs(len(args)),
        out_specs=tuple(_vmem_specs(len(out_shape))),
    )(*args)


def lower_pallas(rhs, inverse, near, far, incoming, want_values):
    count, conds, nv = inverse.shape[0], inverse.shape[1], inverse.shape[2]
    has_inc = not isinstance(incoming, tuple)
    shape = incoming.shape if has_inc else incoming
    width = shape[1]
    has_rhs = rhs is not None

    def kernel(*refs):
        refs = list(refs)
        rhs_ref = refs.pop(0) if has_rhs else None
        d_ref, b_ref, a_ref = refs.pop(0), refs.pop(0), refs.pop(0)
        inc_ref = refs.pop(0) if has_inc else None
        outs = refs
        if want_values:
            val_ref, carry_ref = outs
        else:
            (carry_ref,) = outs
        if width == 1:
            pendings = [inc_ref[0, 0, c] for c in range(conds)]
            partials = [inc_ref[1, 0, c] for c in range(conds)]
            for i in range(count - 1, -1, -1):
                for c in range(conds):
                    now = _rows_times(d_ref, (i, c), rhs_ref[i, c] - pendings[c])
                    pendings[c] = partials[c] + _rows_times(b_ref, (i, c), now)
                    partials[c] = _rows_times(a_ref, (i, c), now)
                    if want_values:
                        val_ref[i, c] = now
            for c in range(conds):
                carry_ref[0, 0, c] = pendings[c]
                carry_ref[1, 0, c] = partials[c]
            return
        _init_carry(carry_ref, inc_ref)

        def step(t, unused):
            i = count - 1 - t
            for k in range(width):
                for c in range(conds):
                    pending = carry_ref[0, k, c]
                    partial_value = carry_ref[1, k, c]
                    if has_rhs:
                        r = rhs_ref[i, c] - pending
                    else:
                        r = -pending
                    now = _rows_times(d_ref, (i, c), r)
                    carry_ref[0, k, c] = partial_value + _rows_times(b_ref, (i, c), now)
                    carry_ref[1, k, c] = _rows_times(a_ref, (i, c), now)
                    if want_values:
                        val_ref[i, c] = now
            return unused

        lax.fori_loop(0, count, step, 0)

    out_shape = [jax.ShapeDtypeStruct(shape, jnp.float32)]
    if want_values:
        out_shape = [jax.ShapeDtypeStruct(rhs.shape, jnp.float32)] + out_shape
    args = ([rhs] if has_rhs else []) + [inverse, near, far] + ([incoming] if has_inc else [])
    return pl.pallas_call(
        kernel,
        out_shape=tuple(out_shape),
        in_specs=_vmem_specs(len(args)),
        out_specs=tuple(_vmem_specs(len(out_shape))),
    )(*args)


def lower_update(rhs, inverse, near, far, incoming, psi, keep):
    count, conds = inverse.shape[0], inverse.shape[1]

    def kernel(rhs_ref, d_ref, b_ref, a_ref, inc_ref, psi_ref, keep_ref, out_ref):
        for c in range(conds):
            pending, partial_value = inc_ref[0, 0, c], inc_ref[1, 0, c]
            for i in range(count - 1, -1, -1):
                now = _rows_times(d_ref, (i, c), rhs_ref[i, c] - pending)
                pending = partial_value + _rows_times(b_ref, (i, c), now)
                partial_value = _rows_times(a_ref, (i, c), now)
                out_ref[i, c] = (psi_ref[i, c] + 0.05 * now) * keep_ref[i : i + 1, :]

    return pl.pallas_call(
        kernel,
        out_shape=jax.ShapeDtypeStruct(psi.shape, jnp.float32),
        in_specs=_vmem_specs(7),
        out_specs=pl.BlockSpec(memory_space=pltpu.VMEM),
    )(rhs, inverse, near, far, incoming, psi, keep)


def upper_then_lower(rhs, near_t, far_t, incoming, inverse, near, far):
    count, conds = near_t.shape[0], near_t.shape[1]
    carry = jax.ShapeDtypeStruct((2, 1) + rhs.shape[1:], jnp.float32)

    def kernel(rhs_ref, nt_ref, ft_ref, inc_ref, d_ref, b_ref, a_ref, val_ref, carry_ref):
        for c in range(conds):
            last, before = inc_ref[0, 0, c], inc_ref[1, 0, c]
            for i in range(count):
                acc = _rows_times(nt_ref, (i, c), last) + _rows_times(ft_ref, (i, c), before)
                before, last = last, rhs_ref[i, c] - acc
                val_ref[i, c] = last
            pending = None
            partial_value = None
            for i in range(count - 1, -1, -1):
                r = val_ref[i, c] if pending is None else val_ref[i, c] - pending
                now = _rows_times(d_ref, (i, c), r)
                near_part = _rows_times(b_ref, (i, c), now)
                pending = near_part if partial_value is None else partial_value + near_part
                partial_value = _rows_times(a_ref, (i, c), now)
            carry_ref[0, 0, c] = pending
            carry_ref[1, 0, c] = partial_value

    return pl.pallas_call(
        kernel,
        out_shape=(jax.ShapeDtypeStruct(rhs.shape, jnp.float32), carry),
        in_specs=_vmem_specs(7),
        out_specs=tuple(_vmem_specs(2)),
    )(rhs, near_t, far_t, incoming, inverse, near, far)


def carry_through(vector, response):
    slots, width, conds, nv, lanes = response.shape
    split = response.reshape(slots, slots, nv, conds, nv, lanes)
    inputs = jnp.transpose(vector, (0, 2, 1, 3))[None, :, :, :, None, :]
    return jnp.sum(jnp.sum(split * inputs, axis=2), axis=1)


def shifted_operators(matrix, steps):
    count = lax.axis_size("gx")
    return [from_behind(matrix, "gx", steps * s) for s in range(1, count - 1)]


def gathered_carry(vector, operators, steps):
    count = lax.axis_size("gx")
    if count == 1:
        return jnp.zeros_like(vector)
    total = from_behind(vector, "gx", steps * (count - 1))
    for s in range(count - 2, 0, -1):
        total = carry_through(total, operators[s - 1]) + from_behind(
            vector, "gx", steps * s
        )
    return total


def relayed_carry(vector, behind, steps):
    count = lax.axis_size("gx")
    if count == 1:
        return jnp.zeros_like(vector)
    nearest = from_behind(vector, "gx", steps)
    if count == 2:
        return nearest
    total = nearest + carry_through(from_behind(vector, "gx", 2 * steps), behind)
    for _ in range(count - 3):
        total = nearest + carry_through(from_behind(total, "gx", steps), behind)
    return total


def on_device(
    psi_old,
    objective_grad,
    near_upper,
    far_upper,
    inverse_diag,
    near_lower,
    far_lower,
    y_inverse,
    z_inverse,
    sens_terms,
    wall_mask,
    cond_index,
    weight_table,
):
    keep_rows = 1.0 - wall_mask.astype(jnp.float32)
    carry_shape = psi_old.shape[1:]
    zeros = jnp.zeros((2, 1) + carry_shape, jnp.float32)
    units = (2, 2 * carry_shape[1]) + carry_shape
    near_t = jnp.swapaxes(near_upper, 2, 3)
    far_t = jnp.swapaxes(far_upper, 2, 3)
    (response,) = upper_pallas(None, near_t, far_t, units, False)
    matrix = response
    (response,) = lower_pallas(None, inverse_diag, near_lower, far_lower, units, False)
    reverse_matrix = response
    upper_products = shifted_operators(matrix, 1)
    psi = psi_old
    for step in range(ITERS):
        if step == 0:
            size = lax.axis_size("gx")
            up = [(i, i + 1) for i in range(size - 1)]
            down = [(j, i) for i, j in up]
            first = psi[:1]
            bundle = jnp.concatenate([first.reshape(-1), reverse_matrix.reshape(-1)])
            bundle = lax.ppermute(bundle, "gx", down)
            after = bundle[: first.size].reshape(first.shape)
            lower_behind = bundle[first.size :].reshape(reverse_matrix.shape)
            before = lax.ppermute(psi[-1:], "gx", up)
            stream_pad = jnp.concatenate([before, psi, after], axis=0)
        else:
            stream_pad = extended(psi, (("gx", 0),), 1)
        span_pad = extended(psi, (("gy", 3),), NZ)
        beside_all = (
            stream_pad[2:] + stream_pad[:-2] + span_pad[..., 2 * NZ :] + span_pad[..., : -2 * NZ]
        )
        rhs = objective_grad + 0.5 * beside_all - 2.0 * psi
        grid = rhs.reshape(rhs.shape[0], rhs.shape[1], rhs.shape[2], rhs.shape[3] // NZ, NZ)
        zres = jnp.einsum(
            "icvjq,cvqk->icvjk", grid, z_inverse, precision=lax.Precision.HIGHEST
        ).reshape(rhs.shape)
        yres = jnp.sum(y_inverse * zres[..., :, None, :], axis=-3)
        (offset,) = upper_pallas(yres, near_t, far_t, zeros, False)
        entering = gathered_carry(offset[:, 0], upper_products, 1)
        upper, offset = upper_then_lower(
            yres, near_t, far_t, entering[:, None], inverse_diag, near_lower, far_lower
        )
        entering = relayed_carry(offset[:, 0], lower_behind, -1)
        psi = lower_update(
            upper, inverse_diag, near_lower, far_lower, entering[:, None], psi, keep_rows
        )
    onehot = (cond_index[:, None] == jnp.arange(weight_table.shape[0])[None, :]).astype(jnp.float32)
    weights = jnp.sum(onehot * weight_table[None, :], axis=1)
    local_sens = jnp.einsum(
        "icvl,icmvl->iml",
        psi * weights[None, :, None, None],
        sens_terms,
        precision=lax.Precision.HIGHEST,
    )
    if lax.axis_size("cond") == 2:
        mesh_sens = local_sens + lax.ppermute(local_sens, "cond", [(0, 1), (1, 0)])
    else:
        mesh_sens = lax.psum(local_sens, "cond")
    return (psi, mesh_sens)


def solution(mesh):
    placed = (
        P("gx", "cond", None, "gy"),
        P("gx", "cond", None, "gy"),
        P("gx", "cond", None, None, "gy"),
        P("gx", "cond", None, None, "gy"),
        P("gx", "cond", None, None, "gy"),
        P("gx", "cond", None, None, "gy"),
        P("gx", "cond", None, None, "gy"),
        P("gx", "cond", None, None, "gy"),
        P("cond", None, None, None),
        P("gx", "cond", None, None, "gy"),
        P("gx", "gy"),
        P("cond"),
        P(),
    )
    return jax.shard_map(
        on_device,
        mesh=mesh,
        in_specs=placed,
        out_specs=(P("gx", "cond", None, "gy"), P("gx", None, "gy")),
        check_vma=False,
    )
```

```python
import jax
import jax.numpy as jnp
from jax import lax
from jax.experimental import pallas as pl
from jax.experimental.pallas import tpu as pltpu
from jax.sharding import PartitionSpec as P


NZ = 32
ITERS = 2


def extended(value, sides, width):
    for axis, dim in sides:
        size, length = (lax.axis_size(axis), value.shape[dim])
        up = [(i, (i + 1) % size) for i in range(size - 1)]
        down = [(j, i) for i, j in up]
        last = lax.slice_in_dim(value, length - width, length, axis=dim)
        first = lax.slice_in_dim(value, 0, width, axis=dim)
        before = lax.ppermute(last, axis, up)
        after = lax.ppermute(first, axis, down)
        value = jnp.concatenate([before, value, after], axis=dim)
    return value


def from_behind(value, axis, steps):
    count = lax.axis_size(axis)
    first, last = (max(0, -steps), min(count, count - steps))
    return lax.ppermute(value, axis, [(source, source + steps) for source in range(first, last)])


def _vmem_specs(n):
    return [pl.BlockSpec(memory_space=pltpu.VMEM) for _ in range(n)]


def _rows_times(blocks_ref, index, vec):
    terms = [blocks_ref[index + (a,)] * vec[a : a + 1, :] for a in range(vec.shape[0])]
    while len(terms) > 1:
        paired = [terms[j] + terms[j + 1] for j in range(0, len(terms) - 1, 2)]
        if len(terms) % 2:
            paired.append(terms[-1])
        terms = paired
    return terms[0]


def _init_carry(carry_ref, inc_ref):
    if inc_ref is not None:
        carry_ref[...] = inc_ref[...]
        return
    slots, width, conds, nv, lanes = carry_ref.shape
    rows = lax.broadcasted_iota(jnp.int32, (nv, lanes), 0)
    for slot in range(slots):
        for k in range(width):
            unit = (rows == k - slot * nv).astype(jnp.float32)
            for c in range(conds):
                carry_ref[slot, k, c] = unit


def upper_pallas(rhs, near_t, far_t, incoming, want_values):
    count, conds, nv = near_t.shape[0], near_t.shape[1], near_t.shape[2]
    has_inc = not isinstance(incoming, tuple)
    shape = incoming.shape if has_inc else incoming
    width = shape[1]
    has_rhs = rhs is not None

    def kernel(*refs):
        refs = list(refs)
        rhs_ref = refs.pop(0) if has_rhs else None
        nt_ref, ft_ref = refs.pop(0), refs.pop(0)
        inc_ref = refs.pop(0) if has_inc else None
        outs = refs
        if want_values:
            val_ref, carry_ref = outs
        else:
            (carry_ref,) = outs
        if width == 1:
            lasts = [inc_ref[0, 0, c] for c in range(conds)]
            befores = [inc_ref[1, 0, c] for c in range(conds)]
            for i in range(count):
                for c in range(conds):
                    acc = _rows_times(nt_ref, (i, c), lasts[c]) + _rows_times(
                        ft_ref, (i, c), befores[c]
                    )
                    now = rhs_ref[i, c] - acc
                    befores[c] = lasts[c]
                    lasts[c] = now
                    if want_values:
                        val_ref[i, c] = now
            for c in range(conds):
                carry_ref[0, 0, c] = lasts[c]
                carry_ref[1, 0, c] = befores[c]
            return
        _init_carry(carry_ref, inc_ref)

        def step(i, unused):
            for k in range(width):
                for c in range(conds):
                    last = carry_ref[0, k, c]
                    before = carry_ref[1, k, c]
                    acc = _rows_times(nt_ref, (i, c), last) + _rows_times(ft_ref, (i, c), before)
                    if has_rhs:
                        now = rhs_ref[i, c] - acc
                    else:
                        now = -acc
                    carry_ref[1, k, c] = last
                    carry_ref[0, k, c] = now
                    if want_values:
                        val_ref[i, c] = now
            return unused

        lax.fori_loop(0, count, step, 0)

    out_shape = [jax.ShapeDtypeStruct(shape, jnp.float32)]
    if want_values:
        out_shape = [jax.ShapeDtypeStruct(rhs.shape, jnp.float32)] + out_shape
    args = ([rhs] if has_rhs else []) + [near_t, far_t] + ([incoming] if has_inc else [])
    return pl.pallas_call(
        kernel,
        out_shape=tuple(out_shape),
        in_specs=_vmem_specs(len(args)),
        out_specs=tuple(_vmem_specs(len(out_shape))),
    )(*args)


def lower_pallas(rhs, inverse, near, far, incoming, want_values):
    count, conds, nv = inverse.shape[0], inverse.shape[1], inverse.shape[2]
    has_inc = not isinstance(incoming, tuple)
    shape = incoming.shape if has_inc else incoming
    width = shape[1]
    has_rhs = rhs is not None

    def kernel(*refs):
        refs = list(refs)
        rhs_ref = refs.pop(0) if has_rhs else None
        d_ref, b_ref, a_ref = refs.pop(0), refs.pop(0), refs.pop(0)
        inc_ref = refs.pop(0) if has_inc else None
        outs = refs
        if want_values:
            val_ref, carry_ref = outs
        else:
            (carry_ref,) = outs
        if width == 1:
            pendings = [inc_ref[0, 0, c] for c in range(conds)]
            partials = [inc_ref[1, 0, c] for c in range(conds)]
            for i in range(count - 1, -1, -1):
                for c in range(conds):
                    now = _rows_times(d_ref, (i, c), rhs_ref[i, c] - pendings[c])
                    pendings[c] = partials[c] + _rows_times(b_ref, (i, c), now)
                    partials[c] = _rows_times(a_ref, (i, c), now)
                    if want_values:
                        val_ref[i, c] = now
            for c in range(conds):
                carry_ref[0, 0, c] = pendings[c]
                carry_ref[1, 0, c] = partials[c]
            return
        _init_carry(carry_ref, inc_ref)

        def step(t, unused):
            i = count - 1 - t
            for k in range(width):
                for c in range(conds):
                    pending = carry_ref[0, k, c]
                    partial_value = carry_ref[1, k, c]
                    if has_rhs:
                        r = rhs_ref[i, c] - pending
                    else:
                        r = -pending
                    now = _rows_times(d_ref, (i, c), r)
                    carry_ref[0, k, c] = partial_value + _rows_times(b_ref, (i, c), now)
                    carry_ref[1, k, c] = _rows_times(a_ref, (i, c), now)
                    if want_values:
                        val_ref[i, c] = now
            return unused

        lax.fori_loop(0, count, step, 0)

    out_shape = [jax.ShapeDtypeStruct(shape, jnp.float32)]
    if want_values:
        out_shape = [jax.ShapeDtypeStruct(rhs.shape, jnp.float32)] + out_shape
    args = ([rhs] if has_rhs else []) + [inverse, near, far] + ([incoming] if has_inc else [])
    return pl.pallas_call(
        kernel,
        out_shape=tuple(out_shape),
        in_specs=_vmem_specs(len(args)),
        out_specs=tuple(_vmem_specs(len(out_shape))),
    )(*args)


def upper_then_lower(rhs, near_t, far_t, incoming, inverse, near, far):
    count, conds = near_t.shape[0], near_t.shape[1]
    carry = jax.ShapeDtypeStruct((2, 1) + rhs.shape[1:], jnp.float32)

    def kernel(rhs_ref, nt_ref, ft_ref, inc_ref, d_ref, b_ref, a_ref, val_ref, carry_ref):
        for c in range(conds):
            last, before = inc_ref[0, 0, c], inc_ref[1, 0, c]
            for i in range(count):
                acc = _rows_times(nt_ref, (i, c), last) + _rows_times(ft_ref, (i, c), before)
                before, last = last, rhs_ref[i, c] - acc
                val_ref[i, c] = last
            pending = None
            partial_value = None
            for i in range(count - 1, -1, -1):
                r = val_ref[i, c] if pending is None else val_ref[i, c] - pending
                now = _rows_times(d_ref, (i, c), r)
                near_part = _rows_times(b_ref, (i, c), now)
                pending = near_part if partial_value is None else partial_value + near_part
                partial_value = _rows_times(a_ref, (i, c), now)
            carry_ref[0, 0, c] = pending
            carry_ref[1, 0, c] = partial_value

    return pl.pallas_call(
        kernel,
        out_shape=(jax.ShapeDtypeStruct(rhs.shape, jnp.float32), carry),
        in_specs=_vmem_specs(7),
        out_specs=tuple(_vmem_specs(2)),
    )(rhs, near_t, far_t, incoming, inverse, near, far)


def carry_through(vector, response):
    slots, width, conds, nv, lanes = response.shape
    split = response.reshape(slots, slots, nv, conds, nv, lanes)
    inputs = jnp.transpose(vector, (0, 2, 1, 3))[None, :, :, :, None, :]
    return jnp.sum(jnp.sum(split * inputs, axis=2), axis=1)


def shifted_operators(matrix, steps):
    count = lax.axis_size("gx")
    return [from_behind(matrix, "gx", steps * s) for s in range(1, count - 1)]


def gathered_carry(vector, operators, steps):
    count = lax.axis_size("gx")
    if count == 1:
        return jnp.zeros_like(vector)
    total = from_behind(vector, "gx", steps * (count - 1))
    for s in range(count - 2, 0, -1):
        total = carry_through(total, operators[s - 1]) + from_behind(
            vector, "gx", steps * s
        )
    return total


def relayed_carry(vector, behind, steps):
    count = lax.axis_size("gx")
    if count == 1:
        return jnp.zeros_like(vector)
    nearest = from_behind(vector, "gx", steps)
    if count == 2:
        return nearest
    total = nearest + carry_through(from_behind(vector, "gx", 2 * steps), behind)
    for _ in range(count - 3):
        total = nearest + carry_through(from_behind(total, "gx", steps), behind)
    return total


def on_device(
    psi_old,
    objective_grad,
    near_upper,
    far_upper,
    inverse_diag,
    near_lower,
    far_lower,
    y_inverse,
    z_inverse,
    sens_terms,
    wall_mask,
    cond_index,
    weight_table,
):
    keep = (1.0 - wall_mask.astype(jnp.float32))[:, None, None, :]
    carry_shape = psi_old.shape[1:]
    zeros = jnp.zeros((2, 1) + carry_shape, jnp.float32)
    units = (2, 2 * carry_shape[1]) + carry_shape
    near_t = jnp.swapaxes(near_upper, 2, 3)
    far_t = jnp.swapaxes(far_upper, 2, 3)
    (response,) = upper_pallas(None, near_t, far_t, units, False)
    matrix = response
    (response,) = lower_pallas(None, inverse_diag, near_lower, far_lower, units, False)
    reverse_matrix = response
    upper_behind = from_behind(matrix, "gx", 1)
    lower_behind = from_behind(reverse_matrix, "gx", -1)
    psi = psi_old
    for step in range(ITERS):
        stream_pad = extended(psi, (("gx", 0),), 1)
        span_pad = extended(psi, (("gy", 3),), NZ)
        beside_all = (
            stream_pad[2:] + stream_pad[:-2] + span_pad[..., 2 * NZ :] + span_pad[..., : -2 * NZ]
        )
        rhs = objective_grad + 0.5 * beside_all - 2.0 * psi
        grid = rhs.reshape(rhs.shape[0], rhs.shape[1], rhs.shape[2], rhs.shape[3] // NZ, NZ)
        zres = jnp.einsum(
            "icvjq,cvqk->icvjk", grid, z_inverse, precision=lax.Precision.HIGHEST
        ).reshape(rhs.shape)
        yres = jnp.sum(y_inverse * zres[..., :, None, :], axis=-3)
        (offset,) = upper_pallas(yres, near_t, far_t, zeros, False)
        entering = relayed_carry(offset[:, 0], upper_behind, 1)
        upper, offset = upper_then_lower(
            yres, near_t, far_t, entering[:, None], inverse_diag, near_lower, far_lower
        )
        entering = relayed_carry(offset[:, 0], lower_behind, -1)
        lower, _ = lower_pallas(upper, inverse_diag, near_lower, far_lower, entering[:, None], True)
        psi = (psi + 0.05 * lower) * keep
    onehot = (cond_index[:, None] == jnp.arange(weight_table.shape[0])[None, :]).astype(jnp.float32)
    weights = jnp.sum(onehot * weight_table[None, :], axis=1)
    local_sens = jnp.einsum(
        "icvl,icmvl->iml",
        psi * weights[None, :, None, None],
        sens_terms,
        precision=lax.Precision.HIGHEST,
    )
    if lax.axis_size("cond") == 2:
        mesh_sens = local_sens + lax.ppermute(local_sens, "cond", [(0, 1), (1, 0)])
    else:
        mesh_sens = lax.psum(local_sens, "cond")
    return (psi, mesh_sens)


def solution(mesh):
    placed = (
        P("gx", "cond", None, "gy"),
        P("gx", "cond", None, "gy"),
        P("gx", "cond", None, None, "gy"),
        P("gx", "cond", None, None, "gy"),
        P("gx", "cond", None, None, "gy"),
        P("gx", "cond", None, None, "gy"),
        P("gx", "cond", None, None, "gy"),
        P("gx", "cond", None, None, "gy"),
        P("cond", None, None, None),
        P("gx", "cond", None, None, "gy"),
        P("gx", "gy"),
        P("cond"),
        P(),
    )
    return jax.shard_map(
        on_device,
        mesh=mesh,
        in_specs=placed,
        out_specs=(P("gx", "cond", None, "gy"), P("gx", None, "gy")),
        check_vma=False,
    )
```

```python
import jax
import jax.numpy as jnp
from jax import lax
from jax.experimental import pallas as pl
from jax.experimental.pallas import tpu as pltpu
from jax.sharding import PartitionSpec as P


NZ = 32
ITERS = 2


def extended(value, sides, width):
    for axis, dim in sides:
        size, length = (lax.axis_size(axis), value.shape[dim])
        up = [(i, (i + 1) % size) for i in range(size - 1)]
        down = [(j, i) for i, j in up]
        last = lax.slice_in_dim(value, length - width, length, axis=dim)
        first = lax.slice_in_dim(value, 0, width, axis=dim)
        before = lax.ppermute(last, axis, up)
        after = lax.ppermute(first, axis, down)
        value = jnp.concatenate([before, value, after], axis=dim)
    return value


def from_behind(value, axis, steps):
    count = lax.axis_size(axis)
    first, last = (max(0, -steps), min(count, count - steps))
    return lax.ppermute(value, axis, [(source, source + steps) for source in range(first, last)])


def _vmem_specs(n):
    return [pl.BlockSpec(memory_space=pltpu.VMEM) for _ in range(n)]


def _rows_times(blocks_ref, index, vec):
    terms = [blocks_ref[index + (a,)] * vec[a : a + 1, :] for a in range(vec.shape[0])]
    while len(terms) > 1:
        paired = [terms[j] + terms[j + 1] for j in range(0, len(terms) - 1, 2)]
        if len(terms) % 2:
            paired.append(terms[-1])
        terms = paired
    return terms[0]


def _init_carry(carry_ref, inc_ref):
    if inc_ref is not None:
        carry_ref[...] = inc_ref[...]
        return
    slots, width, conds, nv, lanes = carry_ref.shape
    rows = lax.broadcasted_iota(jnp.int32, (nv, lanes), 0)
    for slot in range(slots):
        for k in range(width):
            unit = (rows == k - slot * nv).astype(jnp.float32)
            for c in range(conds):
                carry_ref[slot, k, c] = unit


def upper_pallas(rhs, near_t, far_t, incoming, want_values):
    count, conds, nv = near_t.shape[0], near_t.shape[1], near_t.shape[2]
    has_inc = not isinstance(incoming, tuple)
    shape = incoming.shape if has_inc else incoming
    width = shape[1]
    has_rhs = rhs is not None

    def kernel(*refs):
        refs = list(refs)
        rhs_ref = refs.pop(0) if has_rhs else None
        nt_ref, ft_ref = refs.pop(0), refs.pop(0)
        inc_ref = refs.pop(0) if has_inc else None
        outs = refs
        if want_values:
            val_ref, carry_ref = outs
        else:
            (carry_ref,) = outs
        if width == 1:
            lasts = [inc_ref[0, 0, c] for c in range(conds)]
            befores = [inc_ref[1, 0, c] for c in range(conds)]
            for i in range(count):
                for c in range(conds):
                    acc = _rows_times(nt_ref, (i, c), lasts[c]) + _rows_times(
                        ft_ref, (i, c), befores[c]
                    )
                    now = rhs_ref[i, c] - acc
                    befores[c] = lasts[c]
                    lasts[c] = now
                    if want_values:
                        val_ref[i, c] = now
            for c in range(conds):
                carry_ref[0, 0, c] = lasts[c]
                carry_ref[1, 0, c] = befores[c]
            return
        _init_carry(carry_ref, inc_ref)

        def step(i, unused):
            for k in range(width):
                for c in range(conds):
                    last = carry_ref[0, k, c]
                    before = carry_ref[1, k, c]
                    acc = _rows_times(nt_ref, (i, c), last) + _rows_times(ft_ref, (i, c), before)
                    if has_rhs:
                        now = rhs_ref[i, c] - acc
                    else:
                        now = -acc
                    carry_ref[1, k, c] = last
                    carry_ref[0, k, c] = now
                    if want_values:
                        val_ref[i, c] = now
            return unused

        lax.fori_loop(0, count, step, 0, unroll=True)

    out_shape = [jax.ShapeDtypeStruct(shape, jnp.float32)]
    if want_values:
        out_shape = [jax.ShapeDtypeStruct(rhs.shape, jnp.float32)] + out_shape
    args = ([rhs] if has_rhs else []) + [near_t, far_t] + ([incoming] if has_inc else [])
    return pl.pallas_call(
        kernel,
        out_shape=tuple(out_shape),
        in_specs=_vmem_specs(len(args)),
        out_specs=tuple(_vmem_specs(len(out_shape))),
    )(*args)


def lower_pallas(rhs, inverse, near, far, incoming, want_values):
    count, conds, nv = inverse.shape[0], inverse.shape[1], inverse.shape[2]
    has_inc = not isinstance(incoming, tuple)
    shape = incoming.shape if has_inc else incoming
    width = shape[1]
    has_rhs = rhs is not None

    def kernel(*refs):
        refs = list(refs)
        rhs_ref = refs.pop(0) if has_rhs else None
        d_ref, b_ref, a_ref = refs.pop(0), refs.pop(0), refs.pop(0)
        inc_ref = refs.pop(0) if has_inc else None
        outs = refs
        if want_values:
            val_ref, carry_ref = outs
        else:
            (carry_ref,) = outs
        if width == 1:
            pendings = [inc_ref[0, 0, c] for c in range(conds)]
            partials = [inc_ref[1, 0, c] for c in range(conds)]
            for i in range(count - 1, -1, -1):
                for c in range(conds):
                    now = _rows_times(d_ref, (i, c), rhs_ref[i, c] - pendings[c])
                    pendings[c] = partials[c] + _rows_times(b_ref, (i, c), now)
                    partials[c] = _rows_times(a_ref, (i, c), now)
                    if want_values:
                        val_ref[i, c] = now
            for c in range(conds):
                carry_ref[0, 0, c] = pendings[c]
                carry_ref[1, 0, c] = partials[c]
            return
        _init_carry(carry_ref, inc_ref)

        def step(t, unused):
            i = count - 1 - t
            for k in range(width):
                for c in range(conds):
                    pending = carry_ref[0, k, c]
                    partial_value = carry_ref[1, k, c]
                    if has_rhs:
                        r = rhs_ref[i, c] - pending
                    else:
                        r = -pending
                    now = _rows_times(d_ref, (i, c), r)
                    carry_ref[0, k, c] = partial_value + _rows_times(b_ref, (i, c), now)
                    carry_ref[1, k, c] = _rows_times(a_ref, (i, c), now)
                    if want_values:
                        val_ref[i, c] = now
            return unused

        lax.fori_loop(0, count, step, 0, unroll=True)

    out_shape = [jax.ShapeDtypeStruct(shape, jnp.float32)]
    if want_values:
        out_shape = [jax.ShapeDtypeStruct(rhs.shape, jnp.float32)] + out_shape
    args = ([rhs] if has_rhs else []) + [inverse, near, far] + ([incoming] if has_inc else [])
    return pl.pallas_call(
        kernel,
        out_shape=tuple(out_shape),
        in_specs=_vmem_specs(len(args)),
        out_specs=tuple(_vmem_specs(len(out_shape))),
    )(*args)


def upper_then_lower(rhs, near_t, far_t, incoming, inverse, near, far):
    count, conds = near_t.shape[0], near_t.shape[1]
    carry = jax.ShapeDtypeStruct((2, 1) + rhs.shape[1:], jnp.float32)

    def kernel(rhs_ref, nt_ref, ft_ref, inc_ref, d_ref, b_ref, a_ref, val_ref, carry_ref):
        for c in range(conds):
            last, before = inc_ref[0, 0, c], inc_ref[1, 0, c]
            for i in range(count):
                acc = _rows_times(nt_ref, (i, c), last) + _rows_times(ft_ref, (i, c), before)
                before, last = last, rhs_ref[i, c] - acc
                val_ref[i, c] = last
            pending = None
            partial_value = None
            for i in range(count - 1, -1, -1):
                r = val_ref[i, c] if pending is None else val_ref[i, c] - pending
                now = _rows_times(d_ref, (i, c), r)
                near_part = _rows_times(b_ref, (i, c), now)
                pending = near_part if partial_value is None else partial_value + near_part
                partial_value = _rows_times(a_ref, (i, c), now)
            carry_ref[0, 0, c] = pending
            carry_ref[1, 0, c] = partial_value

    return pl.pallas_call(
        kernel,
        out_shape=(jax.ShapeDtypeStruct(rhs.shape, jnp.float32), carry),
        in_specs=_vmem_specs(7),
        out_specs=tuple(_vmem_specs(2)),
    )(rhs, near_t, far_t, incoming, inverse, near, far)


def carry_through(vector, response):
    slots, width, conds, nv, lanes = response.shape
    split = response.reshape(slots, slots, nv, conds, nv, lanes)
    inputs = jnp.transpose(vector, (0, 2, 1, 3))[None, :, :, :, None, :]
    return jnp.sum(jnp.sum(split * inputs, axis=2), axis=1)


def shifted_operators(matrix, steps):
    count = lax.axis_size("gx")
    return [from_behind(matrix, "gx", steps * s) for s in range(1, count - 1)]


def gathered_carry(vector, operators, steps):
    count = lax.axis_size("gx")
    if count == 1:
        return jnp.zeros_like(vector)
    total = from_behind(vector, "gx", steps * (count - 1))
    for s in range(count - 2, 0, -1):
        total = carry_through(total, operators[s - 1]) + from_behind(
            vector, "gx", steps * s
        )
    return total


def relayed_carry(vector, behind, steps):
    count = lax.axis_size("gx")
    if count == 1:
        return jnp.zeros_like(vector)
    nearest = from_behind(vector, "gx", steps)
    if count == 2:
        return nearest
    total = nearest + carry_through(from_behind(vector, "gx", 2 * steps), behind)
    for _ in range(count - 3):
        total = nearest + carry_through(from_behind(total, "gx", steps), behind)
    return total


def on_device(
    psi_old,
    objective_grad,
    near_upper,
    far_upper,
    inverse_diag,
    near_lower,
    far_lower,
    y_inverse,
    z_inverse,
    sens_terms,
    wall_mask,
    cond_index,
    weight_table,
):
    keep = (1.0 - wall_mask.astype(jnp.float32))[:, None, None, :]
    carry_shape = psi_old.shape[1:]
    zeros = jnp.zeros((2, 1) + carry_shape, jnp.float32)
    units = (2, 2 * carry_shape[1]) + carry_shape
    near_t = jnp.swapaxes(near_upper, 2, 3)
    far_t = jnp.swapaxes(far_upper, 2, 3)
    (response,) = upper_pallas(None, near_t, far_t, units, False)
    matrix = response
    (response,) = lower_pallas(None, inverse_diag, near_lower, far_lower, units, False)
    reverse_matrix = response
    upper_products = shifted_operators(matrix, 1)
    lower_behind = from_behind(reverse_matrix, "gx", -1)
    psi = psi_old
    for step in range(ITERS):
        stream_pad = extended(psi, (("gx", 0),), 1)
        span_pad = extended(psi, (("gy", 3),), NZ)
        beside_all = (
            stream_pad[2:] + stream_pad[:-2] + span_pad[..., 2 * NZ :] + span_pad[..., : -2 * NZ]
        )
        rhs = objective_grad + 0.5 * beside_all - 2.0 * psi
        grid = rhs.reshape(rhs.shape[0], rhs.shape[1], rhs.shape[2], rhs.shape[3] // NZ, NZ)
        zres = jnp.einsum(
            "icvjq,cvqk->icvjk", grid, z_inverse, precision=lax.Precision.HIGHEST
        ).reshape(rhs.shape)
        yres = jnp.sum(y_inverse * zres[..., :, None, :], axis=-3)
        (offset,) = upper_pallas(yres, near_t, far_t, zeros, False)
        entering = gathered_carry(offset[:, 0], upper_products, 1)
        upper, offset = upper_then_lower(
            yres, near_t, far_t, entering[:, None], inverse_diag, near_lower, far_lower
        )
        entering = relayed_carry(offset[:, 0], lower_behind, -1)
        lower, _ = lower_pallas(upper, inverse_diag, near_lower, far_lower, entering[:, None], True)
        psi = (psi + 0.05 * lower) * keep
    onehot = (cond_index[:, None] == jnp.arange(weight_table.shape[0])[None, :]).astype(jnp.float32)
    weights = jnp.sum(onehot * weight_table[None, :], axis=1)
    local_sens = jnp.einsum(
        "icvl,icmvl->iml",
        psi * weights[None, :, None, None],
        sens_terms,
        precision=lax.Precision.HIGHEST,
    )
    if lax.axis_size("cond") == 2:
        mesh_sens = local_sens + lax.ppermute(local_sens, "cond", [(0, 1), (1, 0)])
    else:
        mesh_sens = lax.psum(local_sens, "cond")
    return (psi, mesh_sens)


def solution(mesh):
    placed = (
        P("gx", "cond", None, "gy"),
        P("gx", "cond", None, "gy"),
        P("gx", "cond", None, None, "gy"),
        P("gx", "cond", None, None, "gy"),
        P("gx", "cond", None, None, "gy"),
        P("gx", "cond", None, None, "gy"),
        P("gx", "cond", None, None, "gy"),
        P("gx", "cond", None, None, "gy"),
        P("cond", None, None, None),
        P("gx", "cond", None, None, "gy"),
        P("gx", "gy"),
        P("cond"),
        P(),
    )
    return jax.shard_map(
        on_device,
        mesh=mesh,
        in_specs=placed,
        out_specs=(P("gx", "cond", None, "gy"), P("gx", None, "gy")),
        check_vma=False,
    )
```

```python
import jax
import jax.numpy as jnp
from jax import lax
from jax.experimental import pallas as pl
from jax.experimental.pallas import tpu as pltpu
from jax.sharding import PartitionSpec as P


NZ = 32
ITERS = 2


def extended(value, sides, width):
    for axis, dim in sides:
        size, length = (lax.axis_size(axis), value.shape[dim])
        up = [(i, (i + 1) % size) for i in range(size - 1)]
        down = [(j, i) for i, j in up]
        last = lax.slice_in_dim(value, length - width, length, axis=dim)
        first = lax.slice_in_dim(value, 0, width, axis=dim)
        before = lax.ppermute(last, axis, up)
        after = lax.ppermute(first, axis, down)
        value = jnp.concatenate([before, value, after], axis=dim)
    return value


def from_behind(value, axis, steps):
    count = lax.axis_size(axis)
    first, last = (max(0, -steps), min(count, count - steps))
    return lax.ppermute(value, axis, [(source, source + steps) for source in range(first, last)])


def _vmem_specs(n):
    return [pl.BlockSpec(memory_space=pltpu.VMEM) for _ in range(n)]


def _rows_times(blocks_ref, index, vec):
    terms = [blocks_ref[index + (a,)] * vec[a : a + 1, :] for a in range(vec.shape[0])]
    while len(terms) > 1:
        paired = [terms[j] + terms[j + 1] for j in range(0, len(terms) - 1, 2)]
        if len(terms) % 2:
            paired.append(terms[-1])
        terms = paired
    return terms[0]


def _init_carry(carry_ref, inc_ref):
    if inc_ref is not None:
        carry_ref[...] = inc_ref[...]
        return
    slots, width, conds, nv, lanes = carry_ref.shape
    rows = lax.broadcasted_iota(jnp.int32, (nv, lanes), 0)
    for slot in range(slots):
        for k in range(width):
            unit = (rows == k - slot * nv).astype(jnp.float32)
            for c in range(conds):
                carry_ref[slot, k, c] = unit


def upper_pallas(rhs, near_t, far_t, incoming, want_values):
    count, conds, nv = near_t.shape[0], near_t.shape[1], near_t.shape[2]
    has_inc = not isinstance(incoming, tuple)
    shape = incoming.shape if has_inc else incoming
    width = shape[1]
    has_rhs = rhs is not None

    def kernel(*refs):
        refs = list(refs)
        rhs_ref = refs.pop(0) if has_rhs else None
        nt_ref, ft_ref = refs.pop(0), refs.pop(0)
        inc_ref = refs.pop(0) if has_inc else None
        outs = refs
        if want_values:
            val_ref, carry_ref = outs
        else:
            (carry_ref,) = outs
        if width == 1:
            lasts = [inc_ref[0, 0, c] for c in range(conds)]
            befores = [inc_ref[1, 0, c] for c in range(conds)]
            for i in range(count):
                for c in range(conds):
                    acc = _rows_times(nt_ref, (i, c), lasts[c]) + _rows_times(
                        ft_ref, (i, c), befores[c]
                    )
                    now = rhs_ref[i, c] - acc
                    befores[c] = lasts[c]
                    lasts[c] = now
                    if want_values:
                        val_ref[i, c] = now
            for c in range(conds):
                carry_ref[0, 0, c] = lasts[c]
                carry_ref[1, 0, c] = befores[c]
            return
        _init_carry(carry_ref, inc_ref)

        def step(i, unused):
            for k in range(width):
                for c in range(conds):
                    last = carry_ref[0, k, c]
                    before = carry_ref[1, k, c]
                    acc = _rows_times(nt_ref, (i, c), last) + _rows_times(ft_ref, (i, c), before)
                    if has_rhs:
                        now = rhs_ref[i, c] - acc
                    else:
                        now = -acc
                    carry_ref[1, k, c] = last
                    carry_ref[0, k, c] = now
                    if want_values:
                        val_ref[i, c] = now
            return unused

        lax.fori_loop(0, count, step, 0)

    out_shape = [jax.ShapeDtypeStruct(shape, jnp.float32)]
    if want_values:
        out_shape = [jax.ShapeDtypeStruct(rhs.shape, jnp.float32)] + out_shape
    args = ([rhs] if has_rhs else []) + [near_t, far_t] + ([incoming] if has_inc else [])
    return pl.pallas_call(
        kernel,
        out_shape=tuple(out_shape),
        in_specs=_vmem_specs(len(args)),
        out_specs=tuple(_vmem_specs(len(out_shape))),
    )(*args)


def lower_pallas(rhs, inverse, near, far, incoming, want_values):
    count, conds, nv = inverse.shape[0], inverse.shape[1], inverse.shape[2]
    has_inc = not isinstance(incoming, tuple)
    shape = incoming.shape if has_inc else incoming
    width = shape[1]
    has_rhs = rhs is not None

    def kernel(*refs):
        refs = list(refs)
        rhs_ref = refs.pop(0) if has_rhs else None
        d_ref, b_ref, a_ref = refs.pop(0), refs.pop(0), refs.pop(0)
        inc_ref = refs.pop(0) if has_inc else None
        outs = refs
        if want_values:
            val_ref, carry_ref = outs
        else:
            (carry_ref,) = outs
        if width == 1:
            pendings = [inc_ref[0, 0, c] for c in range(conds)]
            partials = [inc_ref[1, 0, c] for c in range(conds)]
            for i in range(count - 1, -1, -1):
                for c in range(conds):
                    now = _rows_times(d_ref, (i, c), rhs_ref[i, c] - pendings[c])
                    pendings[c] = partials[c] + _rows_times(b_ref, (i, c), now)
                    partials[c] = _rows_times(a_ref, (i, c), now)
                    if want_values:
                        val_ref[i, c] = now
            for c in range(conds):
                carry_ref[0, 0, c] = pendings[c]
                carry_ref[1, 0, c] = partials[c]
            return
        _init_carry(carry_ref, inc_ref)

        def step(t, unused):
            i = count - 1 - t
            for k in range(width):
                for c in range(conds):
                    pending = carry_ref[0, k, c]
                    partial_value = carry_ref[1, k, c]
                    if has_rhs:
                        r = rhs_ref[i, c] - pending
                    else:
                        r = -pending
                    now = _rows_times(d_ref, (i, c), r)
                    carry_ref[0, k, c] = partial_value + _rows_times(b_ref, (i, c), now)
                    carry_ref[1, k, c] = _rows_times(a_ref, (i, c), now)
                    if want_values:
                        val_ref[i, c] = now
            return unused

        lax.fori_loop(0, count, step, 0)

    out_shape = [jax.ShapeDtypeStruct(shape, jnp.float32)]
    if want_values:
        out_shape = [jax.ShapeDtypeStruct(rhs.shape, jnp.float32)] + out_shape
    args = ([rhs] if has_rhs else []) + [inverse, near, far] + ([incoming] if has_inc else [])
    return pl.pallas_call(
        kernel,
        out_shape=tuple(out_shape),
        in_specs=_vmem_specs(len(args)),
        out_specs=tuple(_vmem_specs(len(out_shape))),
    )(*args)


def first_upper(zres, y_inverse, near_t, far_t):
    count, conds = near_t.shape[0], near_t.shape[1]
    carry = jax.ShapeDtypeStruct((2, 1) + zres.shape[1:], jnp.float32)

    def kernel(z_ref, y_ref, nt_ref, ft_ref, val_ref, carry_ref):
        for c in range(conds):
            last = before = None
            for i in range(count):
                value = _rows_times(y_ref, (i, c), z_ref[i, c])
                val_ref[i, c] = value
                if last is None:
                    now = value
                elif before is None:
                    now = value - _rows_times(nt_ref, (i, c), last)
                else:
                    now = value - (
                        _rows_times(nt_ref, (i, c), last) + _rows_times(ft_ref, (i, c), before)
                    )
                before, last = last, now
            carry_ref[0, 0, c] = last
            carry_ref[1, 0, c] = before

    return pl.pallas_call(
        kernel,
        out_shape=(jax.ShapeDtypeStruct(zres.shape, jnp.float32), carry),
        in_specs=_vmem_specs(4),
        out_specs=tuple(_vmem_specs(2)),
    )(zres, y_inverse, near_t, far_t)


def upper_then_lower(rhs, near_t, far_t, incoming, inverse, near, far):
    count, conds = near_t.shape[0], near_t.shape[1]
    carry = jax.ShapeDtypeStruct((2, 1) + rhs.shape[1:], jnp.float32)

    def kernel(rhs_ref, nt_ref, ft_ref, inc_ref, d_ref, b_ref, a_ref, val_ref, carry_ref):
        for c in range(conds):
            last, before = inc_ref[0, 0, c], inc_ref[1, 0, c]
            for i in range(count):
                acc = _rows_times(nt_ref, (i, c), last) + _rows_times(ft_ref, (i, c), before)
                before, last = last, rhs_ref[i, c] - acc
                val_ref[i, c] = last
            pending = None
            partial_value = None
            for i in range(count - 1, -1, -1):
                r = val_ref[i, c] if pending is None else val_ref[i, c] - pending
                now = _rows_times(d_ref, (i, c), r)
                near_part = _rows_times(b_ref, (i, c), now)
                pending = near_part if partial_value is None else partial_value + near_part
                partial_value = _rows_times(a_ref, (i, c), now)
            carry_ref[0, 0, c] = pending
            carry_ref[1, 0, c] = partial_value

    return pl.pallas_call(
        kernel,
        out_shape=(jax.ShapeDtypeStruct(rhs.shape, jnp.float32), carry),
        in_specs=_vmem_specs(7),
        out_specs=tuple(_vmem_specs(2)),
    )(rhs, near_t, far_t, incoming, inverse, near, far)


def carry_through(vector, response):
    slots, width, conds, nv, lanes = response.shape
    split = response.reshape(slots, slots, nv, conds, nv, lanes)
    inputs = jnp.transpose(vector, (0, 2, 1, 3))[None, :, :, :, None, :]
    return jnp.sum(jnp.sum(split * inputs, axis=2), axis=1)


def shifted_operators(matrix, steps):
    count = lax.axis_size("gx")
    return [from_behind(matrix, "gx", steps * s) for s in range(1, count - 1)]


def gathered_carry(vector, operators, steps):
    count = lax.axis_size("gx")
    if count == 1:
        return jnp.zeros_like(vector)
    total = from_behind(vector, "gx", steps * (count - 1))
    for s in range(count - 2, 0, -1):
        total = carry_through(total, operators[s - 1]) + from_behind(
            vector, "gx", steps * s
        )
    return total


def relayed_carry(vector, behind, steps):
    count = lax.axis_size("gx")
    if count == 1:
        return jnp.zeros_like(vector)
    nearest = from_behind(vector, "gx", steps)
    if count == 2:
        return nearest
    total = nearest + carry_through(from_behind(vector, "gx", 2 * steps), behind)
    for _ in range(count - 3):
        total = nearest + carry_through(from_behind(total, "gx", steps), behind)
    return total


def on_device(
    psi_old,
    objective_grad,
    near_upper,
    far_upper,
    inverse_diag,
    near_lower,
    far_lower,
    y_inverse,
    z_inverse,
    sens_terms,
    wall_mask,
    cond_index,
    weight_table,
):
    keep = (1.0 - wall_mask.astype(jnp.float32))[:, None, None, :]
    carry_shape = psi_old.shape[1:]
    zeros = jnp.zeros((2, 1) + carry_shape, jnp.float32)
    units = (2, 2 * carry_shape[1]) + carry_shape
    near_t = jnp.swapaxes(near_upper, 2, 3)
    far_t = jnp.swapaxes(far_upper, 2, 3)
    (response,) = upper_pallas(None, near_t, far_t, units, False)
    matrix = response
    (response,) = lower_pallas(None, inverse_diag, near_lower, far_lower, units, False)
    reverse_matrix = response
    upper_products = shifted_operators(matrix, 1)
    lower_behind = from_behind(reverse_matrix, "gx", -1)
    psi = psi_old
    for step in range(ITERS):
        stream_pad = extended(psi, (("gx", 0),), 1)
        span_pad = extended(psi, (("gy", 3),), NZ)
        beside_all = (
            stream_pad[2:] + stream_pad[:-2] + span_pad[..., 2 * NZ :] + span_pad[..., : -2 * NZ]
        )
        rhs = objective_grad + 0.5 * beside_all - 2.0 * psi
        grid = rhs.reshape(rhs.shape[0], rhs.shape[1], rhs.shape[2], rhs.shape[3] // NZ, NZ)
        zres = jnp.einsum(
            "icvjq,cvqk->icvjk", grid, z_inverse, precision=lax.Precision.HIGHEST
        ).reshape(rhs.shape)
        yres, offset = first_upper(zres, y_inverse, near_t, far_t)
        entering = gathered_carry(offset[:, 0], upper_products, 1)
        upper, offset = upper_then_lower(
            yres, near_t, far_t, entering[:, None], inverse_diag, near_lower, far_lower
        )
        entering = relayed_carry(offset[:, 0], lower_behind, -1)
        lower, _ = lower_pallas(upper, inverse_diag, near_lower, far_lower, entering[:, None], True)
        psi = (psi + 0.05 * lower) * keep
    onehot = (cond_index[:, None] == jnp.arange(weight_table.shape[0])[None, :]).astype(jnp.float32)
    weights = jnp.sum(onehot * weight_table[None, :], axis=1)
    local_sens = jnp.einsum(
        "icvl,icmvl->iml",
        psi * weights[None, :, None, None],
        sens_terms,
        precision=lax.Precision.HIGHEST,
    )
    if lax.axis_size("cond") == 2:
        mesh_sens = local_sens + lax.ppermute(local_sens, "cond", [(0, 1), (1, 0)])
    else:
        mesh_sens = lax.psum(local_sens, "cond")
    return (psi, mesh_sens)


def solution(mesh):
    placed = (
        P("gx", "cond", None, "gy"),
        P("gx", "cond", None, "gy"),
        P("gx", "cond", None, None, "gy"),
        P("gx", "cond", None, None, "gy"),
        P("gx", "cond", None, None, "gy"),
        P("gx", "cond", None, None, "gy"),
        P("gx", "cond", None, None, "gy"),
        P("gx", "cond", None, None, "gy"),
        P("cond", None, None, None),
        P("gx", "cond", None, None, "gy"),
        P("gx", "gy"),
        P("cond"),
        P(),
    )
    return jax.shard_map(
        on_device,
        mesh=mesh,
        in_specs=placed,
        out_specs=(P("gx", "cond", None, "gy"), P("gx", None, "gy")),
        check_vma=False,
    )
```

```python
import jax
import jax.numpy as jnp
from jax import lax
from jax.experimental import pallas as pl
from jax.experimental.pallas import tpu as pltpu
from jax.sharding import PartitionSpec as P


NZ = 32
ITERS = 2


def extended(value, sides, width):
    for axis, dim in sides:
        size, length = (lax.axis_size(axis), value.shape[dim])
        up = [(i, (i + 1) % size) for i in range(size - 1)]
        down = [(j, i) for i, j in up]
        last = lax.slice_in_dim(value, length - width, length, axis=dim)
        first = lax.slice_in_dim(value, 0, width, axis=dim)
        before = lax.ppermute(last, axis, up)
        after = lax.ppermute(first, axis, down)
        value = jnp.concatenate([before, value, after], axis=dim)
    return value


def from_behind(value, axis, steps):
    count = lax.axis_size(axis)
    first, last = (max(0, -steps), min(count, count - steps))
    return lax.ppermute(value, axis, [(source, source + steps) for source in range(first, last)])


def _vmem_specs(n):
    return [pl.BlockSpec(memory_space=pltpu.VMEM) for _ in range(n)]


def _rows_times(blocks_ref, index, vec):
    terms = [blocks_ref[index + (a,)] * vec[a : a + 1, :] for a in range(vec.shape[0])]
    while len(terms) > 1:
        paired = [terms[j] + terms[j + 1] for j in range(0, len(terms) - 1, 2)]
        if len(terms) % 2:
            paired.append(terms[-1])
        terms = paired
    return terms[0]


def _init_carry(carry_ref, inc_ref):
    if inc_ref is not None:
        carry_ref[...] = inc_ref[...]
        return
    slots, width, conds, nv, lanes = carry_ref.shape
    rows = lax.broadcasted_iota(jnp.int32, (nv, lanes), 0)
    for slot in range(slots):
        for k in range(width):
            unit = (rows == k - slot * nv).astype(jnp.float32)
            for c in range(conds):
                carry_ref[slot, k, c] = unit


def upper_pallas(rhs, near_t, far_t, incoming, want_values):
    count, conds, nv = near_t.shape[0], near_t.shape[1], near_t.shape[2]
    has_inc = not isinstance(incoming, tuple)
    shape = incoming.shape if has_inc else incoming
    width = shape[1]
    has_rhs = rhs is not None

    def kernel(*refs):
        refs = list(refs)
        rhs_ref = refs.pop(0) if has_rhs else None
        nt_ref, ft_ref = refs.pop(0), refs.pop(0)
        inc_ref = refs.pop(0) if has_inc else None
        outs = refs
        if want_values:
            val_ref, carry_ref = outs
        else:
            (carry_ref,) = outs
        if width == 1:
            lasts = [inc_ref[0, 0, c] for c in range(conds)]
            befores = [inc_ref[1, 0, c] for c in range(conds)]
            for i in range(count):
                for c in range(conds):
                    acc = _rows_times(nt_ref, (i, c), lasts[c]) + _rows_times(
                        ft_ref, (i, c), befores[c]
                    )
                    now = rhs_ref[i, c] - acc
                    befores[c] = lasts[c]
                    lasts[c] = now
                    if want_values:
                        val_ref[i, c] = now
            for c in range(conds):
                carry_ref[0, 0, c] = lasts[c]
                carry_ref[1, 0, c] = befores[c]
            return
        _init_carry(carry_ref, inc_ref)

        def step(i, unused):
            for k in range(width):
                for c in range(conds):
                    last = carry_ref[0, k, c]
                    before = carry_ref[1, k, c]
                    acc = _rows_times(nt_ref, (i, c), last) + _rows_times(ft_ref, (i, c), before)
                    if has_rhs:
                        now = rhs_ref[i, c] - acc
                    else:
                        now = -acc
                    carry_ref[1, k, c] = last
                    carry_ref[0, k, c] = now
                    if want_values:
                        val_ref[i, c] = now
            return unused

        lax.fori_loop(0, count, step, 0)

    out_shape = [jax.ShapeDtypeStruct(shape, jnp.float32)]
    if want_values:
        out_shape = [jax.ShapeDtypeStruct(rhs.shape, jnp.float32)] + out_shape
    args = ([rhs] if has_rhs else []) + [near_t, far_t] + ([incoming] if has_inc else [])
    return pl.pallas_call(
        kernel,
        out_shape=tuple(out_shape),
        in_specs=_vmem_specs(len(args)),
        out_specs=tuple(_vmem_specs(len(out_shape))),
    )(*args)


def lower_pallas(rhs, inverse, near, far, incoming, want_values):
    count, conds, nv = inverse.shape[0], inverse.shape[1], inverse.shape[2]
    has_inc = not isinstance(incoming, tuple)
    shape = incoming.shape if has_inc else incoming
    width = shape[1]
    has_rhs = rhs is not None

    def kernel(*refs):
        refs = list(refs)
        rhs_ref = refs.pop(0) if has_rhs else None
        d_ref, b_ref, a_ref = refs.pop(0), refs.pop(0), refs.pop(0)
        inc_ref = refs.pop(0) if has_inc else None
        outs = refs
        if want_values:
            val_ref, carry_ref = outs
        else:
            (carry_ref,) = outs
        if width == 1:
            pendings = [inc_ref[0, 0, c] for c in range(conds)]
            partials = [inc_ref[1, 0, c] for c in range(conds)]
            for i in range(count - 1, -1, -1):
                for c in range(conds):
                    now = _rows_times(d_ref, (i, c), rhs_ref[i, c] - pendings[c])
                    pendings[c] = partials[c] + _rows_times(b_ref, (i, c), now)
                    partials[c] = _rows_times(a_ref, (i, c), now)
                    if want_values:
                        val_ref[i, c] = now
            for c in range(conds):
                carry_ref[0, 0, c] = pendings[c]
                carry_ref[1, 0, c] = partials[c]
            return
        _init_carry(carry_ref, inc_ref)

        def step(t, unused):
            i = count - 1 - t
            for k in range(width):
                for c in range(conds):
                    pending = carry_ref[0, k, c]
                    partial_value = carry_ref[1, k, c]
                    if has_rhs:
                        r = rhs_ref[i, c] - pending
                    else:
                        r = -pending
                    now = _rows_times(d_ref, (i, c), r)
                    carry_ref[0, k, c] = partial_value + _rows_times(b_ref, (i, c), now)
                    carry_ref[1, k, c] = _rows_times(a_ref, (i, c), now)
                    if want_values:
                        val_ref[i, c] = now
            return unused

        lax.fori_loop(0, count, step, 0)

    out_shape = [jax.ShapeDtypeStruct(shape, jnp.float32)]
    if want_values:
        out_shape = [jax.ShapeDtypeStruct(rhs.shape, jnp.float32)] + out_shape
    args = ([rhs] if has_rhs else []) + [inverse, near, far] + ([incoming] if has_inc else [])
    return pl.pallas_call(
        kernel,
        out_shape=tuple(out_shape),
        in_specs=_vmem_specs(len(args)),
        out_specs=tuple(_vmem_specs(len(out_shape))),
    )(*args)


def first_upper(zres, y_inverse, near_t, far_t):
    count, conds = near_t.shape[0], near_t.shape[1]
    carry = jax.ShapeDtypeStruct((2, 1) + zres.shape[1:], jnp.float32)

    def kernel(z_ref, y_ref, nt_ref, ft_ref, val_ref, carry_ref):
        for c in range(conds):
            last = before = None
            for i in range(count):
                value = _rows_times(y_ref, (i, c), z_ref[i, c])
                val_ref[i, c] = value
                if last is None:
                    now = value
                elif before is None:
                    now = value - _rows_times(nt_ref, (i, c), last)
                else:
                    now = value - (
                        _rows_times(nt_ref, (i, c), last) + _rows_times(ft_ref, (i, c), before)
                    )
                before, last = last, now
            carry_ref[0, 0, c] = last
            carry_ref[1, 0, c] = before

    return pl.pallas_call(
        kernel,
        out_shape=(jax.ShapeDtypeStruct(zres.shape, jnp.float32), carry),
        in_specs=_vmem_specs(4),
        out_specs=tuple(_vmem_specs(2)),
    )(zres, y_inverse, near_t, far_t)


def lower_update(rhs, inverse, near, far, incoming, psi, keep):
    count, conds = inverse.shape[0], inverse.shape[1]

    def kernel(rhs_ref, d_ref, b_ref, a_ref, inc_ref, psi_ref, keep_ref, out_ref):
        for c in range(conds):
            pending, partial_value = inc_ref[0, 0, c], inc_ref[1, 0, c]
            for i in range(count - 1, -1, -1):
                now = _rows_times(d_ref, (i, c), rhs_ref[i, c] - pending)
                pending = partial_value + _rows_times(b_ref, (i, c), now)
                partial_value = _rows_times(a_ref, (i, c), now)
                out_ref[i, c] = (psi_ref[i, c] + 0.05 * now) * keep_ref[i : i + 1, :]

    return pl.pallas_call(
        kernel,
        out_shape=jax.ShapeDtypeStruct(psi.shape, jnp.float32),
        in_specs=_vmem_specs(7),
        out_specs=pl.BlockSpec(memory_space=pltpu.VMEM),
    )(rhs, inverse, near, far, incoming, psi, keep)


def upper_then_lower(rhs, near_t, far_t, incoming, inverse, near, far):
    count, conds = near_t.shape[0], near_t.shape[1]
    carry = jax.ShapeDtypeStruct((2, 1) + rhs.shape[1:], jnp.float32)

    def kernel(rhs_ref, nt_ref, ft_ref, inc_ref, d_ref, b_ref, a_ref, val_ref, carry_ref):
        for c in range(conds):
            last, before = inc_ref[0, 0, c], inc_ref[1, 0, c]
            for i in range(count):
                acc = _rows_times(nt_ref, (i, c), last) + _rows_times(ft_ref, (i, c), before)
                before, last = last, rhs_ref[i, c] - acc
                val_ref[i, c] = last
            pending = None
            partial_value = None
            for i in range(count - 1, -1, -1):
                r = val_ref[i, c] if pending is None else val_ref[i, c] - pending
                now = _rows_times(d_ref, (i, c), r)
                near_part = _rows_times(b_ref, (i, c), now)
                pending = near_part if partial_value is None else partial_value + near_part
                partial_value = _rows_times(a_ref, (i, c), now)
            carry_ref[0, 0, c] = pending
            carry_ref[1, 0, c] = partial_value

    return pl.pallas_call(
        kernel,
        out_shape=(jax.ShapeDtypeStruct(rhs.shape, jnp.float32), carry),
        in_specs=_vmem_specs(7),
        out_specs=tuple(_vmem_specs(2)),
    )(rhs, near_t, far_t, incoming, inverse, near, far)


def carry_through(vector, response):
    slots, width, conds, nv, lanes = response.shape
    split = response.reshape(slots, slots, nv, conds, nv, lanes)
    inputs = jnp.transpose(vector, (0, 2, 1, 3))[None, :, :, :, None, :]
    return jnp.sum(jnp.sum(split * inputs, axis=2), axis=1)


def shifted_operators(matrix, steps):
    count = lax.axis_size("gx")
    return [from_behind(matrix, "gx", steps * s) for s in range(1, count - 1)]


def gathered_carry(vector, operators, steps):
    count = lax.axis_size("gx")
    if count == 1:
        return jnp.zeros_like(vector)
    total = from_behind(vector, "gx", steps * (count - 1))
    for s in range(count - 2, 0, -1):
        total = carry_through(total, operators[s - 1]) + from_behind(
            vector, "gx", steps * s
        )
    return total


def relayed_carry(vector, behind, steps):
    count = lax.axis_size("gx")
    if count == 1:
        return jnp.zeros_like(vector)
    nearest = from_behind(vector, "gx", steps)
    if count == 2:
        return nearest
    total = nearest + carry_through(from_behind(vector, "gx", 2 * steps), behind)
    for _ in range(count - 3):
        total = nearest + carry_through(from_behind(total, "gx", steps), behind)
    return total


def on_device(
    psi_old,
    objective_grad,
    near_upper,
    far_upper,
    inverse_diag,
    near_lower,
    far_lower,
    y_inverse,
    z_inverse,
    sens_terms,
    wall_mask,
    cond_index,
    weight_table,
):
    keep_rows = 1.0 - wall_mask.astype(jnp.float32)
    carry_shape = psi_old.shape[1:]
    zeros = jnp.zeros((2, 1) + carry_shape, jnp.float32)
    units = (2, 2 * carry_shape[1]) + carry_shape
    near_t = jnp.swapaxes(near_upper, 2, 3)
    far_t = jnp.swapaxes(far_upper, 2, 3)
    (response,) = upper_pallas(None, near_t, far_t, units, False)
    matrix = response
    (response,) = lower_pallas(None, inverse_diag, near_lower, far_lower, units, False)
    reverse_matrix = response
    upper_products = shifted_operators(matrix, 1)
    lower_behind = from_behind(reverse_matrix, "gx", -1)
    psi = psi_old
    for step in range(ITERS):
        stream_pad = extended(psi, (("gx", 0),), 1)
        span_pad = extended(psi, (("gy", 3),), NZ)
        beside_all = (
            stream_pad[2:] + stream_pad[:-2] + span_pad[..., 2 * NZ :] + span_pad[..., : -2 * NZ]
        )
        rhs = objective_grad + 0.5 * beside_all - 2.0 * psi
        grid = rhs.reshape(rhs.shape[0], rhs.shape[1], rhs.shape[2], rhs.shape[3] // NZ, NZ)
        zres = jnp.einsum(
            "icvjq,cvqk->icvjk", grid, z_inverse, precision=lax.Precision.HIGHEST
        ).reshape(rhs.shape)
        yres, offset = first_upper(zres, y_inverse, near_t, far_t)
        entering = gathered_carry(offset[:, 0], upper_products, 1)
        upper, offset = upper_then_lower(
            yres, near_t, far_t, entering[:, None], inverse_diag, near_lower, far_lower
        )
        entering = relayed_carry(offset[:, 0], lower_behind, -1)
        psi = lower_update(
            upper, inverse_diag, near_lower, far_lower, entering[:, None], psi, keep_rows
        )
    onehot = (cond_index[:, None] == jnp.arange(weight_table.shape[0])[None, :]).astype(jnp.float32)
    weights = jnp.sum(onehot * weight_table[None, :], axis=1)
    local_sens = jnp.einsum(
        "icvl,icmvl->iml",
        psi * weights[None, :, None, None],
        sens_terms,
        precision=lax.Precision.HIGHEST,
    )
    if lax.axis_size("cond") == 2:
        mesh_sens = local_sens + lax.ppermute(local_sens, "cond", [(0, 1), (1, 0)])
    else:
        mesh_sens = lax.psum(local_sens, "cond")
    return (psi, mesh_sens)


def solution(mesh):
    placed = (
        P("gx", "cond", None, "gy"),
        P("gx", "cond", None, "gy"),
        P("gx", "cond", None, None, "gy"),
        P("gx", "cond", None, None, "gy"),
        P("gx", "cond", None, None, "gy"),
        P("gx", "cond", None, None, "gy"),
        P("gx", "cond", None, None, "gy"),
        P("gx", "cond", None, None, "gy"),
        P("cond", None, None, None),
        P("gx", "cond", None, None, "gy"),
        P("gx", "gy"),
        P("cond"),
        P(),
    )
    return jax.shard_map(
        on_device,
        mesh=mesh,
        in_specs=placed,
        out_specs=(P("gx", "cond", None, "gy"), P("gx", None, "gy")),
        check_vma=False,
    )
```

```python
import jax
import jax.numpy as jnp
from jax import lax
from jax.experimental import pallas as pl
from jax.experimental.pallas import tpu as pltpu
from jax.sharding import PartitionSpec as P


NZ = 32
ITERS = 2


def extended(value, sides, width):
    for axis, dim in sides:
        size, length = (lax.axis_size(axis), value.shape[dim])
        up = [(i, (i + 1) % size) for i in range(size - 1)]
        down = [(j, i) for i, j in up]
        last = lax.slice_in_dim(value, length - width, length, axis=dim)
        first = lax.slice_in_dim(value, 0, width, axis=dim)
        before = lax.ppermute(last, axis, up)
        after = lax.ppermute(first, axis, down)
        value = jnp.concatenate([before, value, after], axis=dim)
    return value


def from_behind(value, axis, steps):
    count = lax.axis_size(axis)
    first, last = (max(0, -steps), min(count, count - steps))
    return lax.ppermute(value, axis, [(source, source + steps) for source in range(first, last)])


def _vmem_specs(n):
    return [pl.BlockSpec(memory_space=pltpu.VMEM) for _ in range(n)]


def _rows_times(blocks_ref, index, vec):
    terms = [blocks_ref[index + (a,)] * vec[a : a + 1, :] for a in range(vec.shape[0])]
    while len(terms) > 1:
        paired = [terms[j] + terms[j + 1] for j in range(0, len(terms) - 1, 2)]
        if len(terms) % 2:
            paired.append(terms[-1])
        terms = paired
    return terms[0]


def _init_carry(carry_ref, inc_ref):
    if inc_ref is not None:
        carry_ref[...] = inc_ref[...]
        return
    slots, width, conds, nv, lanes = carry_ref.shape
    rows = lax.broadcasted_iota(jnp.int32, (nv, lanes), 0)
    for slot in range(slots):
        for k in range(width):
            unit = (rows == k - slot * nv).astype(jnp.float32)
            for c in range(conds):
                carry_ref[slot, k, c] = unit


def upper_pallas(rhs, near_t, far_t, incoming, want_values):
    count, conds, nv = near_t.shape[0], near_t.shape[1], near_t.shape[2]
    has_inc = not isinstance(incoming, tuple)
    shape = incoming.shape if has_inc else incoming
    width = shape[1]
    has_rhs = rhs is not None

    def kernel(*refs):
        refs = list(refs)
        rhs_ref = refs.pop(0) if has_rhs else None
        nt_ref, ft_ref = refs.pop(0), refs.pop(0)
        inc_ref = refs.pop(0) if has_inc else None
        outs = refs
        if want_values:
            val_ref, carry_ref = outs
        else:
            (carry_ref,) = outs
        if width == 1:
            lasts = [inc_ref[0, 0, c] for c in range(conds)]
            befores = [inc_ref[1, 0, c] for c in range(conds)]
            for i in range(count):
                for c in range(conds):
                    acc = _rows_times(nt_ref, (i, c), lasts[c]) + _rows_times(
                        ft_ref, (i, c), befores[c]
                    )
                    now = rhs_ref[i, c] - acc
                    befores[c] = lasts[c]
                    lasts[c] = now
                    if want_values:
                        val_ref[i, c] = now
            for c in range(conds):
                carry_ref[0, 0, c] = lasts[c]
                carry_ref[1, 0, c] = befores[c]
            return
        _init_carry(carry_ref, inc_ref)

        def step(i, unused):
            for k in range(width):
                for c in range(conds):
                    last = carry_ref[0, k, c]
                    before = carry_ref[1, k, c]
                    acc = _rows_times(nt_ref, (i, c), last) + _rows_times(ft_ref, (i, c), before)
                    if has_rhs:
                        now = rhs_ref[i, c] - acc
                    else:
                        now = -acc
                    carry_ref[1, k, c] = last
                    carry_ref[0, k, c] = now
                    if want_values:
                        val_ref[i, c] = now
            return unused

        lax.fori_loop(0, count, step, 0)

    out_shape = [jax.ShapeDtypeStruct(shape, jnp.float32)]
    if want_values:
        out_shape = [jax.ShapeDtypeStruct(rhs.shape, jnp.float32)] + out_shape
    args = ([rhs] if has_rhs else []) + [near_t, far_t] + ([incoming] if has_inc else [])
    return pl.pallas_call(
        kernel,
        out_shape=tuple(out_shape),
        in_specs=_vmem_specs(len(args)),
        out_specs=tuple(_vmem_specs(len(out_shape))),
    )(*args)


def lower_pallas(rhs, inverse, near, far, incoming, want_values):
    count, conds, nv = inverse.shape[0], inverse.shape[1], inverse.shape[2]
    has_inc = not isinstance(incoming, tuple)
    shape = incoming.shape if has_inc else incoming
    width = shape[1]
    has_rhs = rhs is not None

    def kernel(*refs):
        refs = list(refs)
        rhs_ref = refs.pop(0) if has_rhs else None
        d_ref, b_ref, a_ref = refs.pop(0), refs.pop(0), refs.pop(0)
        inc_ref = refs.pop(0) if has_inc else None
        outs = refs
        if want_values:
            val_ref, carry_ref = outs
        else:
            (carry_ref,) = outs
        if width == 1:
            pendings = [inc_ref[0, 0, c] for c in range(conds)]
            partials = [inc_ref[1, 0, c] for c in range(conds)]
            for i in range(count - 1, -1, -1):
                for c in range(conds):
                    now = _rows_times(d_ref, (i, c), rhs_ref[i, c] - pendings[c])
                    pendings[c] = partials[c] + _rows_times(b_ref, (i, c), now)
                    partials[c] = _rows_times(a_ref, (i, c), now)
                    if want_values:
                        val_ref[i, c] = now
            for c in range(conds):
                carry_ref[0, 0, c] = pendings[c]
                carry_ref[1, 0, c] = partials[c]
            return
        _init_carry(carry_ref, inc_ref)

        def step(t, unused):
            i = count - 1 - t
            for k in range(width):
                for c in range(conds):
                    pending = carry_ref[0, k, c]
                    partial_value = carry_ref[1, k, c]
                    if has_rhs:
                        r = rhs_ref[i, c] - pending
                    else:
                        r = -pending
                    now = _rows_times(d_ref, (i, c), r)
                    carry_ref[0, k, c] = partial_value + _rows_times(b_ref, (i, c), now)
                    carry_ref[1, k, c] = _rows_times(a_ref, (i, c), now)
                    if want_values:
                        val_ref[i, c] = now
            return unused

        lax.fori_loop(0, count, step, 0)

    out_shape = [jax.ShapeDtypeStruct(shape, jnp.float32)]
    if want_values:
        out_shape = [jax.ShapeDtypeStruct(rhs.shape, jnp.float32)] + out_shape
    args = ([rhs] if has_rhs else []) + [inverse, near, far] + ([incoming] if has_inc else [])
    return pl.pallas_call(
        kernel,
        out_shape=tuple(out_shape),
        in_specs=_vmem_specs(len(args)),
        out_specs=tuple(_vmem_specs(len(out_shape))),
    )(*args)


def first_upper(zres, y_inverse, near_t, far_t):
    count, conds = near_t.shape[0], near_t.shape[1]
    carry = jax.ShapeDtypeStruct((2, 1) + zres.shape[1:], jnp.float32)

    def kernel(z_ref, y_ref, nt_ref, ft_ref, val_ref, carry_ref):
        for c in range(conds):
            last = before = None
            for i in range(count):
                value = _rows_times(y_ref, (i, c), z_ref[i, c])
                val_ref[i, c] = value
                if last is None:
                    now = value
                elif before is None:
                    now = value - _rows_times(nt_ref, (i, c), last)
                else:
                    now = value - (
                        _rows_times(nt_ref, (i, c), last) + _rows_times(ft_ref, (i, c), before)
                    )
                before, last = last, now
            carry_ref[0, 0, c] = last
            carry_ref[1, 0, c] = before

    return pl.pallas_call(
        kernel,
        out_shape=(jax.ShapeDtypeStruct(zres.shape, jnp.float32), carry),
        in_specs=_vmem_specs(4),
        out_specs=tuple(_vmem_specs(2)),
    )(zres, y_inverse, near_t, far_t)


def upper_then_lower(rhs, near_t, far_t, shifted, operators, inverse, near, far):
    count, conds, nv = near_t.shape[0], near_t.shape[1], near_t.shape[2]
    carry = jax.ShapeDtypeStruct((2, 1) + rhs.shape[1:], jnp.float32)
    n_shift, n_op = len(shifted), len(operators)

    def kernel(*refs):
        refs = list(refs)
        rhs_ref, nt_ref, ft_ref = refs[:3]
        shift_refs = refs[3 : 3 + n_shift]
        op_refs = refs[3 + n_shift : 3 + n_shift + n_op]
        d_ref, b_ref, a_ref, val_ref, carry_ref = refs[3 + n_shift + n_op :]
        for c in range(conds):
            total = [shift_refs[n_shift - 1][slot, c] for slot in range(2)]
            for s in range(n_shift - 1, 0, -1):
                op_ref = op_refs[s - 1]
                mixed = []
                for slot in range(2):
                    terms = []
                    for src_slot in range(2):
                        for v in range(nv):
                            terms.append(
                                op_ref[slot, src_slot * nv + v, c] * total[src_slot][v : v + 1, :]
                            )
                    while len(terms) > 1:
                        paired = [terms[j] + terms[j + 1] for j in range(0, len(terms) - 1, 2)]
                        if len(terms) % 2:
                            paired.append(terms[-1])
                        terms = paired
                    mixed.append(terms[0] + shift_refs[s - 1][slot, c])
                total = mixed
            last, before = total
            for i in range(count):
                acc = _rows_times(nt_ref, (i, c), last) + _rows_times(ft_ref, (i, c), before)
                before, last = last, rhs_ref[i, c] - acc
                val_ref[i, c] = last
            pending = None
            partial_value = None
            for i in range(count - 1, -1, -1):
                r = val_ref[i, c] if pending is None else val_ref[i, c] - pending
                now = _rows_times(d_ref, (i, c), r)
                near_part = _rows_times(b_ref, (i, c), now)
                pending = near_part if partial_value is None else partial_value + near_part
                partial_value = _rows_times(a_ref, (i, c), now)
            carry_ref[0, 0, c] = pending
            carry_ref[1, 0, c] = partial_value

    args = [rhs, near_t, far_t] + list(shifted) + list(operators) + [inverse, near, far]
    return pl.pallas_call(
        kernel,
        out_shape=(jax.ShapeDtypeStruct(rhs.shape, jnp.float32), carry),
        in_specs=_vmem_specs(len(args)),
        out_specs=tuple(_vmem_specs(2)),
    )(*args)


def carry_through(vector, response):
    slots, width, conds, nv, lanes = response.shape
    split = response.reshape(slots, slots, nv, conds, nv, lanes)
    inputs = jnp.transpose(vector, (0, 2, 1, 3))[None, :, :, :, None, :]
    return jnp.sum(jnp.sum(split * inputs, axis=2), axis=1)


def shifted_operators(matrix, steps):
    count = lax.axis_size("gx")
    return [from_behind(matrix, "gx", steps * s) for s in range(1, count - 1)]


def gathered_carry(vector, operators, steps):
    count = lax.axis_size("gx")
    if count == 1:
        return jnp.zeros_like(vector)
    total = from_behind(vector, "gx", steps * (count - 1))
    for s in range(count - 2, 0, -1):
        total = carry_through(total, operators[s - 1]) + from_behind(
            vector, "gx", steps * s
        )
    return total


def relayed_carry(vector, behind, steps):
    count = lax.axis_size("gx")
    if count == 1:
        return jnp.zeros_like(vector)
    nearest = from_behind(vector, "gx", steps)
    if count == 2:
        return nearest
    total = nearest + carry_through(from_behind(vector, "gx", 2 * steps), behind)
    for _ in range(count - 3):
        total = nearest + carry_through(from_behind(total, "gx", steps), behind)
    return total


def on_device(
    psi_old,
    objective_grad,
    near_upper,
    far_upper,
    inverse_diag,
    near_lower,
    far_lower,
    y_inverse,
    z_inverse,
    sens_terms,
    wall_mask,
    cond_index,
    weight_table,
):
    keep = (1.0 - wall_mask.astype(jnp.float32))[:, None, None, :]
    carry_shape = psi_old.shape[1:]
    zeros = jnp.zeros((2, 1) + carry_shape, jnp.float32)
    units = (2, 2 * carry_shape[1]) + carry_shape
    near_t = jnp.swapaxes(near_upper, 2, 3)
    far_t = jnp.swapaxes(far_upper, 2, 3)
    (response,) = upper_pallas(None, near_t, far_t, units, False)
    matrix = response
    (response,) = lower_pallas(None, inverse_diag, near_lower, far_lower, units, False)
    reverse_matrix = response
    upper_products = shifted_operators(matrix, 1)
    lower_behind = from_behind(reverse_matrix, "gx", -1)
    psi = psi_old
    for step in range(ITERS):
        stream_pad = extended(psi, (("gx", 0),), 1)
        span_pad = extended(psi, (("gy", 3),), NZ)
        beside_all = (
            stream_pad[2:] + stream_pad[:-2] + span_pad[..., 2 * NZ :] + span_pad[..., : -2 * NZ]
        )
        rhs = objective_grad + 0.5 * beside_all - 2.0 * psi
        grid = rhs.reshape(rhs.shape[0], rhs.shape[1], rhs.shape[2], rhs.shape[3] // NZ, NZ)
        zres = jnp.einsum(
            "icvjq,cvqk->icvjk", grid, z_inverse, precision=lax.Precision.HIGHEST
        ).reshape(rhs.shape)
        yres, offset = first_upper(zres, y_inverse, near_t, far_t)
        gx_count = lax.axis_size("gx")
        shifted = [from_behind(offset[:, 0], "gx", s) for s in range(1, gx_count)]
        if not shifted:
            shifted = [jnp.zeros_like(offset[:, 0])]
        upper, offset = upper_then_lower(
            yres, near_t, far_t, shifted, upper_products, inverse_diag, near_lower, far_lower
        )
        entering = relayed_carry(offset[:, 0], lower_behind, -1)
        lower, _ = lower_pallas(upper, inverse_diag, near_lower, far_lower, entering[:, None], True)
        psi = (psi + 0.05 * lower) * keep
    onehot = (cond_index[:, None] == jnp.arange(weight_table.shape[0])[None, :]).astype(jnp.float32)
    weights = jnp.sum(onehot * weight_table[None, :], axis=1)
    local_sens = jnp.einsum(
        "icvl,icmvl->iml",
        psi * weights[None, :, None, None],
        sens_terms,
        precision=lax.Precision.HIGHEST,
    )
    if lax.axis_size("cond") == 2:
        mesh_sens = local_sens + lax.ppermute(local_sens, "cond", [(0, 1), (1, 0)])
    else:
        mesh_sens = lax.psum(local_sens, "cond")
    return (psi, mesh_sens)


def solution(mesh):
    placed = (
        P("gx", "cond", None, "gy"),
        P("gx", "cond", None, "gy"),
        P("gx", "cond", None, None, "gy"),
        P("gx", "cond", None, None, "gy"),
        P("gx", "cond", None, None, "gy"),
        P("gx", "cond", None, None, "gy"),
        P("gx", "cond", None, None, "gy"),
        P("gx", "cond", None, None, "gy"),
        P("cond", None, None, None),
        P("gx", "cond", None, None, "gy"),
        P("gx", "gy"),
        P("cond"),
        P(),
    )
    return jax.shard_map(
        on_device,
        mesh=mesh,
        in_specs=placed,
        out_specs=(P("gx", "cond", None, "gy"), P("gx", None, "gy")),
        check_vma=False,
    )
```
